32 devices in a mesh: groups: 2 (over y), ctx: 4 (over z), head: 4 (over x, core).
Axes of the slice: x: 2, y: 2, z: 4, core: 2. Of those that a mesh axis runs over, the one named last changes fastest.
Arguments:
- queries: bfloat16 [8192, 512], P(('groups', 'ctx', 'head')), parts along dimension 0, may hold values from -8 to 8, as said below
- keys: bfloat16 [8192, 512], P(('groups', 'ctx', 'head')), parts along dimension 0, may hold values from -8 to 8
- values: bfloat16 [8192, 4096], P(('groups', 'ctx', 'head')), parts along dimension 0, may hold values from -6 to 6
- gain: float32 [4096], P('head'), may hold values from 0.5 to 1.5
Outputs:
- mixed: bfloat16 [8192, 4096], P(('groups', 'ctx', 'head')), parts along dimension 0
The draws below stay inside these ranges and needn't reach their ends.
There are 2 independent parts, one for each index of `groups`. The reference program is written for one: setup_inputs(seed, part) draws one part's arguments, and reference() takes and returns one part's arrays. A program takes and returns all parts, laid end to end along the dimension named above; an argument that names none is the same for every part. Nothing has to cross between parts.
Inputs may be any that keep to these rules, and one draw needn't show every extreme that they name: `queries`: query entries lie in the stated range.
All inputs are finite; a program needn't handle non-finite values.
Results may differ from the reference program's by a relative error of at most 0.0054.
Values may be sent and summed in bfloat16 or wider, within the bound.
No kernel may reach another device: no remote copies, remote signals or barrier semaphores. Data moves between devices by JAX's collectives and lax.ppermute only.
A program may use at most 128 MiB of HBM per device.

```python
import math
import jax
import jax.numpy as jnp
from jax import lax

HEADS = 32
KD = 16
VD = 128
WINDOW = 64
D = 4096
FEAT = 273
SPAN = 1024
SEQ = 4096


def base_field(key):
    field = jnp.clip(jax.random.normal(key, (SEQ, HEADS, KD), jnp.float32), -4.0, 4.0)
    return field


def draw_queries(key, part):
    field = base_field(jax.random.fold_in(key, 2))
    return field.reshape(SEQ, HEADS * KD).astype(jnp.bfloat16)


def draw_keys(key, part):
    field = base_field(jax.random.fold_in(key, 3))
    return field.reshape(SEQ, HEADS * KD).astype(jnp.bfloat16)


def level_of(own_key, dims, shards, least, top_value):
    factor_of, own = 1.0, jax.random.fold_in(own_key, 6)
    for dim, parts in shards:
        draws = jnp.exp(jax.random.uniform(jax.random.fold_in(own, dim), (parts,), jnp.float32, least / len(shards), top_value / len(shards)))
        factor_of = factor_of * jnp.repeat(draws, dims[dim] // parts).reshape([-1 if axis == dim else 1 for axis in range(len(dims))])
    return factor_of


def gaussian(rng, shape, width, limit, cuts=(), kind=jnp.bfloat16):
    result = jax.random.normal(rng, shape, jnp.float32) * width
    if len(cuts) > 0:
        result = level_of(rng, shape, cuts, -0.22, 0.18) * result
    return jnp.clip(result, min=-limit, max=limit).astype(kind)


def setup_inputs(seed: int = 0, part: int = 0) -> dict:
    streams_of = jax.random.split(jax.random.key(seed), 5)
    own_keys = jax.random.split(jax.random.fold_in(streams_of[4], part), 5)
    return {
        "queries": draw_queries(jax.random.fold_in(jax.random.fold_in(streams_of[4], part), 71), part),
        "keys": draw_keys(jax.random.fold_in(jax.random.fold_in(streams_of[4], part), 71), part),
        "values": gaussian(own_keys[2], (SEQ, D), 1.0, 6.0, ((0, 16),)),
        "gain": jnp.clip(1.0 + 0.1 * jax.random.normal(streams_of[3], (D,), jnp.float32), 0.5, 1.5),
    }


outer_scale = 1.0 / (4.0 * math.sqrt(2.0))
epsilon = 1e-06

def feature_map(vector):
    products = (vector[:, :, None] * vector[:, None, :]).reshape(vector.shape[0], vector.shape[1] * vector.shape[1])
    unit_column = jnp.ones((vector.shape[0], 1), jnp.float32)
    return jnp.concatenate([unit_column, vector * 0.5, products * outer_scale], axis=1)

def reference(queries, keys, values, gain):
    length = queries.shape[0]
    block_rows = min(512, SPAN)
    block_count = length // block_rows

    def one_head(head_index):
        head_index = head_index.astype(jnp.int32)
        query_head = lax.dynamic_slice_in_dim(queries, head_index * KD, KD, 1)
        key_head = lax.dynamic_slice_in_dim(keys, head_index * KD, KD, 1)
        value_head = lax.dynamic_slice_in_dim(values, head_index * VD, VD, 1)
        key_pad = jnp.concatenate([jnp.zeros((WINDOW, KD), jnp.bfloat16), key_head], axis=0)
        value_pad = jnp.concatenate([jnp.zeros((WINDOW, VD), jnp.bfloat16), value_head], axis=0)
        gain_head = lax.dynamic_slice_in_dim(gain, head_index * VD, VD, 0)

        def block_step(state, block_index):
            start = (block_index * block_rows).astype(jnp.int32)
            query_block = lax.dynamic_slice_in_dim(query_head, start, block_rows, 0)
            key_block = lax.dynamic_slice_in_dim(key_head, start, block_rows, 0)
            value_block = lax.dynamic_slice_in_dim(value_head, start, block_rows, 0)
            key_window = lax.dynamic_slice_in_dim(key_pad, start, block_rows + WINDOW, 0)
            value_window = lax.dynamic_slice_in_dim(value_pad, start, block_rows + WINDOW, 0)
            scores = jnp.dot(query_block, key_block.T, preferred_element_type=jnp.float32) * 0.25
            row_pos = jnp.arange(block_rows)[:, None]
            col_pos = jnp.arange(block_rows)[None, :]
            kernel = jnp.where(col_pos <= row_pos, 1.0 + scores + 0.5 * scores * scores, 0.0).astype(jnp.bfloat16)
            intra = jnp.dot(kernel, value_block, preferred_element_type=jnp.float32)
            query_feat = feature_map(query_block.astype(jnp.float32)).astype(jnp.bfloat16)
            key_feat = feature_map(key_block.astype(jnp.float32)).astype(jnp.bfloat16)
            inter = jnp.dot(query_feat, state.astype(jnp.bfloat16), preferred_element_type=jnp.float32)
            state = state + jnp.dot(key_feat.T, value_block, preferred_element_type=jnp.float32)
            window_scores = jnp.dot(query_block, key_window.T, preferred_element_type=jnp.float32) * 0.25
            key_pos = jnp.arange(block_rows + WINDOW)[None, :] - WINDOW
            valid = (key_pos <= row_pos) & (key_pos > row_pos - WINDOW) & (start + key_pos >= 0)
            masked = jnp.where(valid, window_scores, -jnp.inf)
            highest_score = lax.optimization_barrier(jnp.max(masked, axis=1, keepdims=True))
            expo = jnp.where(valid, jnp.exp(window_scores - highest_score), 0.0)
            weights = (expo / lax.optimization_barrier(jnp.sum(expo, axis=1, keepdims=True))).astype(jnp.bfloat16)
            window_out = jnp.dot(weights, value_window, preferred_element_type=jnp.float32)
            return (state, (intra + inter, window_out))
        initial = jnp.zeros((FEAT, VD), jnp.float32)
        final_state, (linear, window) = lax.scan(block_step, initial, jnp.arange(block_count))
        linear = linear.reshape(length, VD)
        window = window.reshape(length, VD)
        scale = lax.rsqrt(lax.optimization_barrier(jnp.mean(linear * linear, axis=1, keepdims=True)) + epsilon)
        return (linear * scale * gain_head + window).astype(jnp.bfloat16)
    outputs = lax.map(one_head, jnp.arange(HEADS))
    return jnp.transpose(outputs, (1, 0, 2)).reshape(length, HEADS * VD)
```

```python
import math

import jax
import jax.numpy as jnp
from jax import lax
from jax.sharding import PartitionSpec as P

HEADS = 32
KD = 16
VD = 128
WINDOW = 64


outer_scale = 1.0 / (4.0 * math.sqrt(2.0))
epsilon = 1e-06


def shifted(shard, axis, by):
    peers = lax.axis_size(axis)
    pairs = [(i, i + by) for i in range(peers) if 0 <= i + by < peers]
    return lax.ppermute(shard, axis, pairs)


def unique_features(vector, doubled):
    lead = vector.shape[:-1]
    pieces = [jnp.ones(lead + (1,), jnp.bfloat16), (vector * 0.5).astype(jnp.bfloat16)]
    for i in range(KD):
        prod = ((vector[..., i : i + 1] * vector[..., i:]) * outer_scale).astype(jnp.bfloat16)
        if doubled and i + 1 < KD:
            prod = jnp.concatenate([prod[..., :1], prod[..., 1:] * 2], axis=-1)
        pieces.append(prod)
    return jnp.concatenate(pieces, axis=-1)


def per_device(queries, keys, values, gain):
    local_tokens = queries.shape[0]
    query_tok = queries.reshape(local_tokens, HEADS, KD)
    key_tok = keys.reshape(local_tokens, HEADS, KD)
    value_tok = values.reshape(local_tokens, HEADS, VD)
    query_head, key_head, value_head = (
        lax.all_to_all(query_tok, "head", split_axis=1, concat_axis=0, tiled=True),
        lax.all_to_all(key_tok, "head", split_axis=1, concat_axis=0, tiled=True),
        lax.all_to_all(value_tok, "head", split_axis=1, concat_axis=0, tiled=True),
    )
    span_rows = query_head.shape[0]
    heads_here = query_head.shape[1]
    block_rows = min(512, span_rows)
    block_count = span_rows // block_rows
    first_span = lax.axis_index("ctx") == 0

    key_feat = unique_features(key_head.astype(jnp.float32), False)
    feat = key_feat.shape[-1]
    block_states = jnp.einsum(
        "nrhf,nrhv->nhfv",
        key_feat.reshape(block_count, block_rows, heads_here, feat),
        value_head.reshape(block_count, block_rows, heads_here, VD),
        preferred_element_type=jnp.float32,
    )
    span_state = jnp.sum(block_states, axis=0)
    everything = lax.all_gather(span_state, "ctx")
    peers = everything.shape[0]
    here = lax.axis_index("ctx")
    entering = jnp.sum(
        jnp.where(
            (jnp.arange(peers) < here)[:, None, None, None], everything, jnp.zeros_like(everything)
        ),
        axis=0,
    )
    before = jnp.concatenate(
        [jnp.zeros_like(block_states[:1]), jnp.cumsum(block_states[:-1], axis=0)], axis=0
    )
    states = (before + entering[None]).astype(jnp.bfloat16)

    query_blocks = query_head.reshape(block_count, block_rows, heads_here, KD)
    key_blocks = key_head.reshape(block_count, block_rows, heads_here, KD)
    value_blocks = value_head.reshape(block_count, block_rows, heads_here, VD)
    scores = (
        jnp.einsum("nrhd,nshd->nhrs", query_blocks, key_blocks, preferred_element_type=jnp.float32)
        * 0.25
    )
    row_pos = jnp.arange(block_rows)[:, None]
    col_pos = jnp.arange(block_rows)[None, :]
    kernel = jnp.where(col_pos <= row_pos, 1.0 + scores + 0.5 * scores * scores, 0.0).astype(
        jnp.bfloat16
    )
    intra = jnp.einsum("nhrs,nshv->nrhv", kernel, value_blocks, preferred_element_type=jnp.float32)
    query_feat = unique_features(query_blocks.astype(jnp.float32), True)
    inter = jnp.einsum("nrhf,nhfv->nrhv", query_feat, states, preferred_element_type=jnp.float32)
    linear = (intra + inter).reshape(span_rows, heads_here, VD)

    tail_keys, tail_values = shifted(
        (key_head[span_rows - WINDOW :], value_head[span_rows - WINDOW :]), "ctx", 1
    )
    chunks = span_rows // WINDOW
    key_prev = jnp.concatenate([tail_keys, key_head[: span_rows - WINDOW]], axis=0)
    value_prev = jnp.concatenate([tail_values, value_head[: span_rows - WINDOW]], axis=0)
    key_win = jnp.concatenate(
        [
            key_prev.reshape(chunks, WINDOW, heads_here, KD),
            key_head.reshape(chunks, WINDOW, heads_here, KD),
        ],
        axis=1,
    )
    value_win = jnp.concatenate(
        [
            value_prev.reshape(chunks, WINDOW, heads_here, VD),
            value_head.reshape(chunks, WINDOW, heads_here, VD),
        ],
        axis=1,
    )
    query_chunks = query_head.reshape(chunks, WINDOW, heads_here, KD)
    window_scores = (
        jnp.einsum("crhd,cphd->chrp", query_chunks, key_win, preferred_element_type=jnp.float32)
        * 0.25
    )
    r_pos = jnp.arange(WINDOW)[:, None]
    p_pos = jnp.arange(2 * WINDOW)[None, :]
    chunk_pos = jnp.arange(chunks)[:, None, None, None]
    valid = (p_pos > r_pos) & (p_pos <= r_pos + WINDOW)
    valid = valid[None, None] & ((chunk_pos > 0) | (p_pos >= WINDOW) | jnp.logical_not(first_span))
    masked = jnp.where(valid, window_scores, -jnp.inf)
    highest_score = jnp.max(masked, axis=3, keepdims=True)
    expo = jnp.where(valid, jnp.exp(window_scores - highest_score), 0.0)
    weights = (expo / jnp.sum(expo, axis=3, keepdims=True)).astype(jnp.bfloat16)
    window = jnp.einsum(
        "chrp,cphv->crhv", weights, value_win, preferred_element_type=jnp.float32
    ).reshape(span_rows, heads_here, VD)

    scale = lax.rsqrt(jnp.mean(linear * linear, axis=2, keepdims=True) + epsilon)
    gains = gain.reshape(heads_here, VD)
    mixed = (linear * scale * gains + window).astype(jnp.bfloat16)
    tokens_back = lax.all_to_all(mixed, "head", split_axis=0, concat_axis=1, tiled=True)
    return tokens_back.reshape(tokens_back.shape[0], HEADS * VD)


def solution(mesh):
    placed = (
        P(("groups", "ctx", "head"), None),
        P(("groups", "ctx", "head"), None),
        P(("groups", "ctx", "head"), None),
        P("head"),
    )
    return jax.shard_map(
        per_device,
        mesh=mesh,
        in_specs=placed,
        out_specs=P(("groups", "ctx", "head"), None),
        check_vma=False,
    )
```

```python
import math

import jax
import numpy as np
import jax.numpy as jnp
from jax import lax
from jax.sharding import PartitionSpec as P

HEADS = 32
KD = 16
VD = 128
WINDOW = 64


outer_scale = 1.0 / (4.0 * math.sqrt(2.0))
epsilon = 1e-06


def shifted(shard, axis, by):
    peers = lax.axis_size(axis)
    pairs = [(i, i + by) for i in range(peers) if 0 <= i + by < peers]
    return lax.ppermute(shard, axis, pairs)


def unique_features(vector, doubled):
    rows, cols = np.triu_indices(KD)
    pick_rows = jnp.asarray(np.eye(KD)[:, rows], jnp.bfloat16)
    pick_cols = jnp.asarray(np.eye(KD)[:, cols], jnp.bfloat16)
    first = jnp.einsum("...d,df->...f", vector, pick_rows, preferred_element_type=jnp.float32)
    second = jnp.einsum("...d,df->...f", vector, pick_cols, preferred_element_type=jnp.float32)
    prod = ((first * second) * outer_scale).astype(jnp.bfloat16)
    if doubled:
        prod = prod * jnp.asarray(np.where(rows == cols, 1.0, 2.0), jnp.bfloat16)
    lead = vector.shape[:-1]
    unit = jnp.ones(lead + (1,), jnp.bfloat16)
    half = (vector.astype(jnp.float32) * 0.5).astype(jnp.bfloat16)
    return jnp.concatenate([unit, half, prod], axis=-1)


def per_device(queries, keys, values, gain):
    local_tokens = queries.shape[0]
    query_tok = queries.reshape(local_tokens, HEADS, KD)
    key_tok = keys.reshape(local_tokens, HEADS, KD)
    value_tok = values.reshape(local_tokens, HEADS, VD)
    query_head, key_head, value_head = (
        lax.all_to_all(query_tok, "head", split_axis=1, concat_axis=0, tiled=True),
        lax.all_to_all(key_tok, "head", split_axis=1, concat_axis=0, tiled=True),
        lax.all_to_all(value_tok, "head", split_axis=1, concat_axis=0, tiled=True),
    )
    span_rows = query_head.shape[0]
    heads_here = query_head.shape[1]
    block_rows = min(512, span_rows)
    block_count = span_rows // block_rows
    first_span = lax.axis_index("ctx") == 0

    key_feat = unique_features(key_head, False)
    feat = key_feat.shape[-1]
    block_states = jnp.einsum(
        "nrhf,nrhv->nhfv",
        key_feat.reshape(block_count, block_rows, heads_here, feat),
        value_head.reshape(block_count, block_rows, heads_here, VD),
        preferred_element_type=jnp.float32,
    )
    span_state = jnp.sum(block_states, axis=0)
    everything = lax.all_gather(span_state, "ctx")
    peers = everything.shape[0]
    here = lax.axis_index("ctx")
    entering = jnp.sum(
        jnp.where(
            (jnp.arange(peers) < here)[:, None, None, None], everything, jnp.zeros_like(everything)
        ),
        axis=0,
    )
    before = jnp.concatenate(
        [jnp.zeros_like(block_states[:1]), jnp.cumsum(block_states[:-1], axis=0)], axis=0
    )
    states = (before + entering[None]).astype(jnp.bfloat16)

    query_blocks = query_head.reshape(block_count, block_rows, heads_here, KD)
    key_blocks = key_head.reshape(block_count, block_rows, heads_here, KD)
    value_blocks = value_head.reshape(block_count, block_rows, heads_here, VD)
    scores = (
        jnp.einsum("nrhd,nshd->nhrs", query_blocks, key_blocks, preferred_element_type=jnp.float32)
        * 0.25
    )
    row_pos = jnp.arange(block_rows)[:, None]
    col_pos = jnp.arange(block_rows)[None, :]
    kernel = jnp.where(col_pos <= row_pos, 1.0 + scores + 0.5 * scores * scores, 0.0).astype(
        jnp.bfloat16
    )
    intra = jnp.einsum("nhrs,nshv->nrhv", kernel, value_blocks, preferred_element_type=jnp.float32)
    query_feat = unique_features(query_blocks, True)
    inter = jnp.einsum("nrhf,nhfv->nrhv", query_feat, states, preferred_element_type=jnp.float32)
    linear = (intra + inter).reshape(span_rows, heads_here, VD)

    tail_keys, tail_values = shifted(
        (key_head[span_rows - WINDOW :], value_head[span_rows - WINDOW :]), "ctx", 1
    )
    chunks = span_rows // WINDOW
    key_prev = jnp.concatenate([tail_keys, key_head[: span_rows - WINDOW]], axis=0)
    value_prev = jnp.concatenate([tail_values, value_head[: span_rows - WINDOW]], axis=0)
    key_win = jnp.concatenate(
        [
            key_prev.reshape(chunks, WINDOW, heads_here, KD),
            key_head.reshape(chunks, WINDOW, heads_here, KD),
        ],
        axis=1,
    )
    value_win = jnp.concatenate(
        [
            value_prev.reshape(chunks, WINDOW, heads_here, VD),
            value_head.reshape(chunks, WINDOW, heads_here, VD),
        ],
        axis=1,
    )
    query_chunks = query_head.reshape(chunks, WINDOW, heads_here, KD)
    window_scores = (
        jnp.einsum("crhd,cphd->chrp", query_chunks, key_win, preferred_element_type=jnp.float32)
        * 0.25
    )
    r_pos = jnp.arange(WINDOW)[:, None]
    p_pos = jnp.arange(2 * WINDOW)[None, :]
    chunk_pos = jnp.arange(chunks)[:, None, None, None]
    valid = (p_pos > r_pos) & (p_pos <= r_pos + WINDOW)
    valid = valid[None, None] & ((chunk_pos > 0) | (p_pos >= WINDOW) | jnp.logical_not(first_span))
    masked = jnp.where(valid, window_scores, -jnp.inf)
    highest_score = jnp.max(masked, axis=3, keepdims=True)
    expo = jnp.where(valid, jnp.exp(window_scores - highest_score), 0.0)
    weights = (expo / jnp.sum(expo, axis=3, keepdims=True)).astype(jnp.bfloat16)
    window = jnp.einsum(
        "chrp,cphv->crhv", weights, value_win, preferred_element_type=jnp.float32
    ).reshape(span_rows, heads_here, VD)

    scale = lax.rsqrt(jnp.mean(linear * linear, axis=2, keepdims=True) + epsilon)
    gains = gain.reshape(heads_here, VD)
    mixed = (linear * scale * gains + window).astype(jnp.bfloat16)
    tokens_back = lax.all_to_all(mixed, "head", split_axis=0, concat_axis=1, tiled=True)
    return tokens_back.reshape(tokens_back.shape[0], HEADS * VD)


def solution(mesh):
    placed = (
        P(("groups", "ctx", "head"), None),
        P(("groups", "ctx", "head"), None),
        P(("groups", "ctx", "head"), None),
        P("head"),
    )
    return jax.shard_map(
        per_device,
        mesh=mesh,
        in_specs=placed,
        out_specs=P(("groups", "ctx", "head"), None),
        check_vma=False,
    )
```

```python
import math

import jax
import numpy as np
import jax.numpy as jnp
from jax import lax
from jax.sharding import PartitionSpec as P

HEADS = 32
KD = 16
VD = 128
WINDOW = 64


outer_scale = 1.0 / (4.0 * math.sqrt(2.0))
epsilon = 1e-06


def shifted(shard, axis, by):
    peers = lax.axis_size(axis)
    pairs = [(i, i + by) for i in range(peers) if 0 <= i + by < peers]
    return lax.ppermute(shard, axis, pairs)


def unique_features(vector, doubled):
    rows, cols = np.triu_indices(KD)
    pick_rows = jnp.asarray(np.eye(KD)[:, rows], jnp.bfloat16)
    pick_cols = jnp.asarray(np.eye(KD)[:, cols], jnp.bfloat16)
    first = jnp.einsum("...d,df->...f", vector, pick_rows, preferred_element_type=jnp.float32)
    second = jnp.einsum("...d,df->...f", vector, pick_cols, preferred_element_type=jnp.float32)
    prod = ((first * second) * outer_scale).astype(jnp.bfloat16)
    if doubled:
        prod = prod * jnp.asarray(np.where(rows == cols, 1.0, 2.0), jnp.bfloat16)
    lead = vector.shape[:-1]
    unit = jnp.ones(lead + (1,), jnp.bfloat16)
    half = (vector.astype(jnp.float32) * 0.5).astype(jnp.bfloat16)
    return jnp.concatenate([unit, half, prod], axis=-1)


def per_device(queries, keys, values, gain):
    local_tokens = queries.shape[0]
    query_tok = queries.reshape(local_tokens, HEADS, KD)
    key_tok = keys.reshape(local_tokens, HEADS, KD)
    value_tok = values.reshape(local_tokens, HEADS, VD)
    packed = jnp.concatenate([query_tok, key_tok, value_tok], axis=2)
    packed = lax.all_to_all(packed, "head", split_axis=1, concat_axis=0, tiled=True)
    query_head = packed[:, :, :KD]
    key_head = packed[:, :, KD : 2 * KD]
    value_head = packed[:, :, 2 * KD :]
    span_rows = query_head.shape[0]
    heads_here = query_head.shape[1]
    block_rows = min(512, span_rows)
    block_count = span_rows // block_rows
    first_span = lax.axis_index("ctx") == 0

    key_feat = unique_features(key_head, False)
    feat = key_feat.shape[-1]
    block_states = jnp.einsum(
        "nrhf,nrhv->nhfv",
        key_feat.reshape(block_count, block_rows, heads_here, feat),
        value_head.reshape(block_count, block_rows, heads_here, VD),
        preferred_element_type=jnp.float32,
    )
    span_state = jnp.sum(block_states, axis=0)
    everything = lax.all_gather(span_state.astype(jnp.bfloat16), "ctx").astype(jnp.float32)
    peers = everything.shape[0]
    here = lax.axis_index("ctx")
    entering = jnp.sum(
        jnp.where(
            (jnp.arange(peers) < here)[:, None, None, None], everything, jnp.zeros_like(everything)
        ),
        axis=0,
    )
    before = jnp.concatenate(
        [jnp.zeros_like(block_states[:1]), jnp.cumsum(block_states[:-1], axis=0)], axis=0
    )
    states = (before + entering[None]).astype(jnp.bfloat16)

    query_blocks = query_head.reshape(block_count, block_rows, heads_here, KD)
    key_blocks = key_head.reshape(block_count, block_rows, heads_here, KD)
    value_blocks = value_head.reshape(block_count, block_rows, heads_here, VD)
    scores = (
        jnp.einsum("nrhd,nshd->nhrs", query_blocks, key_blocks, preferred_element_type=jnp.float32)
        * 0.25
    )
    row_pos = jnp.arange(block_rows)[:, None]
    col_pos = jnp.arange(block_rows)[None, :]
    kernel = jnp.where(col_pos <= row_pos, 1.0 + scores + 0.5 * scores * scores, 0.0).astype(
        jnp.bfloat16
    )
    intra = jnp.einsum("nhrs,nshv->nrhv", kernel, value_blocks, preferred_element_type=jnp.float32)
    query_feat = unique_features(query_blocks, True)
    inter = jnp.einsum("nrhf,nhfv->nrhv", query_feat, states, preferred_element_type=jnp.float32)
    linear = (intra + inter).reshape(span_rows, heads_here, VD)

    tail_keys, tail_values = shifted(
        (key_head[span_rows - WINDOW :], value_head[span_rows - WINDOW :]), "ctx", 1
    )
    chunks = span_rows // WINDOW
    key_prev = jnp.concatenate([tail_keys, key_head[: span_rows - WINDOW]], axis=0)
    value_prev = jnp.concatenate([tail_values, value_head[: span_rows - WINDOW]], axis=0)
    key_win = jnp.concatenate(
        [
            key_prev.reshape(chunks, WINDOW, heads_here, KD),
            key_head.reshape(chunks, WINDOW, heads_here, KD),
        ],
        axis=1,
    )
    value_win = jnp.concatenate(
        [
            value_prev.reshape(chunks, WINDOW, heads_here, VD),
            value_head.reshape(chunks, WINDOW, heads_here, VD),
        ],
        axis=1,
    )
    query_chunks = query_head.reshape(chunks, WINDOW, heads_here, KD)
    window_scores = (
        jnp.einsum("crhd,cphd->chrp", query_chunks, key_win, preferred_element_type=jnp.float32)
        * 0.25
    )
    r_pos = jnp.arange(WINDOW)[:, None]
    p_pos = jnp.arange(2 * WINDOW)[None, :]
    chunk_pos = jnp.arange(chunks)[:, None, None, None]
    valid = (p_pos > r_pos) & (p_pos <= r_pos + WINDOW)
    valid = valid[None, None] & ((chunk_pos > 0) | (p_pos >= WINDOW) | jnp.logical_not(first_span))
    masked = jnp.where(valid, window_scores, -jnp.inf)
    highest_score = jnp.max(masked, axis=3, keepdims=True)
    expo = jnp.where(valid, jnp.exp(window_scores - highest_score), 0.0)
    weights = (expo / jnp.sum(expo, axis=3, keepdims=True)).astype(jnp.bfloat16)
    window = jnp.einsum(
        "chrp,cphv->crhv", weights, value_win, preferred_element_type=jnp.float32
    ).reshape(span_rows, heads_here, VD)

    scale = lax.rsqrt(jnp.mean(linear * linear, axis=2, keepdims=True) + epsilon)
    gains = gain.reshape(heads_here, VD)
    mixed = (linear * scale * gains + window).astype(jnp.bfloat16)
    tokens_back = lax.all_to_all(mixed, "head", split_axis=0, concat_axis=1, tiled=True)
    return tokens_back.reshape(tokens_back.shape[0], HEADS * VD)


def solution(mesh):
    placed = (
        P(("groups", "ctx", "head"), None),
        P(("groups", "ctx", "head"), None),
        P(("groups", "ctx", "head"), None),
        P("head"),
    )
    return jax.shard_map(
        per_device,
        mesh=mesh,
        in_specs=placed,
        out_specs=P(("groups", "ctx", "head"), None),
        check_vma=False,
    )
```

```python
import math

import jax
import numpy as np
import jax.numpy as jnp
from jax import lax
from jax.sharding import PartitionSpec as P

HEADS = 32
KD = 16
VD = 128
WINDOW = 64


outer_scale = 1.0 / (4.0 * math.sqrt(2.0))
epsilon = 1e-06


def shifted(shard, axis, by):
    peers = lax.axis_size(axis)
    pairs = [(i, i + by) for i in range(peers) if 0 <= i + by < peers]
    return lax.ppermute(shard, axis, pairs)


def unique_features(vector, doubled):
    rows, cols = np.triu_indices(KD)
    pick_rows = jnp.asarray(np.eye(KD)[:, rows], jnp.bfloat16)
    pick_cols = jnp.asarray(np.eye(KD)[:, cols], jnp.bfloat16)
    first = jnp.einsum("...d,df->...f", vector, pick_rows, preferred_element_type=jnp.float32)
    second = jnp.einsum("...d,df->...f", vector, pick_cols, preferred_element_type=jnp.float32)
    prod = ((first * second) * outer_scale).astype(jnp.bfloat16)
    if doubled:
        prod = prod * jnp.asarray(np.where(rows == cols, 1.0, 2.0), jnp.bfloat16)
    lead = vector.shape[:-1]
    unit = jnp.ones(lead + (1,), jnp.bfloat16)
    half = (vector.astype(jnp.float32) * 0.5).astype(jnp.bfloat16)
    return jnp.concatenate([unit, half, prod], axis=-1)


def attend(query_head, key_head, value_head, gains, first_span):
    span_rows = query_head.shape[0]
    heads_here = query_head.shape[1]
    block_rows = min(512, span_rows)
    block_count = span_rows // block_rows

    key_feat = unique_features(key_head, False)
    feat = key_feat.shape[-1]
    block_states = jnp.einsum(
        "nrhf,nrhv->nhfv",
        key_feat.reshape(block_count, block_rows, heads_here, feat),
        value_head.reshape(block_count, block_rows, heads_here, VD),
        preferred_element_type=jnp.float32,
    )
    span_state = jnp.sum(block_states, axis=0)
    everything = lax.all_gather(span_state, "ctx")
    peers = everything.shape[0]
    here = lax.axis_index("ctx")
    entering = jnp.sum(
        jnp.where(
            (jnp.arange(peers) < here)[:, None, None, None], everything, jnp.zeros_like(everything)
        ),
        axis=0,
    )
    before = jnp.concatenate(
        [jnp.zeros_like(block_states[:1]), jnp.cumsum(block_states[:-1], axis=0)], axis=0
    )
    states = (before + entering[None]).astype(jnp.bfloat16)

    query_blocks = query_head.reshape(block_count, block_rows, heads_here, KD)
    key_blocks = key_head.reshape(block_count, block_rows, heads_here, KD)
    value_blocks = value_head.reshape(block_count, block_rows, heads_here, VD)
    scores = (
        jnp.einsum("nrhd,nshd->nhrs", query_blocks, key_blocks, preferred_element_type=jnp.float32)
        * 0.25
    )
    row_pos = jnp.arange(block_rows)[:, None]
    col_pos = jnp.arange(block_rows)[None, :]
    kernel = jnp.where(col_pos <= row_pos, 1.0 + scores + 0.5 * scores * scores, 0.0).astype(
        jnp.bfloat16
    )
    intra = jnp.einsum("nhrs,nshv->nrhv", kernel, value_blocks, preferred_element_type=jnp.float32)
    query_feat = unique_features(query_blocks, True)
    inter = jnp.einsum("nrhf,nhfv->nrhv", query_feat, states, preferred_element_type=jnp.float32)
    linear = (intra + inter).reshape(span_rows, heads_here, VD)

    tails = shifted(
        jnp.concatenate([key_head, value_head], axis=2)[span_rows - WINDOW :], "ctx", 1
    )
    tail_keys = tails[:, :, :KD]
    tail_values = tails[:, :, KD:]
    chunks = span_rows // WINDOW
    key_prev = jnp.concatenate([tail_keys, key_head[: span_rows - WINDOW]], axis=0)
    value_prev = jnp.concatenate([tail_values, value_head[: span_rows - WINDOW]], axis=0)
    key_win = jnp.concatenate(
        [
            key_prev.reshape(chunks, WINDOW, heads_here, KD),
            key_head.reshape(chunks, WINDOW, heads_here, KD),
        ],
        axis=1,
    )
    value_win = jnp.concatenate(
        [
            value_prev.reshape(chunks, WINDOW, heads_here, VD),
            value_head.reshape(chunks, WINDOW, heads_here, VD),
        ],
        axis=1,
    )
    query_chunks = query_head.reshape(chunks, WINDOW, heads_here, KD)
    window_scores = (
        jnp.einsum("crhd,cphd->chrp", query_chunks, key_win, preferred_element_type=jnp.float32)
        * 0.25
    )
    r_pos = jnp.arange(WINDOW)[:, None]
    p_pos = jnp.arange(2 * WINDOW)[None, :]
    chunk_pos = jnp.arange(chunks)[:, None, None, None]
    valid = (p_pos > r_pos) & (p_pos <= r_pos + WINDOW)
    valid = valid[None, None] & ((chunk_pos > 0) | (p_pos >= WINDOW) | jnp.logical_not(first_span))
    masked = jnp.where(valid, window_scores, -jnp.inf)
    highest_score = jnp.max(masked, axis=3, keepdims=True)
    expo = jnp.where(valid, jnp.exp(window_scores - highest_score), 0.0)
    weights = (expo / jnp.sum(expo, axis=3, keepdims=True)).astype(jnp.bfloat16)
    window = jnp.einsum(
        "chrp,cphv->crhv", weights, value_win, preferred_element_type=jnp.float32
    ).reshape(span_rows, heads_here, VD)

    scale = lax.rsqrt(jnp.mean(linear * linear, axis=2, keepdims=True) + epsilon)
    return (linear * scale * gains + window).astype(jnp.bfloat16)


def per_device(queries, keys, values, gain):
    local_tokens = queries.shape[0]
    peers = lax.axis_size("head")
    heads_here = HEADS // peers
    groups = 2 if heads_here % 2 == 0 else 1
    group_heads = heads_here // groups
    query_tok = queries.reshape(local_tokens, peers, groups, group_heads, KD)
    key_tok = keys.reshape(local_tokens, peers, groups, group_heads, KD)
    value_tok = values.reshape(local_tokens, peers, groups, group_heads, VD)
    gains = gain.reshape(groups, group_heads, VD)
    first_span = lax.axis_index("ctx") == 0
    span_rows = local_tokens * peers

    def gathered(tok, g, width):
        moved = lax.all_to_all(tok[:, :, g], "head", split_axis=1, concat_axis=0, tiled=True)
        return moved.reshape(span_rows, group_heads, width)

    outs = []
    for g in range(groups):
        mixed = attend(
            gathered(query_tok, g, KD),
            gathered(key_tok, g, KD),
            gathered(value_tok, g, VD),
            gains[g],
            first_span,
        )
        back = lax.all_to_all(mixed, "head", split_axis=0, concat_axis=1, tiled=True)
        outs.append(back.reshape(local_tokens, peers, group_heads, VD))
    tokens_back = jnp.stack(outs, axis=2)
    return tokens_back.reshape(local_tokens, HEADS * VD)


def solution(mesh):
    placed = (
        P(("groups", "ctx", "head"), None),
        P(("groups", "ctx", "head"), None),
        P(("groups", "ctx", "head"), None),
        P("head"),
    )
    return jax.shard_map(
        per_device,
        mesh=mesh,
        in_specs=placed,
        out_specs=P(("groups", "ctx", "head"), None),
        check_vma=False,
    )
```

```python
import math

import jax
import numpy as np
import jax.numpy as jnp
from jax import lax
from jax.experimental import pallas as pl
from jax.experimental.pallas import tpu as pltpu
from jax.sharding import PartitionSpec as P

HEADS = 32
KD = 16
VD = 128
WINDOW = 64


outer_scale = 1.0 / (4.0 * math.sqrt(2.0))
epsilon = 1e-06


def shifted(shard, axis, by):
    peers = lax.axis_size(axis)
    pairs = [(i, i + by) for i in range(peers) if 0 <= i + by < peers]
    return lax.ppermute(shard, axis, pairs)


def unique_features(vector, doubled):
    rows, cols = np.triu_indices(KD)
    pick_rows = jnp.asarray(np.eye(KD)[:, rows], jnp.bfloat16)
    pick_cols = jnp.asarray(np.eye(KD)[:, cols], jnp.bfloat16)
    first = jnp.einsum("...d,df->...f", vector, pick_rows, preferred_element_type=jnp.float32)
    second = jnp.einsum("...d,df->...f", vector, pick_cols, preferred_element_type=jnp.float32)
    prod = ((first * second) * outer_scale).astype(jnp.bfloat16)
    if doubled:
        prod = prod * jnp.asarray(np.where(rows == cols, 1.0, 2.0), jnp.bfloat16)
    lead = vector.shape[:-1]
    unit = jnp.ones(lead + (1,), jnp.bfloat16)
    half = (vector.astype(jnp.float32) * 0.5).astype(jnp.bfloat16)
    return jnp.concatenate([unit, half, prod], axis=-1)


CHUNK = 128


def local_attention_kernel(flag_ref, q_ref, kx_ref, vx_ref, intra_ref, win_ref, *, span_rows, block_rows):
    first_span = flag_ref[0] == 1
    for i in range(span_rows // CHUNK):
        r0 = i * CHUNK
        q_c = q_ref[0, r0 : r0 + CHUNK, :]
        bs = (r0 // block_rows) * block_rows
        width = r0 + CHUNK - bs
        k_i = kx_ref[0, WINDOW + bs : WINDOW + r0 + CHUNK, :]
        v_i = vx_ref[WINDOW + bs : WINDOW + r0 + CHUNK, :]
        scores = (
            lax.dot_general(q_c, k_i, (((1,), (1,)), ((), ())), preferred_element_type=jnp.float32)
            * 0.25
        )
        row = lax.broadcasted_iota(jnp.int32, (CHUNK, width), 0)
        col = lax.broadcasted_iota(jnp.int32, (CHUNK, width), 1)
        kernel = jnp.where(
            col <= row + (r0 - bs), 1.0 + scores + 0.5 * scores * scores, 0.0
        ).astype(jnp.bfloat16)
        intra_ref[r0 : r0 + CHUNK, :] = jnp.dot(kernel, v_i, preferred_element_type=jnp.float32)

        k_w = kx_ref[0, r0 : r0 + CHUNK + WINDOW, :]
        v_w = vx_ref[r0 : r0 + CHUNK + WINDOW, :]
        ws = (
            lax.dot_general(q_c, k_w, (((1,), (1,)), ((), ())), preferred_element_type=jnp.float32)
            * 0.25
        )
        wrow = lax.broadcasted_iota(jnp.int32, (CHUNK, CHUNK + WINDOW), 0)
        wcol = lax.broadcasted_iota(jnp.int32, (CHUNK, CHUNK + WINDOW), 1)
        valid = (wcol > wrow) & (wcol <= wrow + WINDOW)
        if i == 0:
            valid = valid & ((wcol >= WINDOW) | jnp.logical_not(first_span))
        masked = jnp.where(valid, ws, -jnp.inf)
        highest = jnp.max(masked, axis=1, keepdims=True)
        expo = jnp.where(valid, jnp.exp(ws - highest), 0.0)
        weights = (expo / jnp.sum(expo, axis=1, keepdims=True)).astype(jnp.bfloat16)
        win_ref[r0 : r0 + CHUNK, :] = jnp.dot(weights, v_w, preferred_element_type=jnp.float32)


def local_attention(flag, q_hm, kx_hm, vx, block_rows):
    heads_here, span_rows, _ = q_hm.shape
    ext = kx_hm.shape[1]
    body = lambda *refs: local_attention_kernel(*refs, span_rows=span_rows, block_rows=block_rows)
    out = jax.ShapeDtypeStruct((span_rows, heads_here * VD), jnp.float32)
    return pl.pallas_call(
        body,
        grid_spec=pltpu.PrefetchScalarGridSpec(
            num_scalar_prefetch=1,
            grid=(heads_here,),
            in_specs=[
                pl.BlockSpec((1, span_rows, KD), lambda h, f: (h, 0, 0)),
                pl.BlockSpec((1, ext, KD), lambda h, f: (h, 0, 0)),
                pl.BlockSpec((ext, VD), lambda h, f: (0, h)),
            ],
            out_specs=[
                pl.BlockSpec((span_rows, VD), lambda h, f: (0, h)),
                pl.BlockSpec((span_rows, VD), lambda h, f: (0, h)),
            ],
        ),
        out_shape=(out, out),
    )(flag, q_hm, kx_hm, vx)


def per_device(queries, keys, values, gain):
    local_tokens = queries.shape[0]
    query_tok = queries.reshape(local_tokens, HEADS, KD)
    key_tok = keys.reshape(local_tokens, HEADS, KD)
    value_tok = values.reshape(local_tokens, HEADS, VD)
    query_head, key_head, value_head = (
        lax.all_to_all(query_tok, "head", split_axis=1, concat_axis=0, tiled=True),
        lax.all_to_all(key_tok, "head", split_axis=1, concat_axis=0, tiled=True),
        lax.all_to_all(value_tok, "head", split_axis=1, concat_axis=0, tiled=True),
    )
    span_rows = query_head.shape[0]
    heads_here = query_head.shape[1]
    block_rows = min(512, span_rows)
    block_count = span_rows // block_rows
    first_span = lax.axis_index("ctx") == 0

    key_feat = unique_features(key_head, False)
    feat = key_feat.shape[-1]
    block_states = jnp.einsum(
        "nrhf,nrhv->nhfv",
        key_feat.reshape(block_count, block_rows, heads_here, feat),
        value_head.reshape(block_count, block_rows, heads_here, VD),
        preferred_element_type=jnp.float32,
    )
    span_state = jnp.sum(block_states, axis=0)
    everything = lax.all_gather(span_state, "ctx")
    peers = everything.shape[0]
    here = lax.axis_index("ctx")
    entering = jnp.sum(
        jnp.where(
            (jnp.arange(peers) < here)[:, None, None, None], everything, jnp.zeros_like(everything)
        ),
        axis=0,
    )
    before = jnp.concatenate(
        [jnp.zeros_like(block_states[:1]), jnp.cumsum(block_states[:-1], axis=0)], axis=0
    )
    states = (before + entering[None]).astype(jnp.bfloat16)

    query_blocks = query_head.reshape(block_count, block_rows, heads_here, KD)
    query_feat = unique_features(query_blocks, True)
    inter = jnp.einsum("nrhf,nhfv->nrhv", query_feat, states, preferred_element_type=jnp.float32)

    tails = shifted(
        jnp.concatenate([key_head, value_head], axis=2)[span_rows - WINDOW :], "ctx", 1
    )
    key_ext = jnp.concatenate([tails[:, :, :KD], key_head], axis=0)
    value_ext = jnp.concatenate([tails[:, :, KD:], value_head], axis=0)
    flag = first_span.astype(jnp.int32).reshape(1)
    intra, window = local_attention(
        flag,
        jnp.transpose(query_head, (1, 0, 2)),
        jnp.transpose(key_ext, (1, 0, 2)),
        value_ext.reshape(span_rows + WINDOW, heads_here * VD),
        block_rows,
    )
    linear = intra.reshape(span_rows, heads_here, VD) + inter.reshape(span_rows, heads_here, VD)
    window = window.reshape(span_rows, heads_here, VD)

    scale = lax.rsqrt(jnp.mean(linear * linear, axis=2, keepdims=True) + epsilon)
    gains = gain.reshape(heads_here, VD)
    mixed = (linear * scale * gains + window).astype(jnp.bfloat16)
    tokens_back = lax.all_to_all(mixed, "head", split_axis=0, concat_axis=1, tiled=True)
    return tokens_back.reshape(tokens_back.shape[0], HEADS * VD)


def solution(mesh):
    placed = (
        P(("groups", "ctx", "head"), None),
        P(("groups", "ctx", "head"), None),
        P(("groups", "ctx", "head"), None),
        P("head"),
    )
    return jax.shard_map(
        per_device,
        mesh=mesh,
        in_specs=placed,
        out_specs=P(("groups", "ctx", "head"), None),
        check_vma=False,
    )
```

```python
import math

import jax
import numpy as np
import jax.numpy as jnp
from jax import lax
from jax.experimental import pallas as pl
from jax.experimental.pallas import tpu as pltpu
from jax.sharding import PartitionSpec as P

HEADS = 32
KD = 16
VD = 128
WINDOW = 64


outer_scale = 1.0 / (4.0 * math.sqrt(2.0))
epsilon = 1e-06


def shifted(shard, axis, by):
    peers = lax.axis_size(axis)
    pairs = [(i, i + by) for i in range(peers) if 0 <= i + by < peers]
    return lax.ppermute(shard, axis, pairs)


def unique_features(vector, doubled):
    rows, cols = np.triu_indices(KD)
    pick_rows = jnp.asarray(np.eye(KD)[:, rows], jnp.bfloat16)
    pick_cols = jnp.asarray(np.eye(KD)[:, cols], jnp.bfloat16)
    first = jnp.einsum("...d,df->...f", vector, pick_rows, preferred_element_type=jnp.float32)
    second = jnp.einsum("...d,df->...f", vector, pick_cols, preferred_element_type=jnp.float32)
    prod = ((first * second) * outer_scale).astype(jnp.bfloat16)
    if doubled:
        prod = prod * jnp.asarray(np.where(rows == cols, 1.0, 2.0), jnp.bfloat16)
    lead = vector.shape[:-1]
    unit = jnp.ones(lead + (1,), jnp.bfloat16)
    half = (vector.astype(jnp.float32) * 0.5).astype(jnp.bfloat16)
    return jnp.concatenate([unit, half, prod], axis=-1)


CHUNK = 128
LEAD = 128


def local_attention_kernel(flag_ref, q_ref, kt_ref, vx_ref, intra_ref, win_ref, *, span_rows, block_rows):
    first_span = flag_ref[0] == 1
    for i in range(span_rows // CHUNK):
        r0 = i * CHUNK
        q_c = q_ref[0, r0 : r0 + CHUNK, :]
        bs = (r0 // block_rows) * block_rows
        width = r0 + CHUNK - bs
        k_i = kt_ref[0, :, LEAD + bs : LEAD + r0 + CHUNK]
        v_i = vx_ref[LEAD + bs : LEAD + r0 + CHUNK, :]
        scores = jnp.dot(q_c, k_i, preferred_element_type=jnp.float32) * 0.25
        row = lax.broadcasted_iota(jnp.int32, (CHUNK, width), 0)
        col = lax.broadcasted_iota(jnp.int32, (CHUNK, width), 1)
        kernel = jnp.where(
            col <= row + (r0 - bs), 1.0 + scores + 0.5 * scores * scores, 0.0
        ).astype(jnp.bfloat16)
        intra_ref[r0 : r0 + CHUNK, :] = jnp.dot(kernel, v_i, preferred_element_type=jnp.float32)

        k_w = kt_ref[0, :, r0 : r0 + CHUNK + LEAD]
        v_w = vx_ref[r0 : r0 + CHUNK + LEAD, :]
        ws = jnp.dot(q_c, k_w, preferred_element_type=jnp.float32) * 0.25
        wrow = lax.broadcasted_iota(jnp.int32, (CHUNK, CHUNK + LEAD), 0)
        wcol = lax.broadcasted_iota(jnp.int32, (CHUNK, CHUNK + LEAD), 1)
        valid = (wcol > wrow + LEAD - WINDOW) & (wcol <= wrow + LEAD)
        if i == 0:
            valid = valid & ((wcol >= LEAD) | jnp.logical_not(first_span))
        masked = jnp.where(valid, ws, -jnp.inf)
        highest = jnp.max(masked, axis=1, keepdims=True)
        expo = jnp.where(valid, jnp.exp(ws - highest), 0.0)
        weights = (expo / jnp.sum(expo, axis=1, keepdims=True)).astype(jnp.bfloat16)
        win_ref[r0 : r0 + CHUNK, :] = jnp.dot(weights, v_w, preferred_element_type=jnp.float32)


def local_attention(flag, q_hm, kt_hm, vx, block_rows):
    heads_here, span_rows, _ = q_hm.shape
    ext = kt_hm.shape[2]
    body = lambda *refs: local_attention_kernel(*refs, span_rows=span_rows, block_rows=block_rows)
    out = jax.ShapeDtypeStruct((span_rows, heads_here * VD), jnp.float32)
    return pl.pallas_call(
        body,
        grid_spec=pltpu.PrefetchScalarGridSpec(
            num_scalar_prefetch=1,
            grid=(heads_here,),
            in_specs=[
                pl.BlockSpec((1, span_rows, KD), lambda h, f: (h, 0, 0)),
                pl.BlockSpec((1, KD, ext), lambda h, f: (h, 0, 0)),
                pl.BlockSpec((ext, VD), lambda h, f: (0, h)),
            ],
            out_specs=[
                pl.BlockSpec((span_rows, VD), lambda h, f: (0, h)),
                pl.BlockSpec((span_rows, VD), lambda h, f: (0, h)),
            ],
        ),
        out_shape=(out, out),
    )(flag, q_hm, kt_hm, vx)


def mix_kernel(intra_ref, inter_ref, win_ref, gain_ref, out_ref):
    linear = intra_ref[...] + inter_ref[0]
    scale = lax.rsqrt(jnp.mean(linear * linear, axis=1, keepdims=True) + epsilon)
    out_ref[...] = (linear * scale * gain_ref[...] + win_ref[...]).astype(jnp.bfloat16)


def mix(intra, inter_hm, window, gain):
    heads_here, span_rows, _ = inter_hm.shape
    tile = pl.BlockSpec((span_rows, VD), lambda h: (0, h))
    return pl.pallas_call(
        mix_kernel,
        grid=(heads_here,),
        in_specs=[
            tile,
            pl.BlockSpec((1, span_rows, VD), lambda h: (h, 0, 0)),
            tile,
            pl.BlockSpec((1, VD), lambda h: (0, h)),
        ],
        out_specs=tile,
        out_shape=jax.ShapeDtypeStruct((span_rows, heads_here * VD), jnp.bfloat16),
    )(intra, inter_hm, window, gain.reshape(1, heads_here * VD))


def per_device(queries, keys, values, gain):
    local_tokens = queries.shape[0]
    query_tok = queries.reshape(local_tokens, HEADS, KD)
    key_tok = keys.reshape(local_tokens, HEADS, KD)
    value_tok = values.reshape(local_tokens, HEADS, VD)
    query_head, key_head, value_head = (
        lax.all_to_all(query_tok, "head", split_axis=1, concat_axis=0, tiled=True),
        lax.all_to_all(key_tok, "head", split_axis=1, concat_axis=0, tiled=True),
        lax.all_to_all(value_tok, "head", split_axis=1, concat_axis=0, tiled=True),
    )
    span_rows = query_head.shape[0]
    heads_here = query_head.shape[1]
    block_rows = min(512, span_rows)
    block_count = span_rows // block_rows
    first_span = lax.axis_index("ctx") == 0
    query_hm = jnp.transpose(query_head, (1, 0, 2))
    key_hm = jnp.transpose(key_head, (1, 0, 2))

    tails = shifted(
        jnp.concatenate([key_head, value_head], axis=2)[span_rows - WINDOW :], "ctx", 1
    )

    key_feat = unique_features(key_hm, False)
    feat = key_feat.shape[-1]
    block_states = jnp.einsum(
        "hnrf,nrhv->hnfv",
        key_feat.reshape(heads_here, block_count, block_rows, feat),
        value_head.reshape(block_count, block_rows, heads_here, VD),
        preferred_element_type=jnp.float32,
    )
    span_state = jnp.sum(block_states, axis=1)
    tails, span_state = lax.optimization_barrier((tails, span_state))
    everything = lax.all_gather(span_state, "ctx")
    peers = everything.shape[0]
    here = lax.axis_index("ctx")
    entering = jnp.sum(
        jnp.where(
            (jnp.arange(peers) < here)[:, None, None, None], everything, jnp.zeros_like(everything)
        ),
        axis=0,
    )
    before = jnp.concatenate(
        [jnp.zeros_like(block_states[:, :1]), jnp.cumsum(block_states[:, :-1], axis=1)], axis=1
    )
    states = (before + entering[:, None]).astype(jnp.bfloat16)

    query_feat = unique_features(query_hm, True)
    inter = jnp.einsum(
        "hnrf,hnfv->hnrv",
        query_feat.reshape(heads_here, block_count, block_rows, feat),
        states,
        preferred_element_type=jnp.float32,
    ).reshape(heads_here, span_rows, VD)

    lead = jnp.zeros((LEAD - WINDOW, heads_here, KD + VD), jnp.bfloat16)
    key_ext = jnp.concatenate([lead[:, :, :KD], tails[:, :, :KD], key_head], axis=0)
    value_ext = jnp.concatenate([lead[:, :, KD:], tails[:, :, KD:], value_head], axis=0)
    flag = first_span.astype(jnp.int32).reshape(1)
    intra, window = local_attention(
        flag,
        query_hm,
        jnp.transpose(key_ext, (1, 2, 0)),
        value_ext.reshape(span_rows + LEAD, heads_here * VD),
        block_rows,
    )
    mixed = mix(intra, inter, window, gain)
    tokens_back = lax.all_to_all(mixed, "head", split_axis=0, concat_axis=1, tiled=True)
    return tokens_back


def solution(mesh):
    placed = (
        P(("groups", "ctx", "head"), None),
        P(("groups", "ctx", "head"), None),
        P(("groups", "ctx", "head"), None),
        P("head"),
    )
    return jax.shard_map(
        per_device,
        mesh=mesh,
        in_specs=placed,
        out_specs=P(("groups", "ctx", "head"), None),
        check_vma=False,
    )
```

```python
import math

import jax
import numpy as np
import jax.numpy as jnp
from jax import lax
from jax.experimental import pallas as pl
from jax.experimental.pallas import tpu as pltpu
from jax.sharding import PartitionSpec as P

HEADS = 32
KD = 16
VD = 128
WINDOW = 64


outer_scale = 1.0 / (4.0 * math.sqrt(2.0))
epsilon = 1e-06


def shifted(shard, axis, by):
    peers = lax.axis_size(axis)
    pairs = [(i, i + by) for i in range(peers) if 0 <= i + by < peers]
    return lax.ppermute(shard, axis, pairs)


def unique_features(vector, doubled):
    rows, cols = np.triu_indices(KD)
    pick_rows = jnp.asarray(np.eye(KD)[:, rows], jnp.bfloat16)
    pick_cols = jnp.asarray(np.eye(KD)[:, cols], jnp.bfloat16)
    first = jnp.einsum("...d,df->...f", vector, pick_rows, preferred_element_type=jnp.float32)
    second = jnp.einsum("...d,df->...f", vector, pick_cols, preferred_element_type=jnp.float32)
    prod = ((first * second) * outer_scale).astype(jnp.bfloat16)
    if doubled:
        prod = prod * jnp.asarray(np.where(rows == cols, 1.0, 2.0), jnp.bfloat16)
    lead = vector.shape[:-1]
    unit = jnp.ones(lead + (1,), jnp.bfloat16)
    half = (vector.astype(jnp.float32) * 0.5).astype(jnp.bfloat16)
    return jnp.concatenate([unit, half, prod], axis=-1)


CHUNK = 128
LEAD = 128


def local_attention_kernel(flag_ref, q_ref, kt_ref, vx_ref, intra_ref, win_ref, *, span_rows, block_rows):
    first_span = flag_ref[0] == 1
    for i in range(span_rows // CHUNK):
        r0 = i * CHUNK
        q_c = q_ref[0, r0 : r0 + CHUNK, :]
        bs = (r0 // block_rows) * block_rows
        width = r0 + CHUNK - bs
        k_i = kt_ref[0, :, LEAD + bs : LEAD + r0 + CHUNK]
        v_i = vx_ref[0, LEAD + bs : LEAD + r0 + CHUNK, :]
        scores = jnp.dot(q_c, k_i, preferred_element_type=jnp.float32) * 0.25
        row = lax.broadcasted_iota(jnp.int32, (CHUNK, width), 0)
        col = lax.broadcasted_iota(jnp.int32, (CHUNK, width), 1)
        kernel = jnp.where(
            col <= row + (r0 - bs), 1.0 + scores + 0.5 * scores * scores, 0.0
        ).astype(jnp.bfloat16)
        intra_ref[r0 : r0 + CHUNK, :] = jnp.dot(kernel, v_i, preferred_element_type=jnp.float32)

        k_w = kt_ref[0, :, r0 : r0 + CHUNK + LEAD]
        v_w = vx_ref[0, r0 : r0 + CHUNK + LEAD, :]
        ws = jnp.dot(q_c, k_w, preferred_element_type=jnp.float32) * 0.25
        wrow = lax.broadcasted_iota(jnp.int32, (CHUNK, CHUNK + LEAD), 0)
        wcol = lax.broadcasted_iota(jnp.int32, (CHUNK, CHUNK + LEAD), 1)
        valid = (wcol > wrow + LEAD - WINDOW) & (wcol <= wrow + LEAD)
        if i == 0:
            valid = valid & ((wcol >= LEAD) | jnp.logical_not(first_span))
        masked = jnp.where(valid, ws, -jnp.inf)
        highest = jnp.max(masked, axis=1, keepdims=True)
        expo = jnp.where(valid, jnp.exp(ws - highest), 0.0)
        weights = (expo / jnp.sum(expo, axis=1, keepdims=True)).astype(jnp.bfloat16)
        win_ref[r0 : r0 + CHUNK, :] = jnp.dot(weights, v_w, preferred_element_type=jnp.float32)


def local_attention(flag, q_hm, kt_hm, vx, block_rows):
    heads_here, span_rows, _ = q_hm.shape
    ext = kt_hm.shape[2]
    body = lambda *refs: local_attention_kernel(*refs, span_rows=span_rows, block_rows=block_rows)
    out = jax.ShapeDtypeStruct((span_rows, heads_here * VD), jnp.float32)
    return pl.pallas_call(
        body,
        grid_spec=pltpu.PrefetchScalarGridSpec(
            num_scalar_prefetch=1,
            grid=(heads_here,),
            in_specs=[
                pl.BlockSpec((1, span_rows, KD), lambda h, f: (h, 0, 0)),
                pl.BlockSpec((1, KD, ext), lambda h, f: (h, 0, 0)),
                pl.BlockSpec((1, ext, VD), lambda h, f: (h, 0, 0)),
            ],
            out_specs=[
                pl.BlockSpec((span_rows, VD), lambda h, f: (0, h)),
                pl.BlockSpec((span_rows, VD), lambda h, f: (0, h)),
            ],
        ),
        out_shape=(out, out),
    )(flag, q_hm, kt_hm, vx)


def mix_kernel(intra_ref, inter_ref, win_ref, gain_ref, out_ref):
    linear = intra_ref[...] + inter_ref[0]
    scale = lax.rsqrt(jnp.mean(linear * linear, axis=1, keepdims=True) + epsilon)
    out_ref[...] = (linear * scale * gain_ref[...] + win_ref[...]).astype(jnp.bfloat16)


def mix(intra, inter_hm, window, gain):
    heads_here, span_rows, _ = inter_hm.shape
    tile = pl.BlockSpec((span_rows, VD), lambda h: (0, h))
    return pl.pallas_call(
        mix_kernel,
        grid=(heads_here,),
        in_specs=[
            tile,
            pl.BlockSpec((1, span_rows, VD), lambda h: (h, 0, 0)),
            tile,
            pl.BlockSpec((1, VD), lambda h: (0, h)),
        ],
        out_specs=tile,
        out_shape=jax.ShapeDtypeStruct((span_rows, heads_here * VD), jnp.bfloat16),
    )(intra, inter_hm, window, gain.reshape(1, heads_here * VD))


def per_device(queries, keys, values, gain):
    local_tokens = queries.shape[0]

    def to_heads(tok, width):
        tok = jnp.transpose(tok.reshape(local_tokens, HEADS, width), (1, 0, 2))
        return lax.all_to_all(tok, "head", split_axis=0, concat_axis=1, tiled=True)

    query_hm = to_heads(queries, KD)
    key_hm = to_heads(keys, KD)
    value_hm = to_heads(values, VD)
    heads_here, span_rows, _ = query_hm.shape
    block_rows = min(512, span_rows)
    block_count = span_rows // block_rows
    first_span = lax.axis_index("ctx") == 0

    tails = shifted(
        jnp.concatenate([key_hm, value_hm], axis=2)[:, span_rows - WINDOW :], "ctx", 1
    )

    key_feat = unique_features(key_hm, False)
    feat = key_feat.shape[-1]
    block_states = jnp.einsum(
        "hnrf,hnrv->hnfv",
        key_feat.reshape(heads_here, block_count, block_rows, feat),
        value_hm.reshape(heads_here, block_count, block_rows, VD),
        preferred_element_type=jnp.float32,
    )
    span_state = jnp.sum(block_states, axis=1)
    everything = lax.all_gather(span_state, "ctx")
    peers = everything.shape[0]
    here = lax.axis_index("ctx")
    entering = jnp.sum(
        jnp.where(
            (jnp.arange(peers) < here)[:, None, None, None], everything, jnp.zeros_like(everything)
        ),
        axis=0,
    )
    before = jnp.concatenate(
        [jnp.zeros_like(block_states[:, :1]), jnp.cumsum(block_states[:, :-1], axis=1)], axis=1
    )
    states = (before + entering[:, None]).astype(jnp.bfloat16)

    query_feat = unique_features(query_hm, True)
    inter = jnp.einsum(
        "hnrf,hnfv->hnrv",
        query_feat.reshape(heads_here, block_count, block_rows, feat),
        states,
        preferred_element_type=jnp.float32,
    ).reshape(heads_here, span_rows, VD)

    lead = jnp.zeros((heads_here, LEAD - WINDOW, KD + VD), jnp.bfloat16)
    key_ext = jnp.concatenate([lead[:, :, :KD], tails[:, :, :KD], key_hm], axis=1)
    value_ext = jnp.concatenate([lead[:, :, KD:], tails[:, :, KD:], value_hm], axis=1)
    flag = first_span.astype(jnp.int32).reshape(1)
    intra, window = local_attention(
        flag, query_hm, jnp.transpose(key_ext, (0, 2, 1)), value_ext, block_rows
    )
    mixed = mix(intra, inter, window, gain)
    tokens_back = lax.all_to_all(mixed, "head", split_axis=0, concat_axis=1, tiled=True)
    return tokens_back


def solution(mesh):
    placed = (
        P(("groups", "ctx", "head"), None),
        P(("groups", "ctx", "head"), None),
        P(("groups", "ctx", "head"), None),
        P("head"),
    )
    return jax.shard_map(
        per_device,
        mesh=mesh,
        in_specs=placed,
        out_specs=P(("groups", "ctx", "head"), None),
        check_vma=False,
    )
```

```python
import math

import jax
import numpy as np
import jax.numpy as jnp
from jax import lax
from jax.experimental import pallas as pl
from jax.experimental.pallas import tpu as pltpu
from jax.sharding import PartitionSpec as P

HEADS = 32
KD = 16
VD = 128
WINDOW = 64


outer_scale = 1.0 / (4.0 * math.sqrt(2.0))
epsilon = 1e-06


def shifted(shard, axis, by):
    peers = lax.axis_size(axis)
    pairs = [(i, i + by) for i in range(peers) if 0 <= i + by < peers]
    return lax.ppermute(shard, axis, pairs)


def unique_features(vector, doubled):
    rows, cols = np.triu_indices(KD)
    pick_rows = jnp.asarray(np.eye(KD)[:, rows], jnp.bfloat16)
    pick_cols = jnp.asarray(np.eye(KD)[:, cols], jnp.bfloat16)
    first = jnp.einsum("...d,df->...f", vector, pick_rows, preferred_element_type=jnp.float32)
    second = jnp.einsum("...d,df->...f", vector, pick_cols, preferred_element_type=jnp.float32)
    prod = ((first * second) * outer_scale).astype(jnp.bfloat16)
    if doubled:
        prod = prod * jnp.asarray(np.where(rows == cols, 1.0, 2.0), jnp.bfloat16)
    lead = vector.shape[:-1]
    unit = jnp.ones(lead + (1,), jnp.bfloat16)
    half = (vector.astype(jnp.float32) * 0.5).astype(jnp.bfloat16)
    return jnp.concatenate([unit, half, prod], axis=-1)


CHUNK = 128
LEAD = 128


def local_attention_kernel(flag_ref, q_ref, kt_ref, vx_ref, intra_ref, win_ref, *, span_rows, block_rows):
    first_span = flag_ref[0] == 1
    for i in range(span_rows // CHUNK):
        r0 = i * CHUNK
        q_c = q_ref[0, r0 : r0 + CHUNK, :]
        bs = (r0 // block_rows) * block_rows
        width = r0 + CHUNK - bs
        k_i = kt_ref[0, :, LEAD + bs : LEAD + r0 + CHUNK]
        v_i = vx_ref[0, LEAD + bs : LEAD + r0 + CHUNK, :]
        scores = jnp.dot(q_c, k_i, preferred_element_type=jnp.float32) * 0.25
        row = lax.broadcasted_iota(jnp.int32, (CHUNK, width), 0)
        col = lax.broadcasted_iota(jnp.int32, (CHUNK, width), 1)
        kernel = jnp.where(
            col <= row + (r0 - bs), 1.0 + scores + 0.5 * scores * scores, 0.0
        ).astype(jnp.bfloat16)
        intra_ref[r0 : r0 + CHUNK, :] = jnp.dot(kernel, v_i, preferred_element_type=jnp.float32)

        k_w = kt_ref[0, :, r0 : r0 + CHUNK + LEAD]
        v_w = vx_ref[0, r0 : r0 + CHUNK + LEAD, :]
        ws = jnp.dot(q_c, k_w, preferred_element_type=jnp.float32) * 0.25
        wrow = lax.broadcasted_iota(jnp.int32, (CHUNK, CHUNK + LEAD), 0)
        wcol = lax.broadcasted_iota(jnp.int32, (CHUNK, CHUNK + LEAD), 1)
        valid = (wcol > wrow + LEAD - WINDOW) & (wcol <= wrow + LEAD)
        if i == 0:
            valid = valid & ((wcol >= LEAD) | jnp.logical_not(first_span))
        masked = jnp.where(valid, ws, -jnp.inf)
        highest = jnp.max(masked, axis=1, keepdims=True)
        expo = jnp.where(valid, jnp.exp(ws - highest), 0.0)
        weights = (expo / jnp.sum(expo, axis=1, keepdims=True)).astype(jnp.bfloat16)
        win_ref[r0 : r0 + CHUNK, :] = jnp.dot(weights, v_w, preferred_element_type=jnp.float32)


def local_attention(flag, q_hm, kt_hm, vx, block_rows):
    heads_here, span_rows, _ = q_hm.shape
    ext = kt_hm.shape[2]
    body = lambda *refs: local_attention_kernel(*refs, span_rows=span_rows, block_rows=block_rows)
    out = jax.ShapeDtypeStruct((span_rows, heads_here * VD), jnp.float32)
    return pl.pallas_call(
        body,
        grid_spec=pltpu.PrefetchScalarGridSpec(
            num_scalar_prefetch=1,
            grid=(heads_here,),
            in_specs=[
                pl.BlockSpec((1, span_rows, KD), lambda h, f: (h, 0, 0)),
                pl.BlockSpec((1, KD, ext), lambda h, f: (h, 0, 0)),
                pl.BlockSpec((1, ext, VD), lambda h, f: (h, 0, 0)),
            ],
            out_specs=[
                pl.BlockSpec((span_rows, VD), lambda h, f: (0, h)),
                pl.BlockSpec((span_rows, VD), lambda h, f: (0, h)),
            ],
        ),
        out_shape=(out, out),
    )(flag, q_hm, kt_hm, vx)


def mix_kernel(intra_ref, inter_ref, win_ref, gain_ref, out_ref):
    linear = intra_ref[...] + inter_ref[0]
    scale = lax.rsqrt(jnp.mean(linear * linear, axis=1, keepdims=True) + epsilon)
    out_ref[...] = (linear * scale * gain_ref[...] + win_ref[...]).astype(jnp.bfloat16)


def mix(intra, inter_hm, window, gain):
    heads_here, span_rows, _ = inter_hm.shape
    tile = pl.BlockSpec((span_rows, VD), lambda h: (0, h))
    return pl.pallas_call(
        mix_kernel,
        grid=(heads_here,),
        in_specs=[
            tile,
            pl.BlockSpec((1, span_rows, VD), lambda h: (h, 0, 0)),
            tile,
            pl.BlockSpec((1, VD), lambda h: (0, h)),
        ],
        out_specs=tile,
        out_shape=jax.ShapeDtypeStruct((span_rows, heads_here * VD), jnp.bfloat16),
    )(intra, inter_hm, window, gain.reshape(1, heads_here * VD))


def per_device(queries, keys, values, gain):
    local_tokens = queries.shape[0]

    def to_heads(tok, width):
        tok = jnp.transpose(tok.reshape(local_tokens, HEADS, width), (1, 0, 2))
        return lax.all_to_all(tok, "head", split_axis=0, concat_axis=1, tiled=True)

    value_hm = to_heads(values, VD)
    key_hm = to_heads(keys, KD)
    heads_here, span_rows, _ = key_hm.shape
    block_rows = min(512, span_rows)
    block_count = span_rows // block_rows
    first_span = lax.axis_index("ctx") == 0

    tails = shifted(
        jnp.concatenate([key_hm, value_hm], axis=2)[:, span_rows - WINDOW :], "ctx", 1
    )

    key_feat = unique_features(key_hm, False)
    feat = key_feat.shape[-1]
    block_states = jnp.einsum(
        "hnrf,hnrv->hnfv",
        key_feat.reshape(heads_here, block_count, block_rows, feat),
        value_hm.reshape(heads_here, block_count, block_rows, VD),
        preferred_element_type=jnp.float32,
    )
    span_state = jnp.sum(block_states, axis=1)
    everything = lax.all_gather(span_state, "ctx")
    queries, span_state = lax.optimization_barrier((queries, span_state))
    query_hm = to_heads(queries, KD)
    peers = everything.shape[0]
    here = lax.axis_index("ctx")
    entering = jnp.sum(
        jnp.where(
            (jnp.arange(peers) < here)[:, None, None, None], everything, jnp.zeros_like(everything)
        ),
        axis=0,
    )
    before = jnp.concatenate(
        [jnp.zeros_like(block_states[:, :1]), jnp.cumsum(block_states[:, :-1], axis=1)], axis=1
    )
    states = (before + entering[:, None]).astype(jnp.bfloat16)

    query_feat = unique_features(query_hm, True)
    inter = jnp.einsum(
        "hnrf,hnfv->hnrv",
        query_feat.reshape(heads_here, block_count, block_rows, feat),
        states,
        preferred_element_type=jnp.float32,
    ).reshape(heads_here, span_rows, VD)

    lead = jnp.zeros((heads_here, LEAD - WINDOW, KD + VD), jnp.bfloat16)
    key_ext = jnp.concatenate([lead[:, :, :KD], tails[:, :, :KD], key_hm], axis=1)
    value_ext = jnp.concatenate([lead[:, :, KD:], tails[:, :, KD:], value_hm], axis=1)
    flag = first_span.astype(jnp.int32).reshape(1)
    intra, window = local_attention(
        flag, query_hm, jnp.transpose(key_ext, (0, 2, 1)), value_ext, block_rows
    )
    mixed = mix(intra, inter, window, gain)
    tokens_back = lax.all_to_all(mixed, "head", split_axis=0, concat_axis=1, tiled=True)
    return tokens_back


def solution(mesh):
    placed = (
        P(("groups", "ctx", "head"), None),
        P(("groups", "ctx", "head"), None),
        P(("groups", "ctx", "head"), None),
        P("head"),
    )
    return jax.shard_map(
        per_device,
        mesh=mesh,
        in_specs=placed,
        out_specs=P(("groups", "ctx", "head"), None),
        check_vma=False,
    )
```

```python
import math

import jax
import numpy as np
import jax.numpy as jnp
from jax import lax
from jax.experimental import pallas as pl
from jax.experimental.pallas import tpu as pltpu
from jax.sharding import PartitionSpec as P

HEADS = 32
KD = 16
VD = 128
WINDOW = 64


outer_scale = 1.0 / (4.0 * math.sqrt(2.0))
epsilon = 1e-06


def shifted(shard, axis, by):
    peers = lax.axis_size(axis)
    pairs = [(i, i + by) for i in range(peers) if 0 <= i + by < peers]
    return lax.ppermute(shard, axis, pairs)


def unique_features(vector, doubled):
    rows, cols = np.triu_indices(KD)
    pick_rows = jnp.asarray(np.eye(KD)[:, rows], jnp.bfloat16)
    pick_cols = jnp.asarray(np.eye(KD)[:, cols], jnp.bfloat16)
    first = jnp.einsum("...d,df->...f", vector, pick_rows, preferred_element_type=jnp.float32)
    second = jnp.einsum("...d,df->...f", vector, pick_cols, preferred_element_type=jnp.float32)
    prod = ((first * second) * outer_scale).astype(jnp.bfloat16)
    if doubled:
        prod = prod * jnp.asarray(np.where(rows == cols, 1.0, 2.0), jnp.bfloat16)
    lead = vector.shape[:-1]
    unit = jnp.ones(lead + (1,), jnp.bfloat16)
    half = (vector.astype(jnp.float32) * 0.5).astype(jnp.bfloat16)
    return jnp.concatenate([unit, half, prod], axis=-1)


CHUNK = 128
LEAD = 128


def local_attention_kernel(flag_ref, q_ref, kt_ref, vx_ref, intra_ref, win_ref, *, span_rows, block_rows):
    first_span = flag_ref[0] == 1
    for i in range(span_rows // CHUNK):
        r0 = i * CHUNK
        q_c = q_ref[0, r0 : r0 + CHUNK, :]
        bs = (r0 // block_rows) * block_rows
        width = r0 + CHUNK - bs
        k_i = kt_ref[0, :, LEAD + bs : LEAD + r0 + CHUNK]
        v_i = vx_ref[0, LEAD + bs : LEAD + r0 + CHUNK, :]
        scores = jnp.dot(q_c, k_i, preferred_element_type=jnp.float32) * 0.25
        row = lax.broadcasted_iota(jnp.int32, (CHUNK, width), 0)
        col = lax.broadcasted_iota(jnp.int32, (CHUNK, width), 1)
        kernel = jnp.where(
            col <= row + (r0 - bs), 1.0 + scores + 0.5 * scores * scores, 0.0
        ).astype(jnp.bfloat16)
        intra_ref[r0 : r0 + CHUNK, :] = jnp.dot(kernel, v_i, preferred_element_type=jnp.float32)

        k_w = kt_ref[0, :, r0 : r0 + CHUNK + LEAD]
        v_w = vx_ref[0, r0 : r0 + CHUNK + LEAD, :]
        ws = jnp.dot(q_c, k_w, preferred_element_type=jnp.float32) * 0.25
        wrow = lax.broadcasted_iota(jnp.int32, (CHUNK, CHUNK + LEAD), 0)
        wcol = lax.broadcasted_iota(jnp.int32, (CHUNK, CHUNK + LEAD), 1)
        valid = (wcol > wrow + LEAD - WINDOW) & (wcol <= wrow + LEAD)
        if i == 0:
            valid = valid & ((wcol >= LEAD) | jnp.logical_not(first_span))
        masked = jnp.where(valid, ws, -jnp.inf)
        highest = jnp.max(masked, axis=1, keepdims=True)
        expo = jnp.where(valid, jnp.exp(ws - highest), 0.0)
        weights = (expo / jnp.sum(expo, axis=1, keepdims=True)).astype(jnp.bfloat16)
        win_ref[r0 : r0 + CHUNK, :] = jnp.dot(weights, v_w, preferred_element_type=jnp.float32)


def local_attention(flag, q_hm, kt_hm, vx, block_rows):
    heads_here, span_rows, _ = q_hm.shape
    ext = kt_hm.shape[2]
    body = lambda *refs: local_attention_kernel(*refs, span_rows=span_rows, block_rows=block_rows)
    out = jax.ShapeDtypeStruct((span_rows, heads_here * VD), jnp.float32)
    return pl.pallas_call(
        body,
        grid_spec=pltpu.PrefetchScalarGridSpec(
            num_scalar_prefetch=1,
            grid=(heads_here,),
            in_specs=[
                pl.BlockSpec((1, span_rows, KD), lambda h, f: (h, 0, 0)),
                pl.BlockSpec((1, KD, ext), lambda h, f: (h, 0, 0)),
                pl.BlockSpec((1, ext, VD), lambda h, f: (h, 0, 0)),
            ],
            out_specs=[
                pl.BlockSpec((span_rows, VD), lambda h, f: (0, h)),
                pl.BlockSpec((span_rows, VD), lambda h, f: (0, h)),
            ],
        ),
        out_shape=(out, out),
    )(flag, q_hm, kt_hm, vx)


def mix_kernel(intra_ref, qf_ref, st_ref, win_ref, gain_ref, out_ref, *, block_rows):
    for n in range(qf_ref.shape[1]):
        rows = slice(n * block_rows, (n + 1) * block_rows)
        inter = jnp.dot(qf_ref[0, n], st_ref[0, n], preferred_element_type=jnp.float32)
        linear = intra_ref[rows, :] + inter
        scale = lax.rsqrt(jnp.mean(linear * linear, axis=1, keepdims=True) + epsilon)
        out_ref[rows, :] = (linear * scale * gain_ref[...] + win_ref[rows, :]).astype(jnp.bfloat16)


def mix(intra, query_feat, states, window, gain):
    heads_here, block_count, block_rows, feat = query_feat.shape
    span_rows = block_count * block_rows
    tile = pl.BlockSpec((span_rows, VD), lambda h: (0, h))
    return pl.pallas_call(
        lambda *refs: mix_kernel(*refs, block_rows=block_rows),
        grid=(heads_here,),
        in_specs=[
            tile,
            pl.BlockSpec((1, block_count, block_rows, feat), lambda h: (h, 0, 0, 0)),
            pl.BlockSpec((1, block_count, feat, VD), lambda h: (h, 0, 0, 0)),
            tile,
            pl.BlockSpec((1, VD), lambda h: (0, h)),
        ],
        out_specs=tile,
        out_shape=jax.ShapeDtypeStruct((span_rows, heads_here * VD), jnp.bfloat16),
    )(intra, query_feat, states, window, gain.reshape(1, heads_here * VD))


def per_device(queries, keys, values, gain):
    local_tokens = queries.shape[0]

    def to_heads(tok, width):
        tok = jnp.transpose(tok.reshape(local_tokens, HEADS, width), (1, 0, 2))
        return lax.all_to_all(tok, "head", split_axis=0, concat_axis=1, tiled=True)

    value_hm = to_heads(values, VD)
    key_hm = to_heads(keys, KD)
    heads_here, span_rows, _ = key_hm.shape
    block_rows = min(512, span_rows)
    block_count = span_rows // block_rows
    first_span = lax.axis_index("ctx") == 0

    tails = shifted(
        jnp.concatenate([key_hm, value_hm], axis=2)[:, span_rows - WINDOW :], "ctx", 1
    )

    key_feat = unique_features(key_hm.reshape(heads_here, block_count, block_rows, KD), False)
    block_states = jnp.einsum(
        "hnrf,hnrv->hnfv",
        key_feat,
        value_hm.reshape(heads_here, block_count, block_rows, VD),
        preferred_element_type=jnp.float32,
    )
    span_state = jnp.sum(block_states, axis=1)
    everything = lax.all_gather(span_state, "ctx")
    queries, span_state = lax.optimization_barrier((queries, span_state))
    query_hm = to_heads(queries, KD)
    peers = everything.shape[0]
    here = lax.axis_index("ctx")
    entering = jnp.sum(
        jnp.where(
            (jnp.arange(peers) < here)[:, None, None, None], everything, jnp.zeros_like(everything)
        ),
        axis=0,
    )
    before = jnp.concatenate(
        [jnp.zeros_like(block_states[:, :1]), jnp.cumsum(block_states[:, :-1], axis=1)], axis=1
    )
    states = (before + entering[:, None]).astype(jnp.bfloat16)

    query_feat = unique_features(query_hm.reshape(heads_here, block_count, block_rows, KD), True)

    lead = jnp.zeros((heads_here, LEAD - WINDOW, KD + VD), jnp.bfloat16)
    key_ext = jnp.concatenate([lead[:, :, :KD], tails[:, :, :KD], key_hm], axis=1)
    value_ext = jnp.concatenate([lead[:, :, KD:], tails[:, :, KD:], value_hm], axis=1)
    flag = first_span.astype(jnp.int32).reshape(1)
    intra, window = local_attention(
        flag, query_hm, jnp.transpose(key_ext, (0, 2, 1)), value_ext, block_rows
    )
    mixed = mix(intra, query_feat, states, window, gain)
    tokens_back = lax.all_to_all(mixed, "head", split_axis=0, concat_axis=1, tiled=True)
    return tokens_back


def solution(mesh):
    placed = (
        P(("groups", "ctx", "head"), None),
        P(("groups", "ctx", "head"), None),
        P(("groups", "ctx", "head"), None),
        P("head"),
    )
    return jax.shard_map(
        per_device,
        mesh=mesh,
        in_specs=placed,
        out_specs=P(("groups", "ctx", "head"), None),
        check_vma=False,
    )
```

```python
import math

import jax
import numpy as np
import jax.numpy as jnp
from jax import lax
from jax.experimental import pallas as pl
from jax.experimental.pallas import tpu as pltpu
from jax.sharding import PartitionSpec as P

HEADS = 32
KD = 16
VD = 128
WINDOW = 64


outer_scale = 1.0 / (4.0 * math.sqrt(2.0))
epsilon = 1e-06


def shifted(shard, axis, by):
    peers = lax.axis_size(axis)
    pairs = [(i, i + by) for i in range(peers) if 0 <= i + by < peers]
    return lax.ppermute(shard, axis, pairs)


def unique_features(vector, doubled):
    rows, cols = np.triu_indices(KD)
    pick_rows = jnp.asarray(np.eye(KD)[:, rows], jnp.bfloat16)
    pick_cols = jnp.asarray(np.eye(KD)[:, cols], jnp.bfloat16)
    first = jnp.einsum("...d,df->...f", vector, pick_rows, preferred_element_type=jnp.float32)
    second = jnp.einsum("...d,df->...f", vector, pick_cols, preferred_element_type=jnp.float32)
    prod = ((first * second) * outer_scale).astype(jnp.bfloat16)
    if doubled:
        prod = prod * jnp.asarray(np.where(rows == cols, 1.0, 2.0), jnp.bfloat16)
    lead = vector.shape[:-1]
    unit = jnp.ones(lead + (1,), jnp.bfloat16)
    half = (vector.astype(jnp.float32) * 0.5).astype(jnp.bfloat16)
    return jnp.concatenate([unit, half, prod], axis=-1)


CHUNK = 128
LEAD = 128


def local_attention_kernel(flag_ref, q_ref, kt_ref, vx_ref, intra_ref, win_ref, *, span_rows, block_rows):
    first_span = flag_ref[0] == 1
    for i in range(span_rows // CHUNK):
        r0 = i * CHUNK
        q_c = q_ref[0, r0 : r0 + CHUNK, :]
        bs = (r0 // block_rows) * block_rows
        width = r0 + CHUNK - bs
        k_i = kt_ref[0, :, LEAD + bs : LEAD + r0 + CHUNK]
        v_i = vx_ref[0, LEAD + bs : LEAD + r0 + CHUNK, :]
        scores = jnp.dot(q_c, k_i, preferred_element_type=jnp.float32) * 0.25
        row = lax.broadcasted_iota(jnp.int32, (CHUNK, width), 0)
        col = lax.broadcasted_iota(jnp.int32, (CHUNK, width), 1)
        kernel = jnp.where(
            col <= row + (r0 - bs), 1.0 + scores + 0.5 * scores * scores, 0.0
        ).astype(jnp.bfloat16)
        intra_ref[r0 : r0 + CHUNK, :] = jnp.dot(kernel, v_i, preferred_element_type=jnp.float32)

        k_w = kt_ref[0, :, r0 : r0 + CHUNK + LEAD]
        v_w = vx_ref[0, r0 : r0 + CHUNK + LEAD, :]
        ws = jnp.dot(q_c, k_w, preferred_element_type=jnp.float32) * 0.25
        wrow = lax.broadcasted_iota(jnp.int32, (CHUNK, CHUNK + LEAD), 0)
        wcol = lax.broadcasted_iota(jnp.int32, (CHUNK, CHUNK + LEAD), 1)
        valid = (wcol > wrow + LEAD - WINDOW) & (wcol <= wrow + LEAD)
        if i == 0:
            valid = valid & ((wcol >= LEAD) | jnp.logical_not(first_span))
        masked = jnp.where(valid, ws, -jnp.inf)
        highest = jnp.max(masked, axis=1, keepdims=True)
        expo = jnp.where(valid, jnp.exp(ws - highest), 0.0)
        weights = (expo / jnp.sum(expo, axis=1, keepdims=True)).astype(jnp.bfloat16)
        win_ref[r0 : r0 + CHUNK, :] = jnp.dot(weights, v_w, preferred_element_type=jnp.float32)


def local_attention(flag, q_hm, kt_hm, vx, block_rows):
    heads_here, span_rows, _ = q_hm.shape
    ext = kt_hm.shape[2]
    body = lambda *refs: local_attention_kernel(*refs, span_rows=span_rows, block_rows=block_rows)
    out = jax.ShapeDtypeStruct((span_rows, heads_here * VD), jnp.float32)
    return pl.pallas_call(
        body,
        grid_spec=pltpu.PrefetchScalarGridSpec(
            num_scalar_prefetch=1,
            grid=(heads_here,),
            in_specs=[
                pl.BlockSpec((1, span_rows, KD), lambda h, f: (h, 0, 0)),
                pl.BlockSpec((1, KD, ext), lambda h, f: (h, 0, 0)),
                pl.BlockSpec((1, ext, VD), lambda h, f: (h, 0, 0)),
            ],
            out_specs=[
                pl.BlockSpec((span_rows, VD), lambda h, f: (0, h)),
                pl.BlockSpec((span_rows, VD), lambda h, f: (0, h)),
            ],
        ),
        out_shape=(out, out),
    )(flag, q_hm, kt_hm, vx)


def mix_kernel(intra_ref, inter_ref, win_ref, gain_ref, out_ref):
    linear = intra_ref[...] + inter_ref[0]
    scale = lax.rsqrt(jnp.mean(linear * linear, axis=1, keepdims=True) + epsilon)
    out_ref[...] = (linear * scale * gain_ref[...] + win_ref[...]).astype(jnp.bfloat16)


def mix(intra, inter_hm, window, gain):
    heads_here, span_rows, _ = inter_hm.shape
    tile = pl.BlockSpec((span_rows, VD), lambda h: (0, h))
    return pl.pallas_call(
        mix_kernel,
        grid=(heads_here,),
        in_specs=[
            tile,
            pl.BlockSpec((1, span_rows, VD), lambda h: (h, 0, 0)),
            tile,
            pl.BlockSpec((1, VD), lambda h: (0, h)),
        ],
        out_specs=tile,
        out_shape=jax.ShapeDtypeStruct((span_rows, heads_here * VD), jnp.bfloat16),
    )(intra, inter_hm, window, gain.reshape(1, heads_here * VD))


def per_device(queries, keys, values, gain):
    local_tokens = queries.shape[0]

    def to_heads(tok, width):
        tok = jnp.transpose(tok.reshape(local_tokens, HEADS, width), (1, 0, 2))
        return lax.all_to_all(tok, "head", split_axis=0, concat_axis=1, tiled=True)

    value_hm = to_heads(values, VD)
    key_hm = to_heads(keys, KD)
    heads_here, span_rows, _ = key_hm.shape
    block_rows = min(512, span_rows)
    block_count = span_rows // block_rows
    first_span = lax.axis_index("ctx") == 0

    tails = shifted(
        jnp.concatenate([key_hm, value_hm], axis=2)[:, span_rows - WINDOW :], "ctx", 1
    )

    key_feat = unique_features(key_hm.reshape(heads_here, block_count, block_rows, KD), False)
    block_states = jnp.einsum(
        "hnrf,hnrv->hnfv",
        key_feat,
        value_hm.reshape(heads_here, block_count, block_rows, VD),
        preferred_element_type=jnp.float32,
    )
    span_state = jnp.sum(block_states, axis=1)
    everything = lax.all_gather(span_state, "ctx")
    queries, span_state = lax.optimization_barrier((queries, span_state))
    query_hm = to_heads(queries, KD)
    peers = everything.shape[0]
    here = lax.axis_index("ctx")
    entering = jnp.sum(
        jnp.where(
            (jnp.arange(peers) < here)[:, None, None, None], everything, jnp.zeros_like(everything)
        ),
        axis=0,
    )
    before = jnp.concatenate(
        [jnp.zeros_like(block_states[:, :1]), jnp.cumsum(block_states[:, :-1], axis=1)], axis=1
    )
    states = (before + entering[:, None]).astype(jnp.bfloat16)

    query_feat = unique_features(query_hm.reshape(heads_here, block_count, block_rows, KD), True)
    inter = jnp.einsum(
        "hnrf,hnfv->hnrv",
        query_feat,
        states,
        preferred_element_type=jnp.float32,
    ).reshape(heads_here, span_rows, VD)

    lead = jnp.zeros((heads_here, LEAD - WINDOW, KD + VD), jnp.bfloat16)
    key_ext = jnp.concatenate([lead[:, :, :KD], tails[:, :, :KD], key_hm], axis=1)
    value_ext = jnp.concatenate([lead[:, :, KD:], tails[:, :, KD:], value_hm], axis=1)
    flag = first_span.astype(jnp.int32).reshape(1)
    intra, window = local_attention(
        flag, query_hm, jnp.transpose(key_ext, (0, 2, 1)), value_ext, block_rows
    )
    mixed = mix(intra, inter, window, gain)
    tokens_back = lax.all_to_all(mixed, "head", split_axis=0, concat_axis=1, tiled=True)
    return tokens_back


def solution(mesh):
    placed = (
        P(("groups", "ctx", "head"), None),
        P(("groups", "ctx", "head"), None),
        P(("groups", "ctx", "head"), None),
        P("head"),
    )
    return jax.shard_map(
        per_device,
        mesh=mesh,
        in_specs=placed,
        out_specs=P(("groups", "ctx", "head"), None),
        check_vma=False,
    )
```

```python
import math

import jax
import numpy as np
import jax.numpy as jnp
from jax import lax
from jax.experimental import pallas as pl
from jax.experimental.pallas import tpu as pltpu
from jax.sharding import PartitionSpec as P

HEADS = 32
KD = 16
VD = 128
WINDOW = 64


outer_scale = 1.0 / (4.0 * math.sqrt(2.0))
epsilon = 1e-06


def shifted(shard, axis, by):
    peers = lax.axis_size(axis)
    pairs = [(i, i + by) for i in range(peers) if 0 <= i + by < peers]
    return lax.ppermute(shard, axis, pairs)


def unique_features(vector, doubled):
    rows, cols = np.triu_indices(KD)
    pick_rows = jnp.asarray(np.eye(KD)[:, rows], jnp.bfloat16)
    pick_cols = jnp.asarray(np.eye(KD)[:, cols], jnp.bfloat16)
    first = jnp.einsum("...d,df->...f", vector, pick_rows, preferred_element_type=jnp.float32)
    second = jnp.einsum("...d,df->...f", vector, pick_cols, preferred_element_type=jnp.float32)
    prod = ((first * second) * outer_scale).astype(jnp.bfloat16)
    if doubled:
        prod = prod * jnp.asarray(np.where(rows == cols, 1.0, 2.0), jnp.bfloat16)
    lead = vector.shape[:-1]
    unit = jnp.ones(lead + (1,), jnp.bfloat16)
    half = (vector.astype(jnp.float32) * 0.5).astype(jnp.bfloat16)
    return jnp.concatenate([prod, half, unit], axis=-1)


CHUNK = 128
LEAD = 128


def local_attention_kernel(flag_ref, q_ref, kt_ref, vx_ref, intra_ref, win_ref, *, span_rows, block_rows):
    first_span = flag_ref[0] == 1
    for i in range(span_rows // CHUNK):
        r0 = i * CHUNK
        q_c = q_ref[0, r0 : r0 + CHUNK, :]
        bs = (r0 // block_rows) * block_rows
        width = r0 + CHUNK - bs
        k_i = kt_ref[0, :, LEAD + bs : LEAD + r0 + CHUNK]
        v_i = vx_ref[0, LEAD + bs : LEAD + r0 + CHUNK, :]
        scores = jnp.dot(q_c, k_i, preferred_element_type=jnp.float32) * 0.25
        row = lax.broadcasted_iota(jnp.int32, (CHUNK, width), 0)
        col = lax.broadcasted_iota(jnp.int32, (CHUNK, width), 1)
        kernel = jnp.where(
            col <= row + (r0 - bs), 1.0 + scores + 0.5 * scores * scores, 0.0
        ).astype(jnp.bfloat16)
        intra_ref[r0 : r0 + CHUNK, :] = jnp.dot(kernel, v_i, preferred_element_type=jnp.float32)

        k_w = kt_ref[0, :, r0 : r0 + CHUNK + LEAD]
        v_w = vx_ref[0, r0 : r0 + CHUNK + LEAD, :]
        ws = jnp.dot(q_c, k_w, preferred_element_type=jnp.float32) * 0.25
        wrow = lax.broadcasted_iota(jnp.int32, (CHUNK, CHUNK + LEAD), 0)
        wcol = lax.broadcasted_iota(jnp.int32, (CHUNK, CHUNK + LEAD), 1)
        valid = (wcol > wrow + LEAD - WINDOW) & (wcol <= wrow + LEAD)
        if i == 0:
            valid = valid & ((wcol >= LEAD) | jnp.logical_not(first_span))
        masked = jnp.where(valid, ws, -jnp.inf)
        highest = jnp.max(masked, axis=1, keepdims=True)
        expo = jnp.where(valid, jnp.exp(ws - highest), 0.0)
        weights = (expo / jnp.sum(expo, axis=1, keepdims=True)).astype(jnp.bfloat16)
        win_ref[r0 : r0 + CHUNK, :] = jnp.dot(weights, v_w, preferred_element_type=jnp.float32)


def local_attention(flag, q_hm, kt_hm, vx, block_rows):
    heads_here, span_rows, _ = q_hm.shape
    ext = kt_hm.shape[2]
    body = lambda *refs: local_attention_kernel(*refs, span_rows=span_rows, block_rows=block_rows)
    out = jax.ShapeDtypeStruct((span_rows, heads_here * VD), jnp.float32)
    return pl.pallas_call(
        body,
        grid_spec=pltpu.PrefetchScalarGridSpec(
            num_scalar_prefetch=1,
            grid=(heads_here,),
            in_specs=[
                pl.BlockSpec((1, span_rows, KD), lambda h, f: (h, 0, 0)),
                pl.BlockSpec((1, KD, ext), lambda h, f: (h, 0, 0)),
                pl.BlockSpec((1, ext, VD), lambda h, f: (h, 0, 0)),
            ],
            out_specs=[
                pl.BlockSpec((span_rows, VD), lambda h, f: (0, h)),
                pl.BlockSpec((span_rows, VD), lambda h, f: (0, h)),
            ],
        ),
        out_shape=(out, out),
    )(flag, q_hm, kt_hm, vx)


def mix_kernel(
    here_ref, intra_ref, win_ref, q_ref, every_ref, before_ref, pr_ref, pc_ref, w2_ref, gain_ref,
    out_ref, *, block_rows
):
    here = here_ref[0]
    entering = jnp.zeros(every_ref.shape[2:], jnp.float32)
    for k in range(every_ref.shape[0]):
        entering = entering + jnp.where(k < here, every_ref[k, 0], 0.0)
    q = q_ref[0]
    first = jnp.dot(q, pr_ref[...], preferred_element_type=jnp.float32)
    second = jnp.dot(q, pc_ref[...], preferred_element_type=jnp.float32)
    prod = ((first * second) * outer_scale).astype(jnp.bfloat16) * w2_ref[...]
    half = (q.astype(jnp.float32) * 0.5).astype(jnp.bfloat16)
    pairs = prod.shape[1]
    for n in range(before_ref.shape[1]):
        rows = slice(n * block_rows, (n + 1) * block_rows)
        state = before_ref[0, n] + entering
        inter = (
            jnp.dot(prod[rows], state[:pairs].astype(jnp.bfloat16), preferred_element_type=jnp.float32)
            + jnp.dot(
                half[rows],
                state[pairs : pairs + KD].astype(jnp.bfloat16),
                preferred_element_type=jnp.float32,
            )
            + state[pairs + KD :].astype(jnp.bfloat16).astype(jnp.float32)
        )
        linear = intra_ref[rows, :] + inter
        scale = lax.rsqrt(jnp.mean(linear * linear, axis=1, keepdims=True) + epsilon)
        out_ref[rows, :] = (linear * scale * gain_ref[...] + win_ref[rows, :]).astype(jnp.bfloat16)


def mix(here, intra, window, query_hm, everything, before, gain):
    heads_here, span_rows, _ = query_hm.shape
    peers, _, feat, _ = everything.shape
    block_count = before.shape[1]
    rows, cols = np.triu_indices(KD)
    pick_rows = jnp.asarray(np.eye(KD)[:, rows], jnp.bfloat16)
    pick_cols = jnp.asarray(np.eye(KD)[:, cols], jnp.bfloat16)
    doubled = jnp.asarray(np.where(rows == cols, 1.0, 2.0)[None, :], jnp.bfloat16)
    pairs = rows.shape[0]
    tile = pl.BlockSpec((span_rows, VD), lambda h, c: (0, h))
    whole = lambda shape: pl.BlockSpec(shape, lambda h, c: (0, 0))
    return pl.pallas_call(
        lambda *refs: mix_kernel(*refs, block_rows=span_rows // block_count),
        grid_spec=pltpu.PrefetchScalarGridSpec(
            num_scalar_prefetch=1,
            grid=(heads_here,),
            in_specs=[
                tile,
                tile,
                pl.BlockSpec((1, span_rows, KD), lambda h, c: (h, 0, 0)),
                pl.BlockSpec((peers, 1, feat, VD), lambda h, c: (0, h, 0, 0)),
                pl.BlockSpec((1, block_count, feat, VD), lambda h, c: (h, 0, 0, 0)),
                whole((KD, pairs)),
                whole((KD, pairs)),
                whole((1, pairs)),
                pl.BlockSpec((1, VD), lambda h, c: (0, h)),
            ],
            out_specs=tile,
        ),
        out_shape=jax.ShapeDtypeStruct((span_rows, heads_here * VD), jnp.bfloat16),
    )(
        here, intra, window, query_hm, everything, before, pick_rows, pick_cols, doubled,
        gain.reshape(1, heads_here * VD),
    )


def per_device(queries, keys, values, gain):
    local_tokens = queries.shape[0]

    def to_heads(tok, width):
        tok = jnp.transpose(tok.reshape(local_tokens, HEADS, width), (1, 0, 2))
        return lax.all_to_all(tok, "head", split_axis=0, concat_axis=1, tiled=True)

    value_hm = to_heads(values, VD)
    key_hm = to_heads(keys, KD)
    heads_here, span_rows, _ = key_hm.shape
    block_rows = min(512, span_rows)
    block_count = span_rows // block_rows
    first_span = lax.axis_index("ctx") == 0

    tails = shifted(
        jnp.concatenate([key_hm, value_hm], axis=2)[:, span_rows - WINDOW :], "ctx", 1
    )

    key_feat = unique_features(key_hm.reshape(heads_here, block_count, block_rows, KD), False)
    block_states = jnp.einsum(
        "hnrf,hnrv->hnfv",
        key_feat,
        value_hm.reshape(heads_here, block_count, block_rows, VD),
        preferred_element_type=jnp.float32,
    )
    span_state = jnp.sum(block_states, axis=1)
    everything = lax.all_gather(span_state, "ctx")
    queries, span_state = lax.optimization_barrier((queries, span_state))
    query_hm = to_heads(queries, KD)
    before = jnp.concatenate(
        [jnp.zeros_like(block_states[:, :1]), jnp.cumsum(block_states[:, :-1], axis=1)], axis=1
    )

    lead = jnp.zeros((heads_here, LEAD - WINDOW, KD + VD), jnp.bfloat16)
    key_ext = jnp.concatenate([lead[:, :, :KD], tails[:, :, :KD], key_hm], axis=1)
    value_ext = jnp.concatenate([lead[:, :, KD:], tails[:, :, KD:], value_hm], axis=1)
    flag = first_span.astype(jnp.int32).reshape(1)
    intra, window = local_attention(
        flag, query_hm, jnp.transpose(key_ext, (0, 2, 1)), value_ext, block_rows
    )
    here = lax.axis_index("ctx").astype(jnp.int32).reshape(1)
    mixed = mix(here, intra, window, query_hm, everything, before, gain)
    tokens_back = lax.all_to_all(mixed, "head", split_axis=0, concat_axis=1, tiled=True)
    return tokens_back


def solution(mesh):
    placed = (
        P(("groups", "ctx", "head"), None),
        P(("groups", "ctx", "head"), None),
        P(("groups", "ctx", "head"), None),
        P("head"),
    )
    return jax.shard_map(
        per_device,
        mesh=mesh,
        in_specs=placed,
        out_specs=P(("groups", "ctx", "head"), None),
        check_vma=False,
    )
```

```python
import math

import jax
import numpy as np
import jax.numpy as jnp
from jax import lax
from jax.experimental import pallas as pl
from jax.experimental.pallas import tpu as pltpu
from jax.sharding import PartitionSpec as P

HEADS = 32
KD = 16
VD = 128
WINDOW = 64


outer_scale = 1.0 / (4.0 * math.sqrt(2.0))
epsilon = 1e-06


def shifted(shard, axis, by):
    peers = lax.axis_size(axis)
    pairs = [(i, i + by) for i in range(peers) if 0 <= i + by < peers]
    return lax.ppermute(shard, axis, pairs)


def unique_features(vector, doubled):
    rows, cols = np.triu_indices(KD)
    pick_rows = jnp.asarray(np.eye(KD)[:, rows], jnp.bfloat16)
    pick_cols = jnp.asarray(np.eye(KD)[:, cols], jnp.bfloat16)
    first = jnp.einsum("...d,df->...f", vector, pick_rows, preferred_element_type=jnp.float32)
    second = jnp.einsum("...d,df->...f", vector, pick_cols, preferred_element_type=jnp.float32)
    prod = ((first * second) * outer_scale).astype(jnp.bfloat16)
    if doubled:
        prod = prod * jnp.asarray(np.where(rows == cols, 1.0, 2.0), jnp.bfloat16)
    lead = vector.shape[:-1]
    unit = jnp.ones(lead + (1,), jnp.bfloat16)
    half = (vector.astype(jnp.float32) * 0.5).astype(jnp.bfloat16)
    return jnp.concatenate([unit, half, prod], axis=-1)


CHUNK = 128
LEAD = 128


def local_attention_kernel(flag_ref, q_ref, kt_ref, vx_ref, intra_ref, win_ref, *, span_rows, block_rows):
    first_span = flag_ref[0] == 1
    for i in range(span_rows // CHUNK):
        r0 = i * CHUNK
        q_c = q_ref[0, r0 : r0 + CHUNK, :]
        bs = (r0 // block_rows) * block_rows
        width = r0 + CHUNK - bs
        k_i = kt_ref[0, :, LEAD + bs : LEAD + r0 + CHUNK]
        v_i = vx_ref[0, LEAD + bs : LEAD + r0 + CHUNK, :]
        scores = jnp.dot(q_c, k_i, preferred_element_type=jnp.float32) * 0.25
        row = lax.broadcasted_iota(jnp.int32, (CHUNK, width), 0)
        col = lax.broadcasted_iota(jnp.int32, (CHUNK, width), 1)
        kernel = jnp.where(
            col <= row + (r0 - bs), 1.0 + scores + 0.5 * scores * scores, 0.0
        ).astype(jnp.bfloat16)
        intra_ref[r0 : r0 + CHUNK, :] = jnp.dot(kernel, v_i, preferred_element_type=jnp.float32)

        k_w = kt_ref[0, :, r0 : r0 + CHUNK + LEAD]
        v_w = vx_ref[0, r0 : r0 + CHUNK + LEAD, :]
        ws = jnp.dot(q_c, k_w, preferred_element_type=jnp.float32) * 0.25
        wrow = lax.broadcasted_iota(jnp.int32, (CHUNK, CHUNK + LEAD), 0)
        wcol = lax.broadcasted_iota(jnp.int32, (CHUNK, CHUNK + LEAD), 1)
        valid = (wcol > wrow + LEAD - WINDOW) & (wcol <= wrow + LEAD)
        if i == 0:
            valid = valid & ((wcol >= LEAD) | jnp.logical_not(first_span))
        masked = jnp.where(valid, ws, -jnp.inf)
        highest = jnp.max(masked, axis=1, keepdims=True)
        expo = jnp.where(valid, jnp.exp(ws - highest), 0.0)
        weights = (expo / jnp.sum(expo, axis=1, keepdims=True)).astype(jnp.bfloat16)
        win_ref[r0 : r0 + CHUNK, :] = jnp.dot(weights, v_w, preferred_element_type=jnp.float32)


def local_attention(flag, q_hm, kt_hm, vx, block_rows):
    heads_here, span_rows, _ = q_hm.shape
    ext = kt_hm.shape[2]
    body = lambda *refs: local_attention_kernel(*refs, span_rows=span_rows, block_rows=block_rows)
    out = jax.ShapeDtypeStruct((span_rows, heads_here * VD), jnp.float32)
    return pl.pallas_call(
        body,
        grid_spec=pltpu.PrefetchScalarGridSpec(
            num_scalar_prefetch=1,
            grid=(heads_here,),
            in_specs=[
                pl.BlockSpec((1, span_rows, KD), lambda h, f: (h, 0, 0)),
                pl.BlockSpec((1, KD, ext), lambda h, f: (h, 0, 0)),
                pl.BlockSpec((1, ext, VD), lambda h, f: (h, 0, 0)),
            ],
            out_specs=[
                pl.BlockSpec((span_rows, VD), lambda h, f: (0, h)),
                pl.BlockSpec((span_rows, VD), lambda h, f: (0, h)),
            ],
        ),
        out_shape=(out, out),
    )(flag, q_hm, kt_hm, vx)


def mix_kernel(intra_ref, inter_ref, win_ref, gain_ref, out_ref):
    linear = intra_ref[...] + inter_ref[0]
    scale = lax.rsqrt(jnp.mean(linear * linear, axis=1, keepdims=True) + epsilon)
    out_ref[...] = (linear * scale * gain_ref[...] + win_ref[...]).astype(jnp.bfloat16)


def mix(intra, inter_hm, window, gain, offset):
    heads_group, span_rows, _ = inter_hm.shape
    tile = pl.BlockSpec((span_rows, VD), lambda h: (0, h + offset))
    return pl.pallas_call(
        mix_kernel,
        grid=(heads_group,),
        in_specs=[
            tile,
            pl.BlockSpec((1, span_rows, VD), lambda h: (h, 0, 0)),
            tile,
            pl.BlockSpec((1, VD), lambda h: (0, h + offset)),
        ],
        out_specs=pl.BlockSpec((span_rows, VD), lambda h: (0, h)),
        out_shape=jax.ShapeDtypeStruct((span_rows, heads_group * VD), jnp.bfloat16),
    )(intra, inter_hm, window, gain.reshape(1, gain.shape[0]))


def per_device(queries, keys, values, gain):
    local_tokens = queries.shape[0]

    def to_heads(tok, width):
        tok = jnp.transpose(tok.reshape(local_tokens, HEADS, width), (1, 0, 2))
        return lax.all_to_all(tok, "head", split_axis=0, concat_axis=1, tiled=True)

    value_hm = to_heads(values, VD)
    key_hm = to_heads(keys, KD)
    heads_here, span_rows, _ = key_hm.shape
    block_rows = min(512, span_rows)
    block_count = span_rows // block_rows
    first_span = lax.axis_index("ctx") == 0

    tails = shifted(
        jnp.concatenate([key_hm, value_hm], axis=2)[:, span_rows - WINDOW :], "ctx", 1
    )

    key_feat = unique_features(key_hm.reshape(heads_here, block_count, block_rows, KD), False)
    block_states = jnp.einsum(
        "hnrf,hnrv->hnfv",
        key_feat,
        value_hm.reshape(heads_here, block_count, block_rows, VD),
        preferred_element_type=jnp.float32,
    )
    span_state = jnp.sum(block_states, axis=1)
    groups = 2 if heads_here % 2 == 0 else 1
    group_heads = heads_here // groups
    everything = [lax.all_gather(span_state[:group_heads], "ctx")]
    queries, span_state = lax.optimization_barrier((queries, span_state))
    query_hm = to_heads(queries, KD)
    peers = everything[0].shape[0]
    here = lax.axis_index("ctx")
    before = jnp.concatenate(
        [jnp.zeros_like(block_states[:, :1]), jnp.cumsum(block_states[:, :-1], axis=1)], axis=1
    )
    query_feat = unique_features(query_hm.reshape(heads_here, block_count, block_rows, KD), True)

    lead = jnp.zeros((heads_here, LEAD - WINDOW, KD + VD), jnp.bfloat16)
    key_ext = jnp.concatenate([lead[:, :, :KD], tails[:, :, :KD], key_hm], axis=1)
    value_ext = jnp.concatenate([lead[:, :, KD:], tails[:, :, KD:], value_hm], axis=1)
    flag = first_span.astype(jnp.int32).reshape(1)
    intra, window = local_attention(
        flag, query_hm, jnp.transpose(key_ext, (0, 2, 1)), value_ext, block_rows
    )

    outs = []
    for g in range(groups):
        heads = slice(g * group_heads, (g + 1) * group_heads)
        if g > 0:
            span_part, _ = lax.optimization_barrier((span_state[heads], intra))
            everything.append(lax.all_gather(span_part, "ctx"))
        gathered = everything[g]
        if g > 0:
            gathered, outs[-1] = lax.optimization_barrier((gathered, outs[-1]))
        entering = jnp.sum(
            jnp.where(
                (jnp.arange(peers) < here)[:, None, None, None], gathered, jnp.zeros_like(gathered)
            ),
            axis=0,
        )
        states = (before[heads] + entering[:, None]).astype(jnp.bfloat16)
        inter = jnp.einsum(
            "hnrf,hnfv->hnrv", query_feat[heads], states, preferred_element_type=jnp.float32
        ).reshape(group_heads, span_rows, VD)
        mixed = mix(intra, inter, window, gain, g * group_heads)
        back = lax.all_to_all(mixed, "head", split_axis=0, concat_axis=1, tiled=True)
        outs.append(back)
    peers_head = lax.axis_size("head")
    tokens_back = jnp.stack(
        [o.reshape(local_tokens, peers_head, group_heads * VD) for o in outs], axis=2
    )
    return tokens_back.reshape(local_tokens, HEADS * VD)


def solution(mesh):
    placed = (
        P(("groups", "ctx", "head"), None),
        P(("groups", "ctx", "head"), None),
        P(("groups", "ctx", "head"), None),
        P("head"),
    )
    return jax.shard_map(
        per_device,
        mesh=mesh,
        in_specs=placed,
        out_specs=P(("groups", "ctx", "head"), None),
        check_vma=False,
    )
```

```python
import math

import jax
import numpy as np
import jax.numpy as jnp
from jax import lax
from jax.experimental import pallas as pl
from jax.experimental.pallas import tpu as pltpu
from jax.sharding import PartitionSpec as P

HEADS = 32
KD = 16
VD = 128
WINDOW = 64


outer_scale = 1.0 / (4.0 * math.sqrt(2.0))
epsilon = 1e-06


def shifted(shard, axis, by):
    peers = lax.axis_size(axis)
    pairs = [(i, i + by) for i in range(peers) if 0 <= i + by < peers]
    return lax.ppermute(shard, axis, pairs)


def unique_features(vector, doubled):
    rows, cols = np.triu_indices(KD)
    pick_rows = jnp.asarray(np.eye(KD)[:, rows], jnp.bfloat16)
    pick_cols = jnp.asarray(np.eye(KD)[:, cols], jnp.bfloat16)
    first = jnp.einsum("...d,df->...f", vector, pick_rows, preferred_element_type=jnp.float32)
    second = jnp.einsum("...d,df->...f", vector, pick_cols, preferred_element_type=jnp.float32)
    prod = ((first * second) * outer_scale).astype(jnp.bfloat16)
    if doubled:
        prod = prod * jnp.asarray(np.where(rows == cols, 1.0, 2.0), jnp.bfloat16)
    lead = vector.shape[:-1]
    unit = jnp.ones(lead + (1,), jnp.bfloat16)
    half = (vector.astype(jnp.float32) * 0.5).astype(jnp.bfloat16)
    return jnp.concatenate([unit, half, prod], axis=-1)


CHUNK = 128
LEAD = 128


def local_attention_kernel(flag_ref, q_ref, kt_ref, vx_ref, intra_ref, win_ref, *, span_rows, block_rows):
    first_span = flag_ref[0] == 1
    for i in range(span_rows // CHUNK):
        r0 = i * CHUNK
        q_c = q_ref[0, r0 : r0 + CHUNK, :]
        bs = (r0 // block_rows) * block_rows
        width = r0 + CHUNK - bs
        k_i = kt_ref[0, :, LEAD + bs : LEAD + r0 + CHUNK]
        v_i = vx_ref[0, LEAD + bs : LEAD + r0 + CHUNK, :]
        scores = jnp.dot(q_c, k_i, preferred_element_type=jnp.float32) * 0.25
        row = lax.broadcasted_iota(jnp.int32, (CHUNK, width), 0)
        col = lax.broadcasted_iota(jnp.int32, (CHUNK, width), 1)
        kernel = jnp.where(
            col <= row + (r0 - bs), 1.0 + scores + 0.5 * scores * scores, 0.0
        ).astype(jnp.bfloat16)
        intra_ref[r0 : r0 + CHUNK, :] = jnp.dot(kernel, v_i, preferred_element_type=jnp.float32)

        k_w = kt_ref[0, :, r0 : r0 + CHUNK + LEAD]
        v_w = vx_ref[0, r0 : r0 + CHUNK + LEAD, :]
        ws = jnp.dot(q_c, k_w, preferred_element_type=jnp.float32) * 0.25
        wrow = lax.broadcasted_iota(jnp.int32, (CHUNK, CHUNK + LEAD), 0)
        wcol = lax.broadcasted_iota(jnp.int32, (CHUNK, CHUNK + LEAD), 1)
        valid = (wcol > wrow + LEAD - WINDOW) & (wcol <= wrow + LEAD)
        if i == 0:
            valid = valid & ((wcol >= LEAD) | jnp.logical_not(first_span))
        masked = jnp.where(valid, ws, -jnp.inf)
        highest = jnp.max(masked, axis=1, keepdims=True)
        expo = jnp.where(valid, jnp.exp(ws - highest), 0.0)
        weights = (expo / jnp.sum(expo, axis=1, keepdims=True)).astype(jnp.bfloat16)
        win_ref[r0 : r0 + CHUNK, :] = jnp.dot(weights, v_w, preferred_element_type=jnp.float32)


def local_attention(flag, q_hm, kt_hm, vx, block_rows):
    heads_here, span_rows, _ = q_hm.shape
    ext = kt_hm.shape[2]
    body = lambda *refs: local_attention_kernel(*refs, span_rows=span_rows, block_rows=block_rows)
    out = jax.ShapeDtypeStruct((span_rows, heads_here * VD), jnp.float32)
    return pl.pallas_call(
        body,
        grid_spec=pltpu.PrefetchScalarGridSpec(
            num_scalar_prefetch=1,
            grid=(heads_here,),
            in_specs=[
                pl.BlockSpec((1, span_rows, KD), lambda h, f: (h, 0, 0)),
                pl.BlockSpec((1, KD, ext), lambda h, f: (h, 0, 0)),
                pl.BlockSpec((1, ext, VD), lambda h, f: (h, 0, 0)),
            ],
            out_specs=[
                pl.BlockSpec((span_rows, VD), lambda h, f: (0, h)),
                pl.BlockSpec((span_rows, VD), lambda h, f: (0, h)),
            ],
        ),
        out_shape=(out, out),
    )(flag, q_hm, kt_hm, vx)


def mix_kernel(intra_ref, inter_ref, win_ref, gain_ref, out_ref):
    linear = intra_ref[...] + inter_ref[0]
    scale = lax.rsqrt(jnp.mean(linear * linear, axis=1, keepdims=True) + epsilon)
    out_ref[...] = (linear * scale * gain_ref[...] + win_ref[...]).astype(jnp.bfloat16)


def mix(intra, inter_hm, window, gain):
    heads_here, span_rows, _ = inter_hm.shape
    tile = pl.BlockSpec((span_rows, VD), lambda h: (0, h))
    return pl.pallas_call(
        mix_kernel,
        grid=(heads_here,),
        in_specs=[
            tile,
            pl.BlockSpec((1, span_rows, VD), lambda h: (h, 0, 0)),
            tile,
            pl.BlockSpec((1, VD), lambda h: (0, h)),
        ],
        out_specs=tile,
        out_shape=jax.ShapeDtypeStruct((span_rows, heads_here * VD), jnp.bfloat16),
    )(intra, inter_hm, window, gain.reshape(1, heads_here * VD))


def per_device(queries, keys, values, gain):
    local_tokens = queries.shape[0]

    def to_heads(tok, width):
        tok = jnp.transpose(tok.reshape(local_tokens, HEADS, width), (1, 0, 2))
        return lax.all_to_all(tok, "head", split_axis=0, concat_axis=1, tiled=True)

    value_hm = to_heads(values, VD)
    key_hm = to_heads(keys, KD)
    heads_here, span_rows, _ = key_hm.shape
    block_rows = min(512, span_rows)
    block_count = span_rows // block_rows
    first_span = lax.axis_index("ctx") == 0

    tails = shifted(
        jnp.concatenate([key_hm, value_hm], axis=2)[:, span_rows - WINDOW :], "ctx", 1
    )

    key_feat = unique_features(key_hm.reshape(heads_here, block_count, block_rows, KD), False)
    block_states = jnp.einsum(
        "hnrf,hnrv->hnfv",
        key_feat,
        value_hm.reshape(heads_here, block_count, block_rows, VD),
        preferred_element_type=jnp.float32,
    )
    span_state = jnp.sum(block_states, axis=1)
    peers = lax.axis_size("ctx")
    running = span_state
    entering = None
    first_round = span_state
    shift = 1
    while shift < peers:
        received = shifted(running, "ctx", shift)
        entering = received if entering is None else entering + received
        if shift == 1:
            first_round = received
        shift *= 2
        if shift < peers:
            running = running + received
    if entering is None:
        entering = jnp.zeros_like(span_state)
    queries, span_state = lax.optimization_barrier((queries, span_state))
    query_hm = to_heads(queries, KD)
    query_hm, first_round = lax.optimization_barrier((query_hm, first_round))
    before = jnp.concatenate(
        [jnp.zeros_like(block_states[:, :1]), jnp.cumsum(block_states[:, :-1], axis=1)], axis=1
    )
    states = (before + entering[:, None]).astype(jnp.bfloat16)

    query_feat = unique_features(query_hm.reshape(heads_here, block_count, block_rows, KD), True)
    inter = jnp.einsum(
        "hnrf,hnfv->hnrv",
        query_feat,
        states,
        preferred_element_type=jnp.float32,
    ).reshape(heads_here, span_rows, VD)

    lead = jnp.zeros((heads_here, LEAD - WINDOW, KD + VD), jnp.bfloat16)
    key_ext = jnp.concatenate([lead[:, :, :KD], tails[:, :, :KD], key_hm], axis=1)
    value_ext = jnp.concatenate([lead[:, :, KD:], tails[:, :, KD:], value_hm], axis=1)
    flag = first_span.astype(jnp.int32).reshape(1)
    intra, window = local_attention(
        flag, query_hm, jnp.transpose(key_ext, (0, 2, 1)), value_ext, block_rows
    )
    mixed = mix(intra, inter, window, gain)
    tokens_back = lax.all_to_all(mixed, "head", split_axis=0, concat_axis=1, tiled=True)
    return tokens_back


def solution(mesh):
    placed = (
        P(("groups", "ctx", "head"), None),
        P(("groups", "ctx", "head"), None),
        P(("groups", "ctx", "head"), None),
        P("head"),
    )
    return jax.shard_map(
        per_device,
        mesh=mesh,
        in_specs=placed,
        out_specs=P(("groups", "ctx", "head"), None),
        check_vma=False,
    )
```

```python
import math

import jax
import numpy as np
import jax.numpy as jnp
from jax import lax
from jax.experimental import pallas as pl
from jax.experimental.pallas import tpu as pltpu
from jax.sharding import PartitionSpec as P

HEADS = 32
KD = 16
VD = 128
WINDOW = 64


outer_scale = 1.0 / (4.0 * math.sqrt(2.0))
epsilon = 1e-06


def shifted(shard, axis, by):
    peers = lax.axis_size(axis)
    pairs = [(i, i + by) for i in range(peers) if 0 <= i + by < peers]
    return lax.ppermute(shard, axis, pairs)


def unique_features(vector, doubled):
    rows, cols = np.triu_indices(KD)
    pick_rows = jnp.asarray(np.eye(KD)[:, rows], jnp.bfloat16)
    pick_cols = jnp.asarray(np.eye(KD)[:, cols], jnp.bfloat16)
    first = jnp.einsum("...d,df->...f", vector, pick_rows, preferred_element_type=jnp.float32)
    second = jnp.einsum("...d,df->...f", vector, pick_cols, preferred_element_type=jnp.float32)
    prod = ((first * second) * outer_scale).astype(jnp.bfloat16)
    if doubled:
        prod = prod * jnp.asarray(np.where(rows == cols, 1.0, 2.0), jnp.bfloat16)
    lead = vector.shape[:-1]
    unit = jnp.ones(lead + (1,), jnp.bfloat16)
    half = (vector.astype(jnp.float32) * 0.5).astype(jnp.bfloat16)
    return jnp.concatenate([unit, half, prod], axis=-1)


CHUNK = 128
LEAD = 128


def local_attention_kernel(flag_ref, q_ref, kt_ref, vx_ref, intra_ref, win_ref, *, span_rows, block_rows):
    first_span = flag_ref[0] == 1
    for i in range(span_rows // CHUNK):
        r0 = i * CHUNK
        q_c = q_ref[0, r0 : r0 + CHUNK, :]
        bs = (r0 // block_rows) * block_rows
        width = r0 + CHUNK - bs
        k_i = kt_ref[0, :, LEAD + bs : LEAD + r0 + CHUNK]
        v_i = vx_ref[0, LEAD + bs : LEAD + r0 + CHUNK, :]
        scores = jnp.dot(q_c, k_i, preferred_element_type=jnp.float32) * 0.25
        row = lax.broadcasted_iota(jnp.int32, (CHUNK, width), 0)
        col = lax.broadcasted_iota(jnp.int32, (CHUNK, width), 1)
        kernel = jnp.where(
            col <= row + (r0 - bs), 1.0 + scores + 0.5 * scores * scores, 0.0
        ).astype(jnp.bfloat16)
        intra_ref[r0 : r0 + CHUNK, :] = jnp.dot(kernel, v_i, preferred_element_type=jnp.float32)

        k_w = kt_ref[0, :, r0 : r0 + CHUNK + LEAD]
        v_w = vx_ref[0, r0 : r0 + CHUNK + LEAD, :]
        ws = jnp.dot(q_c, k_w, preferred_element_type=jnp.float32) * 0.25
        wrow = lax.broadcasted_iota(jnp.int32, (CHUNK, CHUNK + LEAD), 0)
        wcol = lax.broadcasted_iota(jnp.int32, (CHUNK, CHUNK + LEAD), 1)
        valid = (wcol > wrow + LEAD - WINDOW) & (wcol <= wrow + LEAD)
        if i == 0:
            valid = valid & ((wcol >= LEAD) | jnp.logical_not(first_span))
        masked = jnp.where(valid, ws, -jnp.inf)
        highest = jnp.max(masked, axis=1, keepdims=True)
        expo = jnp.where(valid, jnp.exp(ws - highest), 0.0)
        weights = (expo / jnp.sum(expo, axis=1, keepdims=True)).astype(jnp.bfloat16)
        win_ref[r0 : r0 + CHUNK, :] = jnp.dot(weights, v_w, preferred_element_type=jnp.float32)


def local_attention(flag, q_hm, kt_hm, vx, block_rows):
    heads_here, span_rows, _ = q_hm.shape
    ext = kt_hm.shape[2]
    body = lambda *refs: local_attention_kernel(*refs, span_rows=span_rows, block_rows=block_rows)
    out = jax.ShapeDtypeStruct((span_rows, heads_here * VD), jnp.float32)
    return pl.pallas_call(
        body,
        grid_spec=pltpu.PrefetchScalarGridSpec(
            num_scalar_prefetch=1,
            grid=(heads_here,),
            in_specs=[
                pl.BlockSpec((1, span_rows, KD), lambda h, f: (h, 0, 0)),
                pl.BlockSpec((1, KD, ext), lambda h, f: (h, 0, 0)),
                pl.BlockSpec((1, ext, VD), lambda h, f: (h, 0, 0)),
            ],
            out_specs=[
                pl.BlockSpec((span_rows, VD), lambda h, f: (0, h)),
                pl.BlockSpec((span_rows, VD), lambda h, f: (0, h)),
            ],
        ),
        out_shape=(out, out),
    )(flag, q_hm, kt_hm, vx)


def mix_kernel(intra_ref, inter_ref, win_ref, gain_ref, out_ref):
    linear = intra_ref[...] + inter_ref[0]
    scale = lax.rsqrt(jnp.mean(linear * linear, axis=1, keepdims=True) + epsilon)
    out_ref[...] = (linear * scale * gain_ref[...] + win_ref[...]).astype(jnp.bfloat16)


def mix(intra, inter_hm, window, gain):
    heads_here, span_rows, _ = inter_hm.shape
    tile = pl.BlockSpec((span_rows, VD), lambda h: (0, h))
    return pl.pallas_call(
        mix_kernel,
        grid=(heads_here,),
        in_specs=[
            tile,
            pl.BlockSpec((1, span_rows, VD), lambda h: (h, 0, 0)),
            tile,
            pl.BlockSpec((1, VD), lambda h: (0, h)),
        ],
        out_specs=tile,
        out_shape=jax.ShapeDtypeStruct((span_rows, heads_here * VD), jnp.bfloat16),
    )(intra, inter_hm, window, gain.reshape(1, heads_here * VD))


def per_device(queries, keys, values, gain):
    local_tokens = queries.shape[0]

    def to_heads(tok, width):
        tok = jnp.transpose(tok.reshape(local_tokens, HEADS, width), (1, 0, 2))
        return lax.all_to_all(tok, "head", split_axis=0, concat_axis=1, tiled=True)

    key_hm = to_heads(keys, KD)
    query_hm = to_heads(queries, KD)
    values, query_hm = lax.optimization_barrier((values, query_hm))
    value_hm = to_heads(values, VD)
    heads_here, span_rows, _ = key_hm.shape
    block_rows = min(512, span_rows)
    block_count = span_rows // block_rows
    first_span = lax.axis_index("ctx") == 0

    tails = shifted(
        jnp.concatenate([key_hm, value_hm], axis=2)[:, span_rows - WINDOW :], "ctx", 1
    )

    key_feat = unique_features(key_hm.reshape(heads_here, block_count, block_rows, KD), False)
    block_states = jnp.einsum(
        "hnrf,hnrv->hnfv",
        key_feat,
        value_hm.reshape(heads_here, block_count, block_rows, VD),
        preferred_element_type=jnp.float32,
    )
    span_state = jnp.sum(block_states, axis=1)
    peers = lax.axis_size("ctx")
    running = span_state
    entering = None
    first_round = span_state
    shift = 1
    while shift < peers:
        received = shifted(running, "ctx", shift)
        entering = received if entering is None else entering + received
        if shift == 1:
            first_round = received
        shift *= 2
        if shift < peers:
            running = running + received
    if entering is None:
        entering = jnp.zeros_like(span_state)
    query_hm, first_round = lax.optimization_barrier((query_hm, first_round))
    before = jnp.concatenate(
        [jnp.zeros_like(block_states[:, :1]), jnp.cumsum(block_states[:, :-1], axis=1)], axis=1
    )
    states = (before + entering[:, None]).astype(jnp.bfloat16)

    query_feat = unique_features(query_hm.reshape(heads_here, block_count, block_rows, KD), True)
    inter = jnp.einsum(
        "hnrf,hnfv->hnrv",
        query_feat,
        states,
        preferred_element_type=jnp.float32,
    ).reshape(heads_here, span_rows, VD)

    lead = jnp.zeros((heads_here, LEAD - WINDOW, KD + VD), jnp.bfloat16)
    key_ext = jnp.concatenate([lead[:, :, :KD], tails[:, :, :KD], key_hm], axis=1)
    value_ext = jnp.concatenate([lead[:, :, KD:], tails[:, :, KD:], value_hm], axis=1)
    flag = first_span.astype(jnp.int32).reshape(1)
    intra, window = local_attention(
        flag, query_hm, jnp.transpose(key_ext, (0, 2, 1)), value_ext, block_rows
    )
    mixed = mix(intra, inter, window, gain)
    tokens_back = lax.all_to_all(mixed, "head", split_axis=0, concat_axis=1, tiled=True)
    return tokens_back


def solution(mesh):
    placed = (
        P(("groups", "ctx", "head"), None),
        P(("groups", "ctx", "head"), None),
        P(("groups", "ctx", "head"), None),
        P("head"),
    )
    return jax.shard_map(
        per_device,
        mesh=mesh,
        in_specs=placed,
        out_specs=P(("groups", "ctx", "head"), None),
        check_vma=False,
    )
```

```python
import math

import jax
import numpy as np
import jax.numpy as jnp
from jax import lax
from jax.experimental import pallas as pl
from jax.experimental.pallas import tpu as pltpu
from jax.sharding import PartitionSpec as P

HEADS = 32
KD = 16
VD = 128
WINDOW = 64


outer_scale = 1.0 / (4.0 * math.sqrt(2.0))
epsilon = 1e-06


def shifted(shard, axis, by):
    peers = lax.axis_size(axis)
    pairs = [(i, i + by) for i in range(peers) if 0 <= i + by < peers]
    return lax.ppermute(shard, axis, pairs)


def unique_features(vector, doubled):
    rows, cols = np.triu_indices(KD)
    pick_rows = jnp.asarray(np.eye(KD)[:, rows], jnp.bfloat16)
    pick_cols = jnp.asarray(np.eye(KD)[:, cols], jnp.bfloat16)
    first = jnp.einsum("...d,df->...f", vector, pick_rows, preferred_element_type=jnp.float32)
    second = jnp.einsum("...d,df->...f", vector, pick_cols, preferred_element_type=jnp.float32)
    prod = ((first * second) * outer_scale).astype(jnp.bfloat16)
    if doubled:
        prod = prod * jnp.asarray(np.where(rows == cols, 1.0, 2.0), jnp.bfloat16)
    lead = vector.shape[:-1]
    unit = jnp.ones(lead + (1,), jnp.bfloat16)
    half = (vector.astype(jnp.float32) * 0.5).astype(jnp.bfloat16)
    return jnp.concatenate([unit, half, prod], axis=-1)


CHUNK = 128
LEAD = 128


def local_attention_kernel(
    flag_ref, q_ref, kt_ref, ktail_ref, v_ref, vtail_ref, intra_ref, win_ref, *, span_rows, block_rows
):
    first_span = flag_ref[0] == 1
    for i in range(span_rows // CHUNK):
        r0 = i * CHUNK
        q_c = q_ref[0, r0 : r0 + CHUNK, :]
        bs = (r0 // block_rows) * block_rows
        width = r0 + CHUNK - bs
        k_i = kt_ref[0, :, bs : r0 + CHUNK]
        v_i = v_ref[0, bs : r0 + CHUNK, :]
        scores = jnp.dot(q_c, k_i, preferred_element_type=jnp.float32) * 0.25
        row = lax.broadcasted_iota(jnp.int32, (CHUNK, width), 0)
        col = lax.broadcasted_iota(jnp.int32, (CHUNK, width), 1)
        kernel = jnp.where(
            col <= row + (r0 - bs), 1.0 + scores + 0.5 * scores * scores, 0.0
        ).astype(jnp.bfloat16)
        intra_ref[r0 : r0 + CHUNK, :] = jnp.dot(kernel, v_i, preferred_element_type=jnp.float32)

        if i == 0:
            k_w = jnp.concatenate([ktail_ref[0], kt_ref[0, :, 0:CHUNK]], axis=1)
            v_w = jnp.concatenate([vtail_ref[0], v_ref[0, 0:CHUNK, :]], axis=0)
        else:
            k_w = kt_ref[0, :, r0 - LEAD : r0 + CHUNK]
            v_w = v_ref[0, r0 - LEAD : r0 + CHUNK, :]
        ws = jnp.dot(q_c, k_w, preferred_element_type=jnp.float32) * 0.25
        wrow = lax.broadcasted_iota(jnp.int32, (CHUNK, CHUNK + LEAD), 0)
        wcol = lax.broadcasted_iota(jnp.int32, (CHUNK, CHUNK + LEAD), 1)
        valid = (wcol > wrow + LEAD - WINDOW) & (wcol <= wrow + LEAD)
        if i == 0:
            valid = valid & ((wcol >= LEAD) | jnp.logical_not(first_span))
        masked = jnp.where(valid, ws, -jnp.inf)
        highest = jnp.max(masked, axis=1, keepdims=True)
        expo = jnp.where(valid, jnp.exp(ws - highest), 0.0)
        weights = (expo / jnp.sum(expo, axis=1, keepdims=True)).astype(jnp.bfloat16)
        win_ref[r0 : r0 + CHUNK, :] = jnp.dot(weights, v_w, preferred_element_type=jnp.float32)


def local_attention(flag, q_hm, kt_hm, ktail, v_hm, vtail, block_rows):
    heads_here, span_rows, _ = q_hm.shape
    body = lambda *refs: local_attention_kernel(*refs, span_rows=span_rows, block_rows=block_rows)
    out = jax.ShapeDtypeStruct((span_rows, heads_here * VD), jnp.float32)
    return pl.pallas_call(
        body,
        grid_spec=pltpu.PrefetchScalarGridSpec(
            num_scalar_prefetch=1,
            grid=(heads_here,),
            in_specs=[
                pl.BlockSpec((1, span_rows, KD), lambda h, f: (h, 0, 0)),
                pl.BlockSpec((1, KD, span_rows), lambda h, f: (h, 0, 0)),
                pl.BlockSpec((1, KD, LEAD), lambda h, f: (h, 0, 0)),
                pl.BlockSpec((1, span_rows, VD), lambda h, f: (h, 0, 0)),
                pl.BlockSpec((1, LEAD, VD), lambda h, f: (h, 0, 0)),
            ],
            out_specs=[
                pl.BlockSpec((span_rows, VD), lambda h, f: (0, h)),
                pl.BlockSpec((span_rows, VD), lambda h, f: (0, h)),
            ],
        ),
        out_shape=(out, out),
    )(flag, q_hm, kt_hm, ktail, v_hm, vtail)


def mix_kernel(intra_ref, inter_ref, win_ref, gain_ref, out_ref):
    linear = intra_ref[...] + inter_ref[0]
    scale = lax.rsqrt(jnp.mean(linear * linear, axis=1, keepdims=True) + epsilon)
    out_ref[...] = (linear * scale * gain_ref[...] + win_ref[...]).astype(jnp.bfloat16)


def mix(intra, inter_hm, window, gain):
    heads_here, span_rows, _ = inter_hm.shape
    tile = pl.BlockSpec((span_rows, VD), lambda h: (0, h))
    return pl.pallas_call(
        mix_kernel,
        grid=(heads_here,),
        in_specs=[
            tile,
            pl.BlockSpec((1, span_rows, VD), lambda h: (h, 0, 0)),
            tile,
            pl.BlockSpec((1, VD), lambda h: (0, h)),
        ],
        out_specs=tile,
        out_shape=jax.ShapeDtypeStruct((span_rows, heads_here * VD), jnp.bfloat16),
    )(intra, inter_hm, window, gain.reshape(1, heads_here * VD))


def per_device(queries, keys, values, gain):
    local_tokens = queries.shape[0]

    def to_heads(tok, width):
        tok = jnp.transpose(tok.reshape(local_tokens, HEADS, width), (1, 0, 2))
        return lax.all_to_all(tok, "head", split_axis=0, concat_axis=1, tiled=True)

    value_hm = to_heads(values, VD)
    key_hm = to_heads(keys, KD)
    heads_here, span_rows, _ = key_hm.shape
    block_rows = min(512, span_rows)
    block_count = span_rows // block_rows
    first_span = lax.axis_index("ctx") == 0

    tails = shifted(
        jnp.concatenate([key_hm, value_hm], axis=2)[:, span_rows - WINDOW :], "ctx", 1
    )

    key_feat = unique_features(key_hm.reshape(heads_here, block_count, block_rows, KD), False)
    block_states = jnp.einsum(
        "hnrf,hnrv->hnfv",
        key_feat,
        value_hm.reshape(heads_here, block_count, block_rows, VD),
        preferred_element_type=jnp.float32,
    )
    span_state = jnp.sum(block_states, axis=1)
    peers = lax.axis_size("ctx")
    running = span_state
    entering = None
    first_round = span_state
    shift = 1
    while shift < peers:
        received = shifted(running, "ctx", shift)
        entering = received if entering is None else entering + received
        if shift == 1:
            first_round = received
        shift *= 2
        if shift < peers:
            running = running + received
    if entering is None:
        entering = jnp.zeros_like(span_state)
    queries, span_state = lax.optimization_barrier((queries, span_state))
    query_hm = to_heads(queries, KD)
    query_hm, first_round = lax.optimization_barrier((query_hm, first_round))
    before = jnp.concatenate(
        [jnp.zeros_like(block_states[:, :1]), jnp.cumsum(block_states[:, :-1], axis=1)], axis=1
    )
    states = (before + entering[:, None]).astype(jnp.bfloat16)

    query_feat = unique_features(query_hm.reshape(heads_here, block_count, block_rows, KD), True)
    inter = jnp.einsum(
        "hnrf,hnfv->hnrv",
        query_feat,
        states,
        preferred_element_type=jnp.float32,
    ).reshape(heads_here, span_rows, VD)

    lead = jnp.zeros((heads_here, LEAD - WINDOW, KD + VD), jnp.bfloat16)
    key_tail = jnp.concatenate([lead[:, :, :KD], tails[:, :, :KD]], axis=1)
    value_tail = jnp.concatenate([lead[:, :, KD:], tails[:, :, KD:]], axis=1)
    flag = first_span.astype(jnp.int32).reshape(1)
    intra, window = local_attention(
        flag,
        query_hm,
        jnp.transpose(key_hm, (0, 2, 1)),
        jnp.transpose(key_tail, (0, 2, 1)),
        value_hm,
        value_tail,
        block_rows,
    )
    mixed = mix(intra, inter, window, gain)
    tokens_back = lax.all_to_all(mixed, "head", split_axis=0, concat_axis=1, tiled=True)
    return tokens_back


def solution(mesh):
    placed = (
        P(("groups", "ctx", "head"), None),
        P(("groups", "ctx", "head"), None),
        P(("groups", "ctx", "head"), None),
        P("head"),
    )
    return jax.shard_map(
        per_device,
        mesh=mesh,
        in_specs=placed,
        out_specs=P(("groups", "ctx", "head"), None),
        check_vma=False,
    )
```

```python
import math

import jax
import numpy as np
import jax.numpy as jnp
from jax import lax
from jax.experimental import pallas as pl
from jax.experimental.pallas import tpu as pltpu
from jax.sharding import PartitionSpec as P

HEADS = 32
KD = 16
VD = 128
WINDOW = 64


outer_scale = 1.0 / (4.0 * math.sqrt(2.0))
epsilon = 1e-06


def shifted(shard, axis, by):
    peers = lax.axis_size(axis)
    pairs = [(i, i + by) for i in range(peers) if 0 <= i + by < peers]
    return lax.ppermute(shard, axis, pairs)


def unique_features(vector, doubled):
    rows, cols = np.triu_indices(KD)
    pick_rows = jnp.asarray(np.eye(KD)[:, rows], jnp.bfloat16)
    pick_cols = jnp.asarray(np.eye(KD)[:, cols], jnp.bfloat16)
    first = jnp.einsum("...d,df->...f", vector, pick_rows, preferred_element_type=jnp.float32)
    second = jnp.einsum("...d,df->...f", vector, pick_cols, preferred_element_type=jnp.float32)
    prod = ((first * second) * outer_scale).astype(jnp.bfloat16)
    if doubled:
        prod = prod * jnp.asarray(np.where(rows == cols, 1.0, 2.0), jnp.bfloat16)
    lead = vector.shape[:-1]
    unit = jnp.ones(lead + (1,), jnp.bfloat16)
    half = (vector.astype(jnp.float32) * 0.5).astype(jnp.bfloat16)
    return jnp.concatenate([unit, half, prod], axis=-1)


CHUNK = 128
LEAD = 128


def local_attention_kernel(flag_ref, q_ref, kt_ref, vx_ref, intra_ref, win_ref, *, span_rows, block_rows):
    first_span = flag_ref[0] == 1
    for i in range(span_rows // CHUNK):
        r0 = i * CHUNK
        q_c = q_ref[0, r0 : r0 + CHUNK, :]
        bs = (r0 // block_rows) * block_rows
        width = r0 + CHUNK - bs
        k_i = kt_ref[0, :, LEAD + bs : LEAD + r0 + CHUNK]
        v_i = vx_ref[0, LEAD + bs : LEAD + r0 + CHUNK, :]
        scores = jnp.dot(q_c, k_i, preferred_element_type=jnp.float32) * 0.25
        row = lax.broadcasted_iota(jnp.int32, (CHUNK, width), 0)
        col = lax.broadcasted_iota(jnp.int32, (CHUNK, width), 1)
        kernel = jnp.where(
            col <= row + (r0 - bs), 1.0 + scores + 0.5 * scores * scores, 0.0
        ).astype(jnp.bfloat16)
        intra_ref[r0 : r0 + CHUNK, :] = jnp.dot(kernel, v_i, preferred_element_type=jnp.float32)

        k_w = kt_ref[0, :, r0 : r0 + CHUNK + LEAD]
        v_w = vx_ref[0, r0 : r0 + CHUNK + LEAD, :]
        ws = jnp.dot(q_c, k_w, preferred_element_type=jnp.float32) * 0.25
        wrow = lax.broadcasted_iota(jnp.int32, (CHUNK, CHUNK + LEAD), 0)
        wcol = lax.broadcasted_iota(jnp.int32, (CHUNK, CHUNK + LEAD), 1)
        valid = (wcol > wrow + LEAD - WINDOW) & (wcol <= wrow + LEAD)
        if i == 0:
            valid = valid & ((wcol >= LEAD) | jnp.logical_not(first_span))
        masked = jnp.where(valid, ws, -jnp.inf)
        highest = jnp.max(masked, axis=1, keepdims=True)
        expo = jnp.where(valid, jnp.exp(ws - highest), 0.0)
        weights = (expo / jnp.sum(expo, axis=1, keepdims=True)).astype(jnp.bfloat16)
        win_ref[r0 : r0 + CHUNK, :] = jnp.dot(weights, v_w, preferred_element_type=jnp.float32)


def local_attention(flag, q_hm, kt_hm, vx, block_rows):
    heads_here, span_rows, _ = q_hm.shape
    ext = kt_hm.shape[2]
    body = lambda *refs: local_attention_kernel(*refs, span_rows=span_rows, block_rows=block_rows)
    out = jax.ShapeDtypeStruct((span_rows, heads_here * VD), jnp.float32)
    return pl.pallas_call(
        body,
        grid_spec=pltpu.PrefetchScalarGridSpec(
            num_scalar_prefetch=1,
            grid=(heads_here,),
            in_specs=[
                pl.BlockSpec((1, span_rows, KD), lambda h, f: (h, 0, 0)),
                pl.BlockSpec((1, KD, ext), lambda h, f: (h, 0, 0)),
                pl.BlockSpec((1, ext, VD), lambda h, f: (h, 0, 0)),
            ],
            out_specs=[
                pl.BlockSpec((span_rows, VD), lambda h, f: (0, h)),
                pl.BlockSpec((span_rows, VD), lambda h, f: (0, h)),
            ],
        ),
        out_shape=(out, out),
    )(flag, q_hm, kt_hm, vx)


def mix_kernel(intra_ref, inter_ref, win_ref, gain_ref, out_ref):
    linear = intra_ref[...] + inter_ref[0]
    scale = lax.rsqrt(jnp.mean(linear * linear, axis=1, keepdims=True) + epsilon)
    out_ref[...] = (linear * scale * gain_ref[...] + win_ref[...]).astype(jnp.bfloat16)


def mix(intra, inter_hm, window, gain):
    heads_here, span_rows, _ = inter_hm.shape
    tile = pl.BlockSpec((span_rows, VD), lambda h: (0, h))
    return pl.pallas_call(
        mix_kernel,
        grid=(heads_here,),
        in_specs=[
            tile,
            pl.BlockSpec((1, span_rows, VD), lambda h: (h, 0, 0)),
            tile,
            pl.BlockSpec((1, VD), lambda h: (0, h)),
        ],
        out_specs=tile,
        out_shape=jax.ShapeDtypeStruct((span_rows, heads_here * VD), jnp.bfloat16),
    )(intra, inter_hm, window, gain.reshape(1, heads_here * VD))


def per_device(queries, keys, values, gain):
    local_tokens = queries.shape[0]

    def to_heads(tok, width):
        tok = jnp.transpose(tok.reshape(local_tokens, HEADS, width), (1, 0, 2))
        return lax.all_to_all(tok, "head", split_axis=0, concat_axis=1, tiled=True)

    value_hm = to_heads(values, VD)
    key_hm = to_heads(keys, KD)
    heads_here, span_rows, _ = key_hm.shape
    block_rows = min(512, span_rows)
    block_count = span_rows // block_rows
    first_span = lax.axis_index("ctx") == 0


    key_feat = unique_features(key_hm.reshape(heads_here, block_count, block_rows, KD), False)
    block_states = jnp.einsum(
        "hnrf,hnrv->hnfv",
        key_feat,
        value_hm.reshape(heads_here, block_count, block_rows, VD),
        preferred_element_type=jnp.float32,
    )
    span_state = jnp.sum(block_states, axis=1)
    peers = lax.axis_size("ctx")
    running = span_state
    entering = None
    first_round = span_state
    shift = 1
    tail = jnp.concatenate([key_hm, value_hm], axis=2)[:, span_rows - WINDOW :]
    tail_rows = WINDOW * (KD + VD) // VD
    while shift < peers:
        if shift == 1:
            packed = jnp.concatenate(
                [running, tail.astype(jnp.float32).reshape(heads_here, tail_rows, VD)], axis=1
            )
            got = shifted(packed, "ctx", shift)
            received = got[:, : running.shape[1]]
            tails = got[:, running.shape[1] :].reshape(heads_here, WINDOW, KD + VD)
            tails = tails.astype(jnp.bfloat16)
        else:
            received = shifted(running, "ctx", shift)
        entering = received if entering is None else entering + received
        if shift == 1:
            first_round = received
        shift *= 2
        if shift < peers:
            running = running + received
    if entering is None:
        entering = jnp.zeros_like(span_state)
        tails = jnp.zeros_like(tail)
    queries, span_state = lax.optimization_barrier((queries, span_state))
    query_hm = to_heads(queries, KD)
    query_hm, first_round = lax.optimization_barrier((query_hm, first_round))
    before = jnp.concatenate(
        [jnp.zeros_like(block_states[:, :1]), jnp.cumsum(block_states[:, :-1], axis=1)], axis=1
    )
    states = (before + entering[:, None]).astype(jnp.bfloat16)

    query_feat = unique_features(query_hm.reshape(heads_here, block_count, block_rows, KD), True)
    inter = jnp.einsum(
        "hnrf,hnfv->hnrv",
        query_feat,
        states,
        preferred_element_type=jnp.float32,
    ).reshape(heads_here, span_rows, VD)

    lead = jnp.zeros((heads_here, LEAD - WINDOW, KD + VD), jnp.bfloat16)
    key_ext = jnp.concatenate([lead[:, :, :KD], tails[:, :, :KD], key_hm], axis=1)
    value_ext = jnp.concatenate([lead[:, :, KD:], tails[:, :, KD:], value_hm], axis=1)
    flag = first_span.astype(jnp.int32).reshape(1)
    intra, window = local_attention(
        flag, query_hm, jnp.transpose(key_ext, (0, 2, 1)), value_ext, block_rows
    )
    mixed = mix(intra, inter, window, gain)
    tokens_back = lax.all_to_all(mixed, "head", split_axis=0, concat_axis=1, tiled=True)
    return tokens_back


def solution(mesh):
    placed = (
        P(("groups", "ctx", "head"), None),
        P(("groups", "ctx", "head"), None),
        P(("groups", "ctx", "head"), None),
        P("head"),
    )
    return jax.shard_map(
        per_device,
        mesh=mesh,
        in_specs=placed,
        out_specs=P(("groups", "ctx", "head"), None),
        check_vma=False,
    )
```

```python
import math

import jax
import numpy as np
import jax.numpy as jnp
from jax import lax
from jax.experimental import pallas as pl
from jax.experimental.pallas import tpu as pltpu
from jax.sharding import PartitionSpec as P

HEADS = 32
KD = 16
VD = 128
WINDOW = 64


outer_scale = 1.0 / (4.0 * math.sqrt(2.0))
epsilon = 1e-06


def shifted(shard, axis, by):
    peers = lax.axis_size(axis)
    pairs = [(i, i + by) for i in range(peers) if 0 <= i + by < peers]
    return lax.ppermute(shard, axis, pairs)


def unique_features(vector, doubled):
    rows, cols = np.triu_indices(KD)
    pick_rows = jnp.asarray(np.eye(KD)[:, rows], jnp.bfloat16)
    pick_cols = jnp.asarray(np.eye(KD)[:, cols], jnp.bfloat16)
    first = jnp.einsum("...d,df->...f", vector, pick_rows, preferred_element_type=jnp.float32)
    second = jnp.einsum("...d,df->...f", vector, pick_cols, preferred_element_type=jnp.float32)
    prod = ((first * second) * outer_scale).astype(jnp.bfloat16)
    if doubled:
        prod = prod * jnp.asarray(np.where(rows == cols, 1.0, 2.0), jnp.bfloat16)
    lead = vector.shape[:-1]
    unit = jnp.ones(lead + (1,), jnp.bfloat16)
    half = (vector.astype(jnp.float32) * 0.5).astype(jnp.bfloat16)
    return jnp.concatenate([unit, half, prod], axis=-1)


CHUNK = 128
LEAD = 128


def local_attention_kernel(flag_ref, q_ref, kt_ref, vx_ref, intra_ref, win_ref, *, span_rows, block_rows):
    first_span = flag_ref[0] == 1
    for i in range(span_rows // CHUNK):
        r0 = i * CHUNK
        q_c = q_ref[0, r0 : r0 + CHUNK, :]
        bs = (r0 // block_rows) * block_rows
        width = r0 + CHUNK - bs
        k_i = kt_ref[0, :, LEAD + bs : LEAD + r0 + CHUNK]
        v_i = vx_ref[0, LEAD + bs : LEAD + r0 + CHUNK, :]
        scores = jnp.dot(q_c, k_i, preferred_element_type=jnp.float32) * 0.25
        row = lax.broadcasted_iota(jnp.int32, (CHUNK, width), 0)
        col = lax.broadcasted_iota(jnp.int32, (CHUNK, width), 1)
        kernel = jnp.where(
            col <= row + (r0 - bs), 1.0 + scores + 0.5 * scores * scores, 0.0
        ).astype(jnp.bfloat16)
        intra_ref[r0 : r0 + CHUNK, :] = jnp.dot(kernel, v_i, preferred_element_type=jnp.float32)

        k_w = kt_ref[0, :, r0 : r0 + CHUNK + LEAD]
        v_w = vx_ref[0, r0 : r0 + CHUNK + LEAD, :]
        ws = jnp.dot(q_c, k_w, preferred_element_type=jnp.float32) * 0.25
        wrow = lax.broadcasted_iota(jnp.int32, (CHUNK, CHUNK + LEAD), 0)
        wcol = lax.broadcasted_iota(jnp.int32, (CHUNK, CHUNK + LEAD), 1)
        valid = (wcol > wrow + LEAD - WINDOW) & (wcol <= wrow + LEAD)
        if i == 0:
            valid = valid & ((wcol >= LEAD) | jnp.logical_not(first_span))
        masked = jnp.where(valid, ws, -jnp.inf)
        highest = jnp.max(masked, axis=1, keepdims=True)
        expo = jnp.where(valid, jnp.exp(ws - highest), 0.0)
        weights = (expo / jnp.sum(expo, axis=1, keepdims=True)).astype(jnp.bfloat16)
        win_ref[r0 : r0 + CHUNK, :] = jnp.dot(weights, v_w, preferred_element_type=jnp.float32)


def local_attention(flag, q_hm, kt_hm, vx, block_rows):
    heads_here, span_rows, _ = q_hm.shape
    ext = kt_hm.shape[2]
    body = lambda *refs: local_attention_kernel(*refs, span_rows=span_rows, block_rows=block_rows)
    out = jax.ShapeDtypeStruct((span_rows, heads_here * VD), jnp.float32)
    return pl.pallas_call(
        body,
        grid_spec=pltpu.PrefetchScalarGridSpec(
            num_scalar_prefetch=1,
            grid=(heads_here,),
            in_specs=[
                pl.BlockSpec((1, span_rows, KD), lambda h, f: (h, 0, 0)),
                pl.BlockSpec((1, KD, ext), lambda h, f: (h, 0, 0)),
                pl.BlockSpec((1, ext, VD), lambda h, f: (h, 0, 0)),
            ],
            out_specs=[
                pl.BlockSpec((span_rows, VD), lambda h, f: (0, h)),
                pl.BlockSpec((span_rows, VD), lambda h, f: (0, h)),
            ],
        ),
        out_shape=(out, out),
    )(flag, q_hm, kt_hm, vx)


def mix_kernel(intra_ref, inter_ref, win_ref, gain_ref, out_ref):
    for j in range(inter_ref.shape[0]):
        cols = slice(j * VD, (j + 1) * VD)
        linear = intra_ref[:, cols] + inter_ref[j]
        scale = lax.rsqrt(jnp.mean(linear * linear, axis=1, keepdims=True) + epsilon)
        out_ref[:, cols] = (linear * scale * gain_ref[:, cols] + win_ref[:, cols]).astype(
            jnp.bfloat16
        )


def mix(intra, inter_hm, window, gain):
    heads_here, span_rows, _ = inter_hm.shape
    step = 2 if heads_here % 2 == 0 else 1
    tile = pl.BlockSpec((span_rows, step * VD), lambda h: (0, h))
    return pl.pallas_call(
        mix_kernel,
        grid=(heads_here // step,),
        in_specs=[
            tile,
            pl.BlockSpec((step, span_rows, VD), lambda h: (h, 0, 0)),
            tile,
            pl.BlockSpec((1, step * VD), lambda h: (0, h)),
        ],
        out_specs=tile,
        out_shape=jax.ShapeDtypeStruct((span_rows, heads_here * VD), jnp.bfloat16),
    )(intra, inter_hm, window, gain.reshape(1, heads_here * VD))


def per_device(queries, keys, values, gain):
    local_tokens = queries.shape[0]

    def to_heads(tok, width):
        tok = jnp.transpose(tok.reshape(local_tokens, HEADS, width), (1, 0, 2))
        return lax.all_to_all(tok, "head", split_axis=0, concat_axis=1, tiled=True)

    value_hm = to_heads(values, VD)
    key_hm = to_heads(keys, KD)
    heads_here, span_rows, _ = key_hm.shape
    block_rows = min(512, span_rows)
    block_count = span_rows // block_rows
    first_span = lax.axis_index("ctx") == 0

    tails = shifted(
        jnp.concatenate([key_hm, value_hm], axis=2)[:, span_rows - WINDOW :], "ctx", 1
    )

    key_feat = unique_features(key_hm.reshape(heads_here, block_count, block_rows, KD), False)
    block_states = jnp.einsum(
        "hnrf,hnrv->hnfv",
        key_feat,
        value_hm.reshape(heads_here, block_count, block_rows, VD),
        preferred_element_type=jnp.float32,
    )
    span_state = jnp.sum(block_states, axis=1)
    peers = lax.axis_size("ctx")
    running = span_state
    entering = None
    first_round = span_state
    shift = 1
    while shift < peers:
        received = shifted(running, "ctx", shift)
        entering = received if entering is None else entering + received
        if shift == 1:
            first_round = received
        shift *= 2
        if shift < peers:
            running = running + received
    if entering is None:
        entering = jnp.zeros_like(span_state)
    queries, span_state = lax.optimization_barrier((queries, span_state))
    query_hm = to_heads(queries, KD)
    query_hm, first_round = lax.optimization_barrier((query_hm, first_round))
    before = jnp.concatenate(
        [jnp.zeros_like(block_states[:, :1]), jnp.cumsum(block_states[:, :-1], axis=1)], axis=1
    )
    states = (before + entering[:, None]).astype(jnp.bfloat16)

    query_feat = unique_features(query_hm.reshape(heads_here, block_count, block_rows, KD), True)
    inter = jnp.einsum(
        "hnrf,hnfv->hnrv",
        query_feat,
        states,
        preferred_element_type=jnp.float32,
    ).reshape(heads_here, span_rows, VD)

    lead = jnp.zeros((heads_here, LEAD - WINDOW, KD + VD), jnp.bfloat16)
    key_ext = jnp.concatenate([lead[:, :, :KD], tails[:, :, :KD], key_hm], axis=1)
    value_ext = jnp.concatenate([lead[:, :, KD:], tails[:, :, KD:], value_hm], axis=1)
    flag = first_span.astype(jnp.int32).reshape(1)
    intra, window = local_attention(
        flag, query_hm, jnp.transpose(key_ext, (0, 2, 1)), value_ext, block_rows
    )
    mixed = mix(intra, inter, window, gain)
    tokens_back = lax.all_to_all(mixed, "head", split_axis=0, concat_axis=1, tiled=True)
    return tokens_back


def solution(mesh):
    placed = (
        P(("groups", "ctx", "head"), None),
        P(("groups", "ctx", "head"), None),
        P(("groups", "ctx", "head"), None),
        P("head"),
    )
    return jax.shard_map(
        per_device,
        mesh=mesh,
        in_specs=placed,
        out_specs=P(("groups", "ctx", "head"), None),
        check_vma=False,
    )
```

```python
import math

import jax
import numpy as np
import jax.numpy as jnp
from jax import lax
from jax.experimental import pallas as pl
from jax.experimental.pallas import tpu as pltpu
from jax.sharding import PartitionSpec as P

HEADS = 32
KD = 16
VD = 128
WINDOW = 64


outer_scale = 1.0 / (4.0 * math.sqrt(2.0))
epsilon = 1e-06


def shifted(shard, axis, by):
    peers = lax.axis_size(axis)
    pairs = [(i, i + by) for i in range(peers) if 0 <= i + by < peers]
    return lax.ppermute(shard, axis, pairs)


def unique_features(vector, doubled):
    rows, cols = np.triu_indices(KD)
    pick_rows = jnp.asarray(np.eye(KD)[:, rows], jnp.bfloat16)
    pick_cols = jnp.asarray(np.eye(KD)[:, cols], jnp.bfloat16)
    first = jnp.einsum("...d,df->...f", vector, pick_rows, preferred_element_type=jnp.float32)
    second = jnp.einsum("...d,df->...f", vector, pick_cols, preferred_element_type=jnp.float32)
    prod = ((first * second) * outer_scale).astype(jnp.bfloat16)
    if doubled:
        prod = prod * jnp.asarray(np.where(rows == cols, 1.0, 2.0), jnp.bfloat16)
    lead = vector.shape[:-1]
    unit = jnp.ones(lead + (1,), jnp.bfloat16)
    half = (vector.astype(jnp.float32) * 0.5).astype(jnp.bfloat16)
    return jnp.concatenate([unit, half, prod], axis=-1)


CHUNK = 128
LEAD = 128


def local_attention_kernel(flag_ref, q_ref, kt_ref, vx_ref, intra_ref, win_ref, *, span_rows, block_rows):
    first_span = flag_ref[0] == 1
    for i in range(span_rows // CHUNK):
        r0 = i * CHUNK
        q_c = q_ref[0, r0 : r0 + CHUNK, :]
        bs = (r0 // block_rows) * block_rows
        width = r0 + CHUNK - bs
        k_i = kt_ref[0, :, LEAD + bs : LEAD + r0 + CHUNK]
        v_i = vx_ref[0, LEAD + bs : LEAD + r0 + CHUNK, :]
        scores = jnp.dot(q_c, k_i, preferred_element_type=jnp.float32) * 0.25
        row = lax.broadcasted_iota(jnp.int32, (CHUNK, width), 0)
        col = lax.broadcasted_iota(jnp.int32, (CHUNK, width), 1)
        kernel = jnp.where(
            col <= row + (r0 - bs), 1.0 + scores + 0.5 * scores * scores, 0.0
        ).astype(jnp.bfloat16)
        intra_ref[r0 : r0 + CHUNK, :] = jnp.dot(kernel, v_i, preferred_element_type=jnp.float32)

        k_w = kt_ref[0, :, r0 : r0 + CHUNK + LEAD]
        v_w = vx_ref[0, r0 : r0 + CHUNK + LEAD, :]
        ws = jnp.dot(q_c, k_w, preferred_element_type=jnp.float32) * 0.25
        wrow = lax.broadcasted_iota(jnp.int32, (CHUNK, CHUNK + LEAD), 0)
        wcol = lax.broadcasted_iota(jnp.int32, (CHUNK, CHUNK + LEAD), 1)
        valid = (wcol > wrow + LEAD - WINDOW) & (wcol <= wrow + LEAD)
        if i == 0:
            valid = valid & ((wcol >= LEAD) | jnp.logical_not(first_span))
        masked = jnp.where(valid, ws, -jnp.inf)
        highest = jnp.max(masked, axis=1, keepdims=True)
        expo = jnp.where(valid, jnp.exp(ws - highest), 0.0)
        weights = (expo / jnp.sum(expo, axis=1, keepdims=True)).astype(jnp.bfloat16)
        win_ref[r0 : r0 + CHUNK, :] = jnp.dot(weights, v_w, preferred_element_type=jnp.float32)


def local_attention(flag, q_hm, kt_hm, vx, block_rows):
    heads_here, span_rows, _ = q_hm.shape
    ext = kt_hm.shape[2]
    body = lambda *refs: local_attention_kernel(*refs, span_rows=span_rows, block_rows=block_rows)
    out = jax.ShapeDtypeStruct((span_rows, heads_here * VD), jnp.float32)
    return pl.pallas_call(
        body,
        grid_spec=pltpu.PrefetchScalarGridSpec(
            num_scalar_prefetch=1,
            grid=(heads_here,),
            in_specs=[
                pl.BlockSpec((1, span_rows, KD), lambda h, f: (h, 0, 0)),
                pl.BlockSpec((1, KD, ext), lambda h, f: (h, 0, 0)),
                pl.BlockSpec((1, ext, VD), lambda h, f: (h, 0, 0)),
            ],
            out_specs=[
                pl.BlockSpec((span_rows, VD), lambda h, f: (0, h)),
                pl.BlockSpec((span_rows, VD), lambda h, f: (0, h)),
            ],
        ),
        out_shape=(out, out),
    )(flag, q_hm, kt_hm, vx)


def mix_kernel(intra_ref, inter_ref, win_ref, gain_ref, out_ref):
    for j in range(inter_ref.shape[0]):
        cols = slice(j * VD, (j + 1) * VD)
        linear = intra_ref[:, cols] + inter_ref[j]
        scale = lax.rsqrt(jnp.mean(linear * linear, axis=1, keepdims=True) + epsilon)
        out_ref[:, cols] = (linear * scale * gain_ref[:, cols] + win_ref[:, cols]).astype(
            jnp.bfloat16
        )


def mix(intra, inter_hm, window, gain):
    heads_here, span_rows, _ = inter_hm.shape
    step = 4 if heads_here % 4 == 0 else (2 if heads_here % 2 == 0 else 1)
    tile = pl.BlockSpec((span_rows, step * VD), lambda h: (0, h))
    return pl.pallas_call(
        mix_kernel,
        grid=(heads_here // step,),
        in_specs=[
            tile,
            pl.BlockSpec((step, span_rows, VD), lambda h: (h, 0, 0)),
            tile,
            pl.BlockSpec((1, step * VD), lambda h: (0, h)),
        ],
        out_specs=tile,
        out_shape=jax.ShapeDtypeStruct((span_rows, heads_here * VD), jnp.bfloat16),
    )(intra, inter_hm, window, gain.reshape(1, heads_here * VD))


def per_device(queries, keys, values, gain):
    local_tokens = queries.shape[0]

    def to_heads(tok, width):
        tok = jnp.transpose(tok.reshape(local_tokens, HEADS, width), (1, 0, 2))
        return lax.all_to_all(tok, "head", split_axis=0, concat_axis=1, tiled=True)

    value_hm = to_heads(values, VD)
    key_hm = to_heads(keys, KD)
    heads_here, span_rows, _ = key_hm.shape
    block_rows = min(512, span_rows)
    block_count = span_rows // block_rows
    first_span = lax.axis_index("ctx") == 0

    tails = shifted(
        jnp.concatenate([key_hm, value_hm], axis=2)[:, span_rows - WINDOW :], "ctx", 1
    )

    key_feat = unique_features(key_hm.reshape(heads_here, block_count, block_rows, KD), False)
    block_states = jnp.einsum(
        "hnrf,hnrv->hnfv",
        key_feat,
        value_hm.reshape(heads_here, block_count, block_rows, VD),
        preferred_element_type=jnp.float32,
    )
    span_state = jnp.sum(block_states, axis=1)
    peers = lax.axis_size("ctx")
    running = span_state
    entering = None
    first_round = span_state
    shift = 1
    while shift < peers:
        received = shifted(running, "ctx", shift)
        entering = received if entering is None else entering + received
        if shift == 1:
            first_round = received
        shift *= 2
        if shift < peers:
            running = running + received
    if entering is None:
        entering = jnp.zeros_like(span_state)
    queries, span_state = lax.optimization_barrier((queries, span_state))
    query_hm = to_heads(queries, KD)
    query_hm, first_round = lax.optimization_barrier((query_hm, first_round))
    before = jnp.concatenate(
        [jnp.zeros_like(block_states[:, :1]), jnp.cumsum(block_states[:, :-1], axis=1)], axis=1
    )
    states = (before + entering[:, None]).astype(jnp.bfloat16)

    query_feat = unique_features(query_hm.reshape(heads_here, block_count, block_rows, KD), True)
    inter = jnp.einsum(
        "hnrf,hnfv->hnrv",
        query_feat,
        states,
        preferred_element_type=jnp.float32,
    ).reshape(heads_here, span_rows, VD)

    lead = jnp.zeros((heads_here, LEAD - WINDOW, KD + VD), jnp.bfloat16)
    key_ext = jnp.concatenate([lead[:, :, :KD], tails[:, :, :KD], key_hm], axis=1)
    value_ext = jnp.concatenate([lead[:, :, KD:], tails[:, :, KD:], value_hm], axis=1)
    flag = first_span.astype(jnp.int32).reshape(1)
    intra, window = local_attention(
        flag, query_hm, jnp.transpose(key_ext, (0, 2, 1)), value_ext, block_rows
    )
    mixed = mix(intra, inter, window, gain)
    tokens_back = lax.all_to_all(mixed, "head", split_axis=0, concat_axis=1, tiled=True)
    return tokens_back


def solution(mesh):
    placed = (
        P(("groups", "ctx", "head"), None),
        P(("groups", "ctx", "head"), None),
        P(("groups", "ctx", "head"), None),
        P("head"),
    )
    return jax.shard_map(
        per_device,
        mesh=mesh,
        in_specs=placed,
        out_specs=P(("groups", "ctx", "head"), None),
        check_vma=False,
    )
```

```python
import math

import jax
import numpy as np
import jax.numpy as jnp
from jax import lax
from jax.experimental import pallas as pl
from jax.experimental.pallas import tpu as pltpu
from jax.sharding import PartitionSpec as P

HEADS = 32
KD = 16
VD = 128
WINDOW = 64


outer_scale = 1.0 / (4.0 * math.sqrt(2.0))
epsilon = 1e-06


def shifted(shard, axis, by):
    peers = lax.axis_size(axis)
    pairs = [(i, i + by) for i in range(peers) if 0 <= i + by < peers]
    return lax.ppermute(shard, axis, pairs)


def unique_features(vector, doubled):
    rows, cols = np.triu_indices(KD)
    pick_rows = jnp.asarray(np.eye(KD)[:, rows], jnp.bfloat16)
    pick_cols = jnp.asarray(np.eye(KD)[:, cols], jnp.bfloat16)
    first = jnp.einsum("...d,df->...f", vector, pick_rows, preferred_element_type=jnp.float32)
    second = jnp.einsum("...d,df->...f", vector, pick_cols, preferred_element_type=jnp.float32)
    prod = ((first * second) * outer_scale).astype(jnp.bfloat16)
    if doubled:
        prod = prod * jnp.asarray(np.where(rows == cols, 1.0, 2.0), jnp.bfloat16)
    lead = vector.shape[:-1]
    unit = jnp.ones(lead + (1,), jnp.bfloat16)
    half = (vector.astype(jnp.float32) * 0.5).astype(jnp.bfloat16)
    return jnp.concatenate([unit, half, prod], axis=-1)


CHUNK = 128
LEAD = 128


def local_attention_kernel(flag_ref, q_ref, kt_ref, vx_ref, intra_ref, win_ref, *, span_rows, block_rows):
    first_span = flag_ref[0] == 1
    for j in range(q_ref.shape[0]):
        one_head(j, first_span, q_ref, kt_ref, vx_ref, intra_ref, win_ref, span_rows, block_rows)


def one_head(j, first_span, q_ref, kt_ref, vx_ref, intra_ref, win_ref, span_rows, block_rows):
    cols = slice(j * VD, (j + 1) * VD)
    for i in range(span_rows // CHUNK):
        r0 = i * CHUNK
        q_c = q_ref[j, r0 : r0 + CHUNK, :]
        bs = (r0 // block_rows) * block_rows
        width = r0 + CHUNK - bs
        k_i = kt_ref[j, :, LEAD + bs : LEAD + r0 + CHUNK]
        v_i = vx_ref[j, LEAD + bs : LEAD + r0 + CHUNK, :]
        scores = jnp.dot(q_c, k_i, preferred_element_type=jnp.float32) * 0.25
        row = lax.broadcasted_iota(jnp.int32, (CHUNK, width), 0)
        col = lax.broadcasted_iota(jnp.int32, (CHUNK, width), 1)
        kernel = jnp.where(
            col <= row + (r0 - bs), 1.0 + scores + 0.5 * scores * scores, 0.0
        ).astype(jnp.bfloat16)
        intra_ref[r0 : r0 + CHUNK, cols] = jnp.dot(kernel, v_i, preferred_element_type=jnp.float32)

        k_w = kt_ref[j, :, r0 : r0 + CHUNK + LEAD]
        v_w = vx_ref[j, r0 : r0 + CHUNK + LEAD, :]
        ws = jnp.dot(q_c, k_w, preferred_element_type=jnp.float32) * 0.25
        wrow = lax.broadcasted_iota(jnp.int32, (CHUNK, CHUNK + LEAD), 0)
        wcol = lax.broadcasted_iota(jnp.int32, (CHUNK, CHUNK + LEAD), 1)
        valid = (wcol > wrow + LEAD - WINDOW) & (wcol <= wrow + LEAD)
        if i == 0:
            valid = valid & ((wcol >= LEAD) | jnp.logical_not(first_span))
        masked = jnp.where(valid, ws, -jnp.inf)
        highest = jnp.max(masked, axis=1, keepdims=True)
        expo = jnp.where(valid, jnp.exp(ws - highest), 0.0)
        weights = (expo / jnp.sum(expo, axis=1, keepdims=True)).astype(jnp.bfloat16)
        win_ref[r0 : r0 + CHUNK, cols] = jnp.dot(weights, v_w, preferred_element_type=jnp.float32)


def local_attention(flag, q_hm, kt_hm, vx, block_rows):
    heads_here, span_rows, _ = q_hm.shape
    ext = kt_hm.shape[2]
    step = 2 if heads_here % 2 == 0 else 1
    body = lambda *refs: local_attention_kernel(*refs, span_rows=span_rows, block_rows=block_rows)
    out = jax.ShapeDtypeStruct((span_rows, heads_here * VD), jnp.float32)
    return pl.pallas_call(
        body,
        grid_spec=pltpu.PrefetchScalarGridSpec(
            num_scalar_prefetch=1,
            grid=(heads_here // step,),
            in_specs=[
                pl.BlockSpec((step, span_rows, KD), lambda h, f: (h, 0, 0)),
                pl.BlockSpec((step, KD, ext), lambda h, f: (h, 0, 0)),
                pl.BlockSpec((step, ext, VD), lambda h, f: (h, 0, 0)),
            ],
            out_specs=[
                pl.BlockSpec((span_rows, step * VD), lambda h, f: (0, h)),
                pl.BlockSpec((span_rows, step * VD), lambda h, f: (0, h)),
            ],
        ),
        out_shape=(out, out),
    )(flag, q_hm, kt_hm, vx)


def mix_kernel(intra_ref, inter_ref, win_ref, gain_ref, out_ref):
    for j in range(inter_ref.shape[0]):
        cols = slice(j * VD, (j + 1) * VD)
        linear = intra_ref[:, cols] + inter_ref[j]
        scale = lax.rsqrt(jnp.mean(linear * linear, axis=1, keepdims=True) + epsilon)
        out_ref[:, cols] = (linear * scale * gain_ref[:, cols] + win_ref[:, cols]).astype(
            jnp.bfloat16
        )


def mix(intra, inter_hm, window, gain):
    heads_here, span_rows, _ = inter_hm.shape
    step = 4 if heads_here % 4 == 0 else (2 if heads_here % 2 == 0 else 1)
    tile = pl.BlockSpec((span_rows, step * VD), lambda h: (0, h))
    return pl.pallas_call(
        mix_kernel,
        grid=(heads_here // step,),
        in_specs=[
            tile,
            pl.BlockSpec((step, span_rows, VD), lambda h: (h, 0, 0)),
            tile,
            pl.BlockSpec((1, step * VD), lambda h: (0, h)),
        ],
        out_specs=tile,
        out_shape=jax.ShapeDtypeStruct((span_rows, heads_here * VD), jnp.bfloat16),
    )(intra, inter_hm, window, gain.reshape(1, heads_here * VD))


def per_device(queries, keys, values, gain):
    local_tokens = queries.shape[0]

    def to_heads(tok, width):
        tok = jnp.transpose(tok.reshape(local_tokens, HEADS, width), (1, 0, 2))
        return lax.all_to_all(tok, "head", split_axis=0, concat_axis=1, tiled=True)

    value_hm = to_heads(values, VD)
    key_hm = to_heads(keys, KD)
    heads_here, span_rows, _ = key_hm.shape
    block_rows = min(512, span_rows)
    block_count = span_rows // block_rows
    first_span = lax.axis_index("ctx") == 0

    tails = shifted(
        jnp.concatenate([key_hm, value_hm], axis=2)[:, span_rows - WINDOW :], "ctx", 1
    )

    key_feat = unique_features(key_hm.reshape(heads_here, block_count, block_rows, KD), False)
    block_states = jnp.einsum(
        "hnrf,hnrv->hnfv",
        key_feat,
        value_hm.reshape(heads_here, block_count, block_rows, VD),
        preferred_element_type=jnp.float32,
    )
    span_state = jnp.sum(block_states, axis=1)
    peers = lax.axis_size("ctx")
    running = span_state
    entering = None
    first_round = span_state
    shift = 1
    while shift < peers:
        received = shifted(running, "ctx", shift)
        entering = received if entering is None else entering + received
        if shift == 1:
            first_round = received
        shift *= 2
        if shift < peers:
            running = running + received
    if entering is None:
        entering = jnp.zeros_like(span_state)
    queries, span_state = lax.optimization_barrier((queries, span_state))
    query_hm = to_heads(queries, KD)
    query_hm, first_round = lax.optimization_barrier((query_hm, first_round))
    before = jnp.concatenate(
        [jnp.zeros_like(block_states[:, :1]), jnp.cumsum(block_states[:, :-1], axis=1)], axis=1
    )
    states = (before + entering[:, None]).astype(jnp.bfloat16)

    query_feat = unique_features(query_hm.reshape(heads_here, block_count, block_rows, KD), True)
    inter = jnp.einsum(
        "hnrf,hnfv->hnrv",
        query_feat,
        states,
        preferred_element_type=jnp.float32,
    ).reshape(heads_here, span_rows, VD)

    lead = jnp.zeros((heads_here, LEAD - WINDOW, KD + VD), jnp.bfloat16)
    key_ext = jnp.concatenate([lead[:, :, :KD], tails[:, :, :KD], key_hm], axis=1)
    value_ext = jnp.concatenate([lead[:, :, KD:], tails[:, :, KD:], value_hm], axis=1)
    flag = first_span.astype(jnp.int32).reshape(1)
    intra, window = local_attention(
        flag, query_hm, jnp.transpose(key_ext, (0, 2, 1)), value_ext, block_rows
    )
    mixed = mix(intra, inter, window, gain)
    tokens_back = lax.all_to_all(mixed, "head", split_axis=0, concat_axis=1, tiled=True)
    return tokens_back


def solution(mesh):
    placed = (
        P(("groups", "ctx", "head"), None),
        P(("groups", "ctx", "head"), None),
        P(("groups", "ctx", "head"), None),
        P("head"),
    )
    return jax.shard_map(
        per_device,
        mesh=mesh,
        in_specs=placed,
        out_specs=P(("groups", "ctx", "head"), None),
        check_vma=False,
    )
```

```python
import math

import jax
import numpy as np
import jax.numpy as jnp
from jax import lax
from jax.experimental import pallas as pl
from jax.experimental.pallas import tpu as pltpu
from jax.sharding import PartitionSpec as P

HEADS = 32
KD = 16
VD = 128
WINDOW = 64


outer_scale = 1.0 / (4.0 * math.sqrt(2.0))
epsilon = 1e-06


def shifted(shard, axis, by):
    peers = lax.axis_size(axis)
    pairs = [(i, i + by) for i in range(peers) if 0 <= i + by < peers]
    return lax.ppermute(shard, axis, pairs)


def unique_features(vector, doubled):
    rows, cols = np.triu_indices(KD)
    pick_rows = jnp.asarray(np.eye(KD)[:, rows], jnp.bfloat16)
    pick_cols = jnp.asarray(np.eye(KD)[:, cols], jnp.bfloat16)
    first = jnp.einsum("...d,df->...f", vector, pick_rows, preferred_element_type=jnp.float32)
    second = jnp.einsum("...d,df->...f", vector, pick_cols, preferred_element_type=jnp.float32)
    prod = ((first * second) * outer_scale).astype(jnp.bfloat16)
    if doubled:
        prod = prod * jnp.asarray(np.where(rows == cols, 1.0, 2.0), jnp.bfloat16)
    lead = vector.shape[:-1]
    unit = jnp.ones(lead + (1,), jnp.bfloat16)
    half = (vector.astype(jnp.float32) * 0.5).astype(jnp.bfloat16)
    return jnp.concatenate([unit, half, prod], axis=-1)


CHUNK = 128
LEAD = 128


def local_attention_kernel(flag_ref, q_ref, kt_ref, vx_ref, intra_ref, win_ref, *, span_rows, block_rows):
    first_span = flag_ref[0] == 1
    for j in range(q_ref.shape[0]):
        one_head(j, first_span, q_ref, kt_ref, vx_ref, intra_ref, win_ref, span_rows, block_rows)


def one_head(j, first_span, q_ref, kt_ref, vx_ref, intra_ref, win_ref, span_rows, block_rows):
    cols = slice(j * VD, (j + 1) * VD)
    for i in range(span_rows // CHUNK):
        r0 = i * CHUNK
        q_c = q_ref[j, r0 : r0 + CHUNK, :]
        bs = (r0 // block_rows) * block_rows
        width = r0 + CHUNK - bs
        k_i = kt_ref[j, :, LEAD + bs : LEAD + r0 + CHUNK]
        v_i = vx_ref[j, LEAD + bs : LEAD + r0 + CHUNK, :]
        scores = jnp.dot(q_c, k_i, preferred_element_type=jnp.float32) * 0.25
        row = lax.broadcasted_iota(jnp.int32, (CHUNK, width), 0)
        col = lax.broadcasted_iota(jnp.int32, (CHUNK, width), 1)
        kernel = jnp.where(
            col <= row + (r0 - bs), 1.0 + scores + 0.5 * scores * scores, 0.0
        ).astype(jnp.bfloat16)
        intra_ref[r0 : r0 + CHUNK, cols] = jnp.dot(kernel, v_i, preferred_element_type=jnp.float32)

        k_w = kt_ref[j, :, r0 : r0 + CHUNK + LEAD]
        v_w = vx_ref[j, r0 : r0 + CHUNK + LEAD, :]
        ws = jnp.dot(q_c, k_w, preferred_element_type=jnp.float32) * 0.25
        wrow = lax.broadcasted_iota(jnp.int32, (CHUNK, CHUNK + LEAD), 0)
        wcol = lax.broadcasted_iota(jnp.int32, (CHUNK, CHUNK + LEAD), 1)
        valid = (wcol > wrow + LEAD - WINDOW) & (wcol <= wrow + LEAD)
        if i == 0:
            valid = valid & ((wcol >= LEAD) | jnp.logical_not(first_span))
        masked = jnp.where(valid, ws, -jnp.inf)
        highest = jnp.max(masked, axis=1, keepdims=True)
        expo = jnp.where(valid, jnp.exp(ws - highest), 0.0)
        weights = (expo / jnp.sum(expo, axis=1, keepdims=True)).astype(jnp.bfloat16)
        win_ref[r0 : r0 + CHUNK, cols] = jnp.dot(weights, v_w, preferred_element_type=jnp.float32)


def local_attention(flag, q_hm, kt_hm, vx, block_rows):
    heads_here, span_rows, _ = q_hm.shape
    ext = kt_hm.shape[2]
    step = 4 if heads_here % 4 == 0 else (2 if heads_here % 2 == 0 else 1)
    body = lambda *refs: local_attention_kernel(*refs, span_rows=span_rows, block_rows=block_rows)
    out = jax.ShapeDtypeStruct((span_rows, heads_here * VD), jnp.float32)
    return pl.pallas_call(
        body,
        grid_spec=pltpu.PrefetchScalarGridSpec(
            num_scalar_prefetch=1,
            grid=(heads_here // step,),
            in_specs=[
                pl.BlockSpec((step, span_rows, KD), lambda h, f: (h, 0, 0)),
                pl.BlockSpec((step, KD, ext), lambda h, f: (h, 0, 0)),
                pl.BlockSpec((step, ext, VD), lambda h, f: (h, 0, 0)),
            ],
            out_specs=[
                pl.BlockSpec((span_rows, step * VD), lambda h, f: (0, h)),
                pl.BlockSpec((span_rows, step * VD), lambda h, f: (0, h)),
            ],
        ),
        out_shape=(out, out),
    )(flag, q_hm, kt_hm, vx)


def mix_kernel(intra_ref, inter_ref, win_ref, gain_ref, out_ref):
    for j in range(inter_ref.shape[0]):
        cols = slice(j * VD, (j + 1) * VD)
        linear = intra_ref[:, cols] + inter_ref[j]
        scale = lax.rsqrt(jnp.mean(linear * linear, axis=1, keepdims=True) + epsilon)
        out_ref[:, cols] = (linear * scale * gain_ref[:, cols] + win_ref[:, cols]).astype(
            jnp.bfloat16
        )


def mix(intra, inter_hm, window, gain):
    heads_here, span_rows, _ = inter_hm.shape
    step = 4 if heads_here % 4 == 0 else (2 if heads_here % 2 == 0 else 1)
    tile = pl.BlockSpec((span_rows, step * VD), lambda h: (0, h))
    return pl.pallas_call(
        mix_kernel,
        grid=(heads_here // step,),
        in_specs=[
            tile,
            pl.BlockSpec((step, span_rows, VD), lambda h: (h, 0, 0)),
            tile,
            pl.BlockSpec((1, step * VD), lambda h: (0, h)),
        ],
        out_specs=tile,
        out_shape=jax.ShapeDtypeStruct((span_rows, heads_here * VD), jnp.bfloat16),
    )(intra, inter_hm, window, gain.reshape(1, heads_here * VD))


def per_device(queries, keys, values, gain):
    local_tokens = queries.shape[0]

    def to_heads(tok, width):
        tok = jnp.transpose(tok.reshape(local_tokens, HEADS, width), (1, 0, 2))
        return lax.all_to_all(tok, "head", split_axis=0, concat_axis=1, tiled=True)

    value_hm = to_heads(values, VD)
    key_hm = to_heads(keys, KD)
    heads_here, span_rows, _ = key_hm.shape
    block_rows = min(512, span_rows)
    block_count = span_rows // block_rows
    first_span = lax.axis_index("ctx") == 0

    tails = shifted(
        jnp.concatenate([key_hm, value_hm], axis=2)[:, span_rows - WINDOW :], "ctx", 1
    )

    key_feat = unique_features(key_hm.reshape(heads_here, block_count, block_rows, KD), False)
    block_states = jnp.einsum(
        "hnrf,hnrv->hnfv",
        key_feat,
        value_hm.reshape(heads_here, block_count, block_rows, VD),
        preferred_element_type=jnp.float32,
    )
    span_state = jnp.sum(block_states, axis=1)
    peers = lax.axis_size("ctx")
    running = span_state
    entering = None
    first_round = span_state
    shift = 1
    while shift < peers:
        received = shifted(running, "ctx", shift)
        entering = received if entering is None else entering + received
        if shift == 1:
            first_round = received
        shift *= 2
        if shift < peers:
            running = running + received
    if entering is None:
        entering = jnp.zeros_like(span_state)
    queries, span_state = lax.optimization_barrier((queries, span_state))
    query_hm = to_heads(queries, KD)
    query_hm, first_round = lax.optimization_barrier((query_hm, first_round))
    before = jnp.concatenate(
        [jnp.zeros_like(block_states[:, :1]), jnp.cumsum(block_states[:, :-1], axis=1)], axis=1
    )
    states = (before + entering[:, None]).astype(jnp.bfloat16)

    query_feat = unique_features(query_hm.reshape(heads_here, block_count, block_rows, KD), True)
    inter = jnp.einsum(
        "hnrf,hnfv->hnrv",
        query_feat,
        states,
        preferred_element_type=jnp.float32,
    ).reshape(heads_here, span_rows, VD)

    lead = jnp.zeros((heads_here, LEAD - WINDOW, KD + VD), jnp.bfloat16)
    key_ext = jnp.concatenate([lead[:, :, :KD], tails[:, :, :KD], key_hm], axis=1)
    value_ext = jnp.concatenate([lead[:, :, KD:], tails[:, :, KD:], value_hm], axis=1)
    flag = first_span.astype(jnp.int32).reshape(1)
    intra, window = local_attention(
        flag, query_hm, jnp.transpose(key_ext, (0, 2, 1)), value_ext, block_rows
    )
    mixed = mix(intra, inter, window, gain)
    tokens_back = lax.all_to_all(mixed, "head", split_axis=0, concat_axis=1, tiled=True)
    return tokens_back


def solution(mesh):
    placed = (
        P(("groups", "ctx", "head"), None),
        P(("groups", "ctx", "head"), None),
        P(("groups", "ctx", "head"), None),
        P("head"),
    )
    return jax.shard_map(
        per_device,
        mesh=mesh,
        in_specs=placed,
        out_specs=P(("groups", "ctx", "head"), None),
        check_vma=False,
    )
```

```python
import math

import jax
import numpy as np
import jax.numpy as jnp
from jax import lax
from jax.experimental import pallas as pl
from jax.experimental.pallas import tpu as pltpu
from jax.sharding import PartitionSpec as P

HEADS = 32
KD = 16
VD = 128
WINDOW = 64


outer_scale = 1.0 / (4.0 * math.sqrt(2.0))
epsilon = 1e-06


def shifted(shard, axis, by):
    peers = lax.axis_size(axis)
    pairs = [(i, i + by) for i in range(peers) if 0 <= i + by < peers]
    return lax.ppermute(shard, axis, pairs)


def unique_features(vector, doubled):
    rows, cols = np.triu_indices(KD)
    pick_rows = jnp.asarray(np.eye(KD)[:, rows], jnp.bfloat16)
    pick_cols = jnp.asarray(np.eye(KD)[:, cols], jnp.bfloat16)
    first = jnp.einsum("...d,df->...f", vector, pick_rows, preferred_element_type=jnp.float32)
    second = jnp.einsum("...d,df->...f", vector, pick_cols, preferred_element_type=jnp.float32)
    prod = ((first * second) * outer_scale).astype(jnp.bfloat16)
    if doubled:
        prod = prod * jnp.asarray(np.where(rows == cols, 1.0, 2.0), jnp.bfloat16)
    lead = vector.shape[:-1]
    unit = jnp.ones(lead + (1,), jnp.bfloat16)
    half = (vector.astype(jnp.float32) * 0.5).astype(jnp.bfloat16)
    return jnp.concatenate([unit, half, prod], axis=-1)


CHUNK = 128
LEAD = 128


def local_attention_kernel(flag_ref, q_ref, kt_ref, vx_ref, intra_ref, win_ref, *, span_rows, block_rows):
    first_span = flag_ref[0] == 1
    for j in range(q_ref.shape[0]):
        one_head(j, first_span, q_ref, kt_ref, vx_ref, intra_ref, win_ref, span_rows, block_rows)


def one_head(j, first_span, q_ref, kt_ref, vx_ref, intra_ref, win_ref, span_rows, block_rows):
    cols = slice(j * VD, (j + 1) * VD)
    for i in range(span_rows // CHUNK):
        r0 = i * CHUNK
        q_c = q_ref[j, r0 : r0 + CHUNK, :]
        bs = (r0 // block_rows) * block_rows
        width = r0 + CHUNK - bs
        k_i = kt_ref[j, :, LEAD + bs : LEAD + r0 + CHUNK]
        v_i = vx_ref[j, LEAD + bs : LEAD + r0 + CHUNK, :]
        scores = jnp.dot(q_c, k_i, preferred_element_type=jnp.float32) * 0.25
        row = lax.broadcasted_iota(jnp.int32, (CHUNK, width), 0)
        col = lax.broadcasted_iota(jnp.int32, (CHUNK, width), 1)
        kernel = jnp.where(
            col <= row + (r0 - bs), 1.0 + scores + 0.5 * scores * scores, 0.0
        ).astype(jnp.bfloat16)
        intra_ref[r0 : r0 + CHUNK, cols] = jnp.dot(kernel, v_i, preferred_element_type=jnp.float32)

        k_w = kt_ref[j, :, r0 : r0 + CHUNK + LEAD]
        v_w = vx_ref[j, r0 : r0 + CHUNK + LEAD, :]
        ws = jnp.dot(q_c, k_w, preferred_element_type=jnp.float32) * 0.25
        wrow = lax.broadcasted_iota(jnp.int32, (CHUNK, CHUNK + LEAD), 0)
        wcol = lax.broadcasted_iota(jnp.int32, (CHUNK, CHUNK + LEAD), 1)
        valid = (wcol > wrow + LEAD - WINDOW) & (wcol <= wrow + LEAD)
        if i == 0:
            valid = valid & ((wcol >= LEAD) | jnp.logical_not(first_span))
        masked = jnp.where(valid, ws, -jnp.inf)
        highest = jnp.max(masked, axis=1, keepdims=True)
        expo = jnp.where(valid, jnp.exp(ws - highest), 0.0)
        weights = (expo / jnp.sum(expo, axis=1, keepdims=True)).astype(jnp.bfloat16)
        win_ref[r0 : r0 + CHUNK, cols] = jnp.dot(weights, v_w, preferred_element_type=jnp.float32)


def local_attention(flag, q_hm, kt_hm, vx, block_rows):
    heads_here, span_rows, _ = q_hm.shape
    ext = kt_hm.shape[2]
    step = 4 if heads_here % 4 == 0 else (2 if heads_here % 2 == 0 else 1)
    body = lambda *refs: local_attention_kernel(*refs, span_rows=span_rows, block_rows=block_rows)
    out = jax.ShapeDtypeStruct((span_rows, heads_here * VD), jnp.float32)
    return pl.pallas_call(
        body,
        grid_spec=pltpu.PrefetchScalarGridSpec(
            num_scalar_prefetch=1,
            grid=(heads_here // step,),
            in_specs=[
                pl.BlockSpec((step, span_rows, KD), lambda h, f: (h, 0, 0)),
                pl.BlockSpec((step, KD, ext), lambda h, f: (h, 0, 0)),
                pl.BlockSpec((step, ext, VD), lambda h, f: (h, 0, 0)),
            ],
            out_specs=[
                pl.BlockSpec((span_rows, step * VD), lambda h, f: (0, h)),
                pl.BlockSpec((span_rows, step * VD), lambda h, f: (0, h)),
            ],
        ),
        out_shape=(out, out),
    )(flag, q_hm, kt_hm, vx)


def mix_kernel(intra_ref, inter_ref, win_ref, gain_ref, out_ref):
    for j in range(inter_ref.shape[0]):
        cols = slice(j * VD, (j + 1) * VD)
        linear = intra_ref[:, cols] + inter_ref[j]
        scale = lax.rsqrt(jnp.mean(linear * linear, axis=1, keepdims=True) + epsilon)
        out_ref[:, cols] = (linear * scale * gain_ref[:, cols] + win_ref[:, cols]).astype(
            jnp.bfloat16
        )


def mix(intra, inter_hm, window, gain):
    heads_here, span_rows, _ = inter_hm.shape
    step = 4 if heads_here % 4 == 0 else (2 if heads_here % 2 == 0 else 1)
    tile = pl.BlockSpec((span_rows, step * VD), lambda h: (0, h))
    return pl.pallas_call(
        mix_kernel,
        grid=(heads_here // step,),
        in_specs=[
            tile,
            pl.BlockSpec((step, span_rows, VD), lambda h: (h, 0, 0)),
            tile,
            pl.BlockSpec((1, step * VD), lambda h: (0, h)),
        ],
        out_specs=tile,
        out_shape=jax.ShapeDtypeStruct((span_rows, heads_here * VD), jnp.bfloat16),
    )(intra, inter_hm, window, gain.reshape(1, heads_here * VD))


def per_device(queries, keys, values, gain):
    local_tokens = queries.shape[0]

    def to_heads(tok, width):
        tok = jnp.transpose(tok.reshape(local_tokens, HEADS, width), (1, 0, 2))
        return lax.all_to_all(tok, "head", split_axis=0, concat_axis=1, tiled=True)

    value_hm = to_heads(values, VD)
    key_hm = to_heads(keys, KD)
    heads_here, span_rows, _ = key_hm.shape
    block_rows = min(512, span_rows)
    block_count = span_rows // block_rows
    first_span = lax.axis_index("ctx") == 0

    tails = shifted(
        jnp.concatenate([key_hm, value_hm], axis=2)[:, span_rows - WINDOW :], "ctx", 1
    )

    key_feat = unique_features(key_hm.reshape(heads_here, block_count, block_rows, KD), False)
    block_states = jnp.einsum(
        "hnrf,hnrv->hnfv",
        key_feat,
        value_hm.reshape(heads_here, block_count, block_rows, VD),
        preferred_element_type=jnp.float32,
    )
    span_state = jnp.sum(block_states, axis=1)
    peers = lax.axis_size("ctx")
    running = span_state
    entering = None
    arrivals = []
    first_round = span_state
    shift = 1
    while shift < peers:
        received = shifted(running, "ctx", shift)
        entering = received if entering is None else entering + received
        arrivals.append(received)
        if shift == 1:
            first_round = received
        shift *= 2
        if shift < peers:
            running = running + received
    if entering is None:
        entering = jnp.zeros_like(span_state)
    queries, span_state = lax.optimization_barrier((queries, span_state))
    query_hm = to_heads(queries, KD)
    query_hm, first_round = lax.optimization_barrier((query_hm, first_round))
    before = jnp.concatenate(
        [jnp.zeros_like(block_states[:, :1]), jnp.cumsum(block_states[:, :-1], axis=1)], axis=1
    )
    for received in arrivals:
        before = before + received[:, None]
    states = before.astype(jnp.bfloat16)

    query_feat = unique_features(query_hm.reshape(heads_here, block_count, block_rows, KD), True)
    inter = jnp.einsum(
        "hnrf,hnfv->hnrv",
        query_feat,
        states,
        preferred_element_type=jnp.float32,
    ).reshape(heads_here, span_rows, VD)

    lead = jnp.zeros((heads_here, LEAD - WINDOW, KD + VD), jnp.bfloat16)
    key_ext = jnp.concatenate([lead[:, :, :KD], tails[:, :, :KD], key_hm], axis=1)
    value_ext = jnp.concatenate([lead[:, :, KD:], tails[:, :, KD:], value_hm], axis=1)
    flag = first_span.astype(jnp.int32).reshape(1)
    intra, window = local_attention(
        flag, query_hm, jnp.transpose(key_ext, (0, 2, 1)), value_ext, block_rows
    )
    mixed = mix(intra, inter, window, gain)
    tokens_back = lax.all_to_all(mixed, "head", split_axis=0, concat_axis=1, tiled=True)
    return tokens_back


def solution(mesh):
    placed = (
        P(("groups", "ctx", "head"), None),
        P(("groups", "ctx", "head"), None),
        P(("groups", "ctx", "head"), None),
        P("head"),
    )
    return jax.shard_map(
        per_device,
        mesh=mesh,
        in_specs=placed,
        out_specs=P(("groups", "ctx", "head"), None),
        check_vma=False,
    )
```

```python
import math

import jax
import numpy as np
import jax.numpy as jnp
from jax import lax
from jax.experimental import pallas as pl
from jax.experimental.pallas import tpu as pltpu
from jax.sharding import PartitionSpec as P

HEADS = 32
KD = 16
VD = 128
WINDOW = 64


outer_scale = 1.0 / (4.0 * math.sqrt(2.0))
epsilon = 1e-06


def shifted(shard, axis, by):
    peers = lax.axis_size(axis)
    pairs = [(i, i + by) for i in range(peers) if 0 <= i + by < peers]
    return lax.ppermute(shard, axis, pairs)


def unique_features(vector, doubled):
    rows, cols = np.triu_indices(KD)
    pick_rows = jnp.asarray(np.eye(KD)[:, rows], jnp.bfloat16)
    pick_cols = jnp.asarray(np.eye(KD)[:, cols], jnp.bfloat16)
    first = jnp.einsum("...d,df->...f", vector, pick_rows, preferred_element_type=jnp.float32)
    second = jnp.einsum("...d,df->...f", vector, pick_cols, preferred_element_type=jnp.float32)
    prod = ((first * second) * outer_scale).astype(jnp.bfloat16)
    if doubled:
        prod = prod * jnp.asarray(np.where(rows == cols, 1.0, 2.0), jnp.bfloat16)
    lead = vector.shape[:-1]
    unit = jnp.ones(lead + (1,), jnp.bfloat16)
    half = (vector.astype(jnp.float32) * 0.5).astype(jnp.bfloat16)
    return jnp.concatenate([unit, half, prod], axis=-1)


CHUNK = 128
LEAD = 128


def local_attention_kernel(flag_ref, q_ref, kt_ref, vx_ref, intra_ref, win_ref, *, span_rows, block_rows):
    first_span = flag_ref[0] == 1
    for j in range(q_ref.shape[0]):
        one_head(j, first_span, q_ref, kt_ref, vx_ref, intra_ref, win_ref, span_rows, block_rows)


def one_head(j, first_span, q_ref, kt_ref, vx_ref, intra_ref, win_ref, span_rows, block_rows):
    cols = slice(j * VD, (j + 1) * VD)
    for i in range(span_rows // CHUNK):
        r0 = i * CHUNK
        q_c = q_ref[j, r0 : r0 + CHUNK, :]
        bs = (r0 // block_rows) * block_rows
        width = r0 + CHUNK - bs
        k_i = kt_ref[j, :, LEAD + bs : LEAD + r0 + CHUNK]
        v_i = vx_ref[j, LEAD + bs : LEAD + r0 + CHUNK, :]
        scores = jnp.dot(q_c, k_i, preferred_element_type=jnp.float32) * 0.25
        row = lax.broadcasted_iota(jnp.int32, (CHUNK, width), 0)
        col = lax.broadcasted_iota(jnp.int32, (CHUNK, width), 1)
        kernel = jnp.where(
            col <= row + (r0 - bs), 1.0 + scores + 0.5 * scores * scores, 0.0
        ).astype(jnp.bfloat16)
        intra_ref[r0 : r0 + CHUNK, cols] = jnp.dot(kernel, v_i, preferred_element_type=jnp.float32)

        v_w = vx_ref[j, r0 : r0 + CHUNK + LEAD, :]
        if r0 - bs >= LEAD:
            ws = scores[:, r0 - bs - LEAD : r0 - bs + CHUNK]
        else:
            k_w = kt_ref[j, :, r0 : r0 + CHUNK + LEAD]
            ws = jnp.dot(q_c, k_w, preferred_element_type=jnp.float32) * 0.25
        wrow = lax.broadcasted_iota(jnp.int32, (CHUNK, CHUNK + LEAD), 0)
        wcol = lax.broadcasted_iota(jnp.int32, (CHUNK, CHUNK + LEAD), 1)
        valid = (wcol > wrow + LEAD - WINDOW) & (wcol <= wrow + LEAD)
        if i == 0:
            valid = valid & ((wcol >= LEAD) | jnp.logical_not(first_span))
        masked = jnp.where(valid, ws, -jnp.inf)
        highest = jnp.max(masked, axis=1, keepdims=True)
        expo = jnp.where(valid, jnp.exp(ws - highest), 0.0)
        weights = (expo / jnp.sum(expo, axis=1, keepdims=True)).astype(jnp.bfloat16)
        win_ref[r0 : r0 + CHUNK, cols] = jnp.dot(weights, v_w, preferred_element_type=jnp.float32)


def local_attention(flag, q_hm, kt_hm, vx, block_rows):
    heads_here, span_rows, _ = q_hm.shape
    ext = kt_hm.shape[2]
    step = 4 if heads_here % 4 == 0 else (2 if heads_here % 2 == 0 else 1)
    body = lambda *refs: local_attention_kernel(*refs, span_rows=span_rows, block_rows=block_rows)
    out = jax.ShapeDtypeStruct((span_rows, heads_here * VD), jnp.float32)
    return pl.pallas_call(
        body,
        grid_spec=pltpu.PrefetchScalarGridSpec(
            num_scalar_prefetch=1,
            grid=(heads_here // step,),
            in_specs=[
                pl.BlockSpec((step, span_rows, KD), lambda h, f: (h, 0, 0)),
                pl.BlockSpec((step, KD, ext), lambda h, f: (h, 0, 0)),
                pl.BlockSpec((step, ext, VD), lambda h, f: (h, 0, 0)),
            ],
            out_specs=[
                pl.BlockSpec((span_rows, step * VD), lambda h, f: (0, h)),
                pl.BlockSpec((span_rows, step * VD), lambda h, f: (0, h)),
            ],
        ),
        out_shape=(out, out),
    )(flag, q_hm, kt_hm, vx)


def mix_kernel(intra_ref, inter_ref, win_ref, gain_ref, out_ref):
    for j in range(inter_ref.shape[0]):
        cols = slice(j * VD, (j + 1) * VD)
        linear = intra_ref[:, cols] + inter_ref[j]
        scale = lax.rsqrt(jnp.mean(linear * linear, axis=1, keepdims=True) + epsilon)
        out_ref[:, cols] = (linear * scale * gain_ref[:, cols] + win_ref[:, cols]).astype(
            jnp.bfloat16
        )


def mix(intra, inter_hm, window, gain):
    heads_here, span_rows, _ = inter_hm.shape
    step = 4 if heads_here % 4 == 0 else (2 if heads_here % 2 == 0 else 1)
    tile = pl.BlockSpec((span_rows, step * VD), lambda h: (0, h))
    return pl.pallas_call(
        mix_kernel,
        grid=(heads_here // step,),
        in_specs=[
            tile,
            pl.BlockSpec((step, span_rows, VD), lambda h: (h, 0, 0)),
            tile,
            pl.BlockSpec((1, step * VD), lambda h: (0, h)),
        ],
        out_specs=tile,
        out_shape=jax.ShapeDtypeStruct((span_rows, heads_here * VD), jnp.bfloat16),
    )(intra, inter_hm, window, gain.reshape(1, heads_here * VD))


def per_device(queries, keys, values, gain):
    local_tokens = queries.shape[0]

    def to_heads(tok, width):
        tok = jnp.transpose(tok.reshape(local_tokens, HEADS, width), (1, 0, 2))
        return lax.all_to_all(tok, "head", split_axis=0, concat_axis=1, tiled=True)

    value_hm = to_heads(values, VD)
    key_hm = to_heads(keys, KD)
    heads_here, span_rows, _ = key_hm.shape
    block_rows = min(512, span_rows)
    block_count = span_rows // block_rows
    first_span = lax.axis_index("ctx") == 0

    tails = shifted(
        jnp.concatenate([key_hm, value_hm], axis=2)[:, span_rows - WINDOW :], "ctx", 1
    )

    key_feat = unique_features(key_hm.reshape(heads_here, block_count, block_rows, KD), False)
    block_states = jnp.einsum(
        "hnrf,hnrv->hnfv",
        key_feat,
        value_hm.reshape(heads_here, block_count, block_rows, VD),
        preferred_element_type=jnp.float32,
    )
    span_state = jnp.sum(block_states, axis=1)
    peers = lax.axis_size("ctx")
    running = span_state
    entering = None
    first_round = span_state
    shift = 1
    while shift < peers:
        received = shifted(running, "ctx", shift)
        entering = received if entering is None else entering + received
        if shift == 1:
            first_round = received
        shift *= 2
        if shift < peers:
            running = running + received
    if entering is None:
        entering = jnp.zeros_like(span_state)
    queries, span_state = lax.optimization_barrier((queries, span_state))
    query_hm = to_heads(queries, KD)
    query_hm, first_round = lax.optimization_barrier((query_hm, first_round))
    before = jnp.concatenate(
        [jnp.zeros_like(block_states[:, :1]), jnp.cumsum(block_states[:, :-1], axis=1)], axis=1
    )
    states = (before + entering[:, None]).astype(jnp.bfloat16)

    query_feat = unique_features(query_hm.reshape(heads_here, block_count, block_rows, KD), True)
    inter = jnp.einsum(
        "hnrf,hnfv->hnrv",
        query_feat,
        states,
        preferred_element_type=jnp.float32,
    ).reshape(heads_here, span_rows, VD)

    lead = jnp.zeros((heads_here, LEAD - WINDOW, KD + VD), jnp.bfloat16)
    key_ext = jnp.concatenate([lead[:, :, :KD], tails[:, :, :KD], key_hm], axis=1)
    value_ext = jnp.concatenate([lead[:, :, KD:], tails[:, :, KD:], value_hm], axis=1)
    flag = first_span.astype(jnp.int32).reshape(1)
    intra, window = local_attention(
        flag, query_hm, jnp.transpose(key_ext, (0, 2, 1)), value_ext, block_rows
    )
    mixed = mix(intra, inter, window, gain)
    tokens_back = lax.all_to_all(mixed, "head", split_axis=0, concat_axis=1, tiled=True)
    return tokens_back


def solution(mesh):
    placed = (
        P(("groups", "ctx", "head"), None),
        P(("groups", "ctx", "head"), None),
        P(("groups", "ctx", "head"), None),
        P("head"),
    )
    return jax.shard_map(
        per_device,
        mesh=mesh,
        in_specs=placed,
        out_specs=P(("groups", "ctx", "head"), None),
        check_vma=False,
    )
```

```python
import math

import jax
import numpy as np
import jax.numpy as jnp
from jax import lax
from jax.experimental import pallas as pl
from jax.experimental.pallas import tpu as pltpu
from jax.sharding import PartitionSpec as P

HEADS = 32
KD = 16
VD = 128
WINDOW = 64


outer_scale = 1.0 / (4.0 * math.sqrt(2.0))
epsilon = 1e-06


def shifted(shard, axis, by):
    peers = lax.axis_size(axis)
    pairs = [(i, i + by) for i in range(peers) if 0 <= i + by < peers]
    return lax.ppermute(shard, axis, pairs)


def unique_features(vector, doubled):
    rows, cols = np.triu_indices(KD)
    pick_rows = jnp.asarray(np.eye(KD)[:, rows], jnp.bfloat16)
    pick_cols = jnp.asarray(np.eye(KD)[:, cols], jnp.bfloat16)
    first = jnp.einsum("...d,df->...f", vector, pick_rows, preferred_element_type=jnp.float32)
    second = jnp.einsum("...d,df->...f", vector, pick_cols, preferred_element_type=jnp.float32)
    prod = ((first * second) * outer_scale).astype(jnp.bfloat16)
    if doubled:
        prod = prod * jnp.asarray(np.where(rows == cols, 1.0, 2.0), jnp.bfloat16)
    lead = vector.shape[:-1]
    unit = jnp.ones(lead + (1,), jnp.bfloat16)
    half = (vector.astype(jnp.float32) * 0.5).astype(jnp.bfloat16)
    return jnp.concatenate([unit, half, prod], axis=-1)


CHUNK = 128
LEAD = 128


def local_attention_kernel(flag_ref, q_ref, kt_ref, vx_ref, intra_ref, win_ref, *, span_rows, block_rows):
    first_span = flag_ref[0] == 1
    for j in range(q_ref.shape[0]):
        one_head(j, first_span, q_ref, kt_ref, vx_ref, intra_ref, win_ref, span_rows, block_rows)


def one_head(j, first_span, q_ref, kt_ref, vx_ref, intra_ref, win_ref, span_rows, block_rows):
    cols = slice(j * VD, (j + 1) * VD)
    for i in range(span_rows // CHUNK):
        r0 = i * CHUNK
        q_c = q_ref[j, r0 : r0 + CHUNK, :]
        bs = (r0 // block_rows) * block_rows
        width = r0 + CHUNK - bs
        k_i = kt_ref[j, :, LEAD + bs : LEAD + r0 + CHUNK]
        v_i = vx_ref[j, LEAD + bs : LEAD + r0 + CHUNK, :]
        scores = jnp.dot(q_c, k_i, preferred_element_type=jnp.float32) * 0.25
        row = lax.broadcasted_iota(jnp.int32, (CHUNK, width), 0)
        col = lax.broadcasted_iota(jnp.int32, (CHUNK, width), 1)
        kernel = jnp.where(
            col <= row + (r0 - bs), 1.0 + scores + 0.5 * scores * scores, 0.0
        ).astype(jnp.bfloat16)
        intra_ref[r0 : r0 + CHUNK, cols] = jnp.dot(kernel, v_i, preferred_element_type=jnp.float32)

        k_w = kt_ref[j, :, r0 : r0 + CHUNK + LEAD]
        v_w = vx_ref[j, r0 : r0 + CHUNK + LEAD, :]
        ws = jnp.dot(q_c, k_w, preferred_element_type=jnp.float32) * 0.25
        wrow = lax.broadcasted_iota(jnp.int32, (CHUNK, CHUNK + LEAD), 0)
        wcol = lax.broadcasted_iota(jnp.int32, (CHUNK, CHUNK + LEAD), 1)
        valid = (wcol > wrow + LEAD - WINDOW) & (wcol <= wrow + LEAD)
        if i == 0:
            valid = valid & ((wcol >= LEAD) | jnp.logical_not(first_span))
        masked = jnp.where(valid, ws, -jnp.inf)
        highest = jnp.max(masked, axis=1, keepdims=True)
        expo = jnp.where(valid, jnp.exp(ws - highest), 0.0)
        weights = (expo / jnp.sum(expo, axis=1, keepdims=True)).astype(jnp.bfloat16)
        win_ref[r0 : r0 + CHUNK, cols] = jnp.dot(weights, v_w, preferred_element_type=jnp.float32)


def local_attention(flag, q_hm, kt_hm, vx, block_rows):
    heads_here, span_rows, _ = q_hm.shape
    ext = kt_hm.shape[2]
    step = 4 if heads_here % 4 == 0 else (2 if heads_here % 2 == 0 else 1)
    body = lambda *refs: local_attention_kernel(*refs, span_rows=span_rows, block_rows=block_rows)
    out = jax.ShapeDtypeStruct((span_rows, heads_here * VD), jnp.float32)
    return pl.pallas_call(
        body,
        grid_spec=pltpu.PrefetchScalarGridSpec(
            num_scalar_prefetch=1,
            grid=(heads_here // step,),
            in_specs=[
                pl.BlockSpec((step, span_rows, KD), lambda h, f: (h, 0, 0)),
                pl.BlockSpec((step, KD, ext), lambda h, f: (h, 0, 0)),
                pl.BlockSpec((step, ext, VD), lambda h, f: (h, 0, 0)),
            ],
            out_specs=[
                pl.BlockSpec((span_rows, step * VD), lambda h, f: (0, h)),
                pl.BlockSpec((span_rows, step * VD), lambda h, f: (0, h)),
            ],
        ),
        out_shape=(out, out),
    )(flag, q_hm, kt_hm, vx)


def mix_kernel(intra_ref, inter_ref, win_ref, gain_ref, out_ref):
    for j in range(inter_ref.shape[0]):
        cols = slice(j * VD, (j + 1) * VD)
        linear = intra_ref[:, cols] + inter_ref[j]
        scale = lax.rsqrt(jnp.mean(linear * linear, axis=1, keepdims=True) + epsilon)
        out_ref[:, cols] = (linear * scale * gain_ref[:, cols] + win_ref[:, cols]).astype(
            jnp.bfloat16
        )


def mix(intra, inter_hm, window, gain):
    heads_here, span_rows, _ = inter_hm.shape
    step = heads_here
    tile = pl.BlockSpec((span_rows, step * VD), lambda h: (0, h))
    return pl.pallas_call(
        mix_kernel,
        grid=(heads_here // step,),
        in_specs=[
            tile,
            pl.BlockSpec((step, span_rows, VD), lambda h: (h, 0, 0)),
            tile,
            pl.BlockSpec((1, step * VD), lambda h: (0, h)),
        ],
        out_specs=tile,
        out_shape=jax.ShapeDtypeStruct((span_rows, heads_here * VD), jnp.bfloat16),
    )(intra, inter_hm, window, gain.reshape(1, heads_here * VD))


def per_device(queries, keys, values, gain):
    local_tokens = queries.shape[0]

    def to_heads(tok, width):
        tok = jnp.transpose(tok.reshape(local_tokens, HEADS, width), (1, 0, 2))
        return lax.all_to_all(tok, "head", split_axis=0, concat_axis=1, tiled=True)

    value_hm = to_heads(values, VD)
    key_hm = to_heads(keys, KD)
    heads_here, span_rows, _ = key_hm.shape
    block_rows = min(512, span_rows)
    block_count = span_rows // block_rows
    first_span = lax.axis_index("ctx") == 0

    tails = shifted(
        jnp.concatenate([key_hm, value_hm], axis=2)[:, span_rows - WINDOW :], "ctx", 1
    )

    key_feat = unique_features(key_hm.reshape(heads_here, block_count, block_rows, KD), False)
    block_states = jnp.einsum(
        "hnrf,hnrv->hnfv",
        key_feat,
        value_hm.reshape(heads_here, block_count, block_rows, VD),
        preferred_element_type=jnp.float32,
    )
    span_state = jnp.sum(block_states, axis=1)
    peers = lax.axis_size("ctx")
    running = span_state
    entering = None
    first_round = span_state
    shift = 1
    while shift < peers:
        received = shifted(running, "ctx", shift)
        entering = received if entering is None else entering + received
        if shift == 1:
            first_round = received
        shift *= 2
        if shift < peers:
            running = running + received
    if entering is None:
        entering = jnp.zeros_like(span_state)
    queries, span_state = lax.optimization_barrier((queries, span_state))
    query_hm = to_heads(queries, KD)
    query_hm, first_round = lax.optimization_barrier((query_hm, first_round))
    before = jnp.concatenate(
        [jnp.zeros_like(block_states[:, :1]), jnp.cumsum(block_states[:, :-1], axis=1)], axis=1
    )
    states = (before + entering[:, None]).astype(jnp.bfloat16)

    query_feat = unique_features(query_hm.reshape(heads_here, block_count, block_rows, KD), True)
    inter = jnp.einsum(
        "hnrf,hnfv->hnrv",
        query_feat,
        states,
        preferred_element_type=jnp.float32,
    ).reshape(heads_here, span_rows, VD)

    lead = jnp.zeros((heads_here, LEAD - WINDOW, KD + VD), jnp.bfloat16)
    key_ext = jnp.concatenate([lead[:, :, :KD], tails[:, :, :KD], key_hm], axis=1)
    value_ext = jnp.concatenate([lead[:, :, KD:], tails[:, :, KD:], value_hm], axis=1)
    flag = first_span.astype(jnp.int32).reshape(1)
    intra, window = local_attention(
        flag, query_hm, jnp.transpose(key_ext, (0, 2, 1)), value_ext, block_rows
    )
    mixed = mix(intra, inter, window, gain)
    tokens_back = lax.all_to_all(mixed, "head", split_axis=0, concat_axis=1, tiled=True)
    return tokens_back


def solution(mesh):
    placed = (
        P(("groups", "ctx", "head"), None),
        P(("groups", "ctx", "head"), None),
        P(("groups", "ctx", "head"), None),
        P("head"),
    )
    return jax.shard_map(
        per_device,
        mesh=mesh,
        in_specs=placed,
        out_specs=P(("groups", "ctx", "head"), None),
        check_vma=False,
    )
```
